32 devices in a mesh: lat: 8 (over y, x, core), lon: 4 (over z).
Axes of the slice: x: 2, y: 2, z: 4, core: 2. Of those that a mesh axis runs over, the one named last changes fastest.
Arguments:
- grad_output: bfloat16 [64, 720, 128], P('lat', 'lon'), may hold values from -6 to 6
- band_rows: int32 [8], replicated, may hold values from 1 to 8, 60 in all
- legendre: float32 [192, 360, 64], P('lat'), may hold values from -0.75 to 0.75
- quad_weights: float32 [64], replicated, may hold values from 0.3 to 3
- spectral_filter: float32 [2, 360, 128], replicated, may hold values from -6 to 6
- disco_kernel: float32 [64, 9, 9], replicated, may hold values from -2 to 2
- disco_weight: bfloat16 [128, 9, 128], replicated, may hold values from -0.1875 to 0.1875
Outputs:
- grad_input: bfloat16 [64, 720, 128], P('lat', 'lon')
The draws below stay inside these ranges and needn't reach their ends.
Inputs may be any that keep to these rules, and one draw needn't show every extreme that they name: Bands follow each other from north to south; the live rows of band b fill its first band_rows[b] slots, and all bands together hold 60 rows.
All inputs are finite; a program needn't handle non-finite values.
Results may differ from the reference program's by a relative error of at most 0.0048.
Values may be sent and summed in bfloat16 or wider, within the bound.
No kernel may reach another device: no remote copies, remote signals or barrier semaphores. Data moves between devices by JAX's collectives and lax.ppermute only.
A program may use at most 64 MiB of HBM per device.

```python
import math
import jax
import jax.numpy as jnp
import numpy as np
from jax import lax

C = 128
K = 9
TAPS = 9
M = 192
L = 360
ROWS_DEV = 8
BANDS = 8
NLAT = 64
LIVE = 60
NLON = 720
N_LAT = 8


def level_of(rng, shape, pieces, least, high):
    def one(dim, shards_of):
        draws = jax.random.uniform(jax.random.fold_in(jax.random.fold_in(rng, 6), dim), (shards_of,), jnp.float32, least / len(pieces), high / len(pieces))
        return jnp.repeat(jnp.exp(draws), shape[dim] // shards_of).reshape((-1,) + (1,) * (len(shape) - dim - 1))

    loudness = one(*pieces[0])
    for cut in pieces[1:]:
        loudness = loudness * one(*cut)
    return loudness


def split_up(number_of, total, limit, lean):
    weights = [(1 << 20) // math.isqrt(grade ** lean) + 1 for grade in range(2, number_of + 1)]
    rest, counts = total - limit - (number_of - 1), [1] * (number_of - 1)
    while rest > 0:
        candidates = [i for i in range(number_of - 1) if counts[i] < limit]
        mass, left = sum([weights[i] for i in candidates]), rest
        for i in candidates:
            extra = min(limit - counts[i], max(1, left * weights[i] // mass), rest)
            counts[i] = counts[i] + extra
            rest = rest - extra
    return np.array([limit] + counts)


def ragged(rng, count, total, limit, lean):
    if count == 2:
        one = jax.random.randint(rng, (), max(1, total - limit), min(limit, total - 1) + 1)
        return jnp.stack([one, total - one])
    tallies = jnp.asarray(split_up(count, total, limit, lean), jnp.int32)
    twos = (count - 1) // 2
    donor, taker = tallies[1:1 + 2 * twos:2], tallies[2:2 + 2 * twos:2]
    room = jnp.minimum(donor - 1, limit - taker)
    moved = jax.random.randint(jax.random.fold_in(rng, 1), (twos,), 0, 1 << 20) % (room + 1)
    tallies = tallies.at[1:1 + 2 * twos:2].set(donor - moved).at[2:2 + 2 * twos:2].set(taker + moved)
    return tallies[jax.random.permutation(jax.random.fold_in(rng, 2), count)]


def bell_draw(own_key, shape, width, reach, cuts=(), kind=jnp.bfloat16):
    level = level_of(own_key, shape, cuts, -0.22, 0.18) if cuts else 1.0
    values = jax.random.normal(own_key, shape, jnp.float32) * width * level
    return jnp.minimum(jnp.maximum(values, -reach), reach).astype(kind)


def setup_inputs(seed: int = 0) -> dict:
    arg_keys = jax.random.split(jax.random.key(seed), 8)
    return {
        "grad_output": bell_draw(arg_keys[0], (NLAT, NLON, C), 1.0, 6.0, ((0, 8), (1, 4))),
        "band_rows": ragged(arg_keys[1], BANDS, LIVE, ROWS_DEV, 2).astype(jnp.int32),
        "legendre": bell_draw(arg_keys[2], (M, L, NLAT), LIVE ** -0.5, 0.75, ((0, 8),), jnp.float32),
        "quad_weights": jnp.clip(jnp.exp(jax.random.uniform(arg_keys[3], (NLAT,), jnp.float32, math.log(0.3), math.log(3.0))), 0.3, 3.0),
        "spectral_filter": bell_draw(arg_keys[4], (2, L, C), 1.0, 6.0, (), jnp.float32),
        "disco_kernel": bell_draw(arg_keys[5], (NLAT, TAPS, K), TAPS ** -0.5, 2.0, (), jnp.float32),
        "disco_weight": bell_draw(arg_keys[6], (C, K, C), (K * C) ** -0.5, 0.1875),
    }


highest = lax.Precision.HIGHEST


def make_trig(mode_count, point_count):
    wavenumber = lax.broadcasted_iota(jnp.int32, (point_count, mode_count), 1)
    position = lax.broadcasted_iota(jnp.int32, (point_count, mode_count), 0)
    angles = ((wavenumber * position) % point_count).astype(jnp.float32) * (2.0 * jnp.pi / point_count)
    scaled = jnp.stack([jnp.cos(angles), -jnp.sin(angles)], axis=2) * (point_count ** -0.5)
    return scaled.reshape(point_count, 2 * mode_count)


def tap_products(source_field, kernel_rows, disco_weight):
    row_count, lon_count, channels = source_field.shape
    kernel_kinds = disco_weight.shape[1]
    mixtures = jnp.dot(source_field.reshape(row_count * lon_count, channels),
                       disco_weight.reshape(channels, kernel_kinds * channels),
                       preferred_element_type=jnp.float32)
    mixtures = mixtures.reshape(row_count, lon_count, kernel_kinds, channels)
    return jnp.einsum('rnkc,rtk->rntc', mixtures, kernel_rows, precision=highest).astype(jnp.bfloat16)


def reference(grad_output, band_rows, legendre, quad_weights, spectral_filter, disco_kernel, disco_weight):
    slot_ids = jnp.arange(NLAT, dtype=jnp.int32)
    slot_band = slot_ids // ROWS_DEV
    slot_level = slot_ids % ROWS_DEV
    band_start = (jnp.cumsum(band_rows) - band_rows).astype(jnp.int32)
    live_slot = slot_level < band_rows[slot_band]
    global_row = (band_start[slot_band] + slot_level).astype(jnp.int32)
    masked = jnp.where(live_slot[:, None, None], grad_output, jnp.zeros_like(grad_output))
    trig_table = make_trig(M, NLON)

    def forward_band(band_block):
        spectra = jnp.einsum('snc,nk->skc', band_block.astype(jnp.float32), trig_table, precision=highest)
        return spectra.astype(jnp.bfloat16)

    spectra = lax.map(forward_band, masked.reshape(N_LAT, ROWS_DEV, NLON, C)).reshape(NLAT, M, 2, C)
    coefficients = jnp.einsum('mls,smpc->lmpc', legendre, spectra.astype(jnp.float32), precision=highest)
    filter_real = spectral_filter[0][:, None, :]
    filter_imag = spectral_filter[1][:, None, :]
    real_part = coefficients[:, :, 0, :]
    imag_part = coefficients[:, :, 1, :]
    filtered = jnp.stack([filter_real * real_part + filter_imag * imag_part,
                          filter_real * imag_part - filter_imag * real_part], axis=2)
    returned = jnp.einsum('mls,lmpc->smpc', legendre, filtered, precision=highest)
    returned = (returned * quad_weights[:, None, None, None]).astype(jnp.bfloat16)

    def inverse_band(band_block):
        flat_modes = band_block.reshape(ROWS_DEV, 2 * M, C).astype(jnp.float32)
        return jnp.einsum('skc,nk->snc', flat_modes, trig_table, precision=highest).astype(jnp.bfloat16)

    spectral = lax.map(inverse_band, returned.reshape(N_LAT, ROWS_DEV, M, 2, C)).reshape(NLAT, NLON, C)

    block_rows = 32
    block_count = (LIVE + block_rows - 1) // block_rows
    pad_total = block_count * block_rows + 2
    target = jnp.where(live_slot, global_row + 1, pad_total).astype(jnp.int32)
    padded_field = jnp.zeros((pad_total, NLON, C), jnp.bfloat16).at[target].set(masked, mode="drop")
    padded_kernel = jnp.zeros((pad_total, TAPS, K), jnp.float32).at[target].set(disco_kernel, mode="drop")

    def disco_block(start):
        field_rows = lax.dynamic_slice_in_dim(padded_field, start, block_rows + 2, 0)
        kernel_rows = lax.dynamic_slice_in_dim(padded_kernel, start, block_rows + 2, 0)
        products = tap_products(field_rows, kernel_rows, disco_weight).astype(jnp.float32)
        summed = jnp.zeros((block_rows, NLON, C), jnp.float32)
        for row_step in (1, 0, -1):
            source = products[1 - row_step:1 - row_step + block_rows]
            for col_step in (-1, 0, 1):
                tap_index = 3 * (row_step + 1) + col_step + 1
                summed = summed + jnp.roll(source[:, :, tap_index, :], col_step, axis=1)
        return summed

    starts = jnp.arange(block_count, dtype=jnp.int32) * block_rows
    disco_term = lax.map(disco_block, starts).reshape(block_count * block_rows, NLON, C)
    disco_slots = disco_term[jnp.clip(global_row, 0, LIVE - 1)]
    summed = masked.astype(jnp.float32) + disco_slots + spectral.astype(jnp.float32)
    return jnp.where(live_slot[:, None, None], summed, 0.0).astype(jnp.bfloat16)
```

```python
import jax
import jax.numpy as jnp
from jax import lax
from jax.experimental import pallas as pl
from jax.experimental.pallas import tpu as pltpu
from jax.sharding import PartitionSpec as P

highest = lax.Precision.HIGHEST
tripled = lax.Precision.HIGH


def make_trig(mode_count, point_count):
    wavenumber = lax.broadcasted_iota(jnp.int32, (point_count, mode_count), 1)
    position = lax.broadcasted_iota(jnp.int32, (point_count, mode_count), 0)
    angles = (wavenumber * position % point_count).astype(jnp.float32) * (
        2.0 * jnp.pi / point_count
    )
    scaled = jnp.stack([jnp.cos(angles), -jnp.sin(angles)], axis=2) * point_count ** (-0.5)
    return scaled.reshape(point_count, 2 * mode_count)


CHUNK = 64


def round_up(value, step):
    return -(-value // step) * step


def disco_body(src_ref, coef_ref, ext_ref, w_ref, out_ref, mix_ref):
    row_total = ext_ref.shape[0]
    slot_total = out_ref.shape[0]
    kinds = w_ref.shape[1] // w_ref.shape[0]
    channels = w_ref.shape[0]
    for r in range(row_total):
        mix_ref[r] = jnp.dot(ext_ref[r], w_ref[...], preferred_element_type=jnp.float32)

    def slot_step(s, carry):
        for c0 in range(0, out_ref.shape[1], CHUNK):
            acc = jnp.zeros((CHUNK, channels), jnp.float32)
            for a_i in range(3):
                row = src_ref[s * 3 + a_i]
                for b_i in range(3):
                    for k in range(kinds):
                        coef = coef_ref[((s * 3 + a_i) * 3 + b_i) * kinds + k]
                        acc = acc + coef * mix_ref[
                            row, pl.ds(c0 + 2 - b_i, CHUNK), pl.ds(k * channels, channels)
                        ]
            out_ref[s, pl.ds(c0, CHUNK), :] = acc
        return carry

    lax.fori_loop(0, slot_total, slot_step, 0)


def disco_apply(src, coef, ext, weight_flat, slot_total, lon_count):
    row_total, lon_pad, channels = ext.shape
    out_rows = round_up(lon_count, CHUNK)
    smem = pltpu.MemorySpace.SMEM if hasattr(pltpu, "MemorySpace") else pltpu.SMEM
    return pl.pallas_call(
        disco_body,
        out_shape=jax.ShapeDtypeStruct((slot_total, out_rows, channels), jnp.float32),
        in_specs=[
            pl.BlockSpec(memory_space=smem),
            pl.BlockSpec(memory_space=smem),
            pl.BlockSpec(memory_space=pltpu.VMEM),
            pl.BlockSpec(memory_space=pltpu.VMEM),
        ],
        out_specs=pl.BlockSpec(memory_space=pltpu.VMEM),
        scratch_shapes=[pltpu.VMEM((row_total, lon_pad, weight_flat.shape[1]), jnp.float32)],
    )(src, coef, ext, weight_flat)


def disco_tables(band_rows, disco_kernel, band_index, band_total, row_count):
    slot_ids = jnp.arange(row_count, dtype=jnp.int32)
    live_rows = band_rows[band_index]
    has_next = slot_ids + 1 < live_rows
    prev_band = jnp.maximum(band_index - 1, 0)
    next_band = jnp.minimum(band_index + 1, band_total - 1)
    base = band_index * row_count
    up_src = jnp.where(slot_ids == 0, 0, slot_ids)
    down_src = jnp.where(has_next, slot_ids + 2, row_count + 1)
    src = jnp.stack([up_src, slot_ids + 1, down_src], axis=1)
    up_row = jnp.where(
        slot_ids == 0, prev_band * row_count + band_rows[prev_band] - 1, base + slot_ids - 1
    )
    down_row = jnp.where(has_next, base + slot_ids + 1, next_band * row_count)
    kernel_row = jnp.stack([up_row, base + slot_ids, down_row], axis=1)
    kernel_row = jnp.clip(kernel_row, 0, disco_kernel.shape[0] - 1)
    up_ok = (slot_ids > 0) | (band_index > 0)
    down_ok = has_next | (band_index < band_total - 1)
    valid = jnp.stack([up_ok, jnp.ones_like(up_ok), down_ok], axis=1)
    gathered = disco_kernel[kernel_row]
    gathered = gathered.reshape(row_count, 3, 3, 3, disco_kernel.shape[2])
    coef = jnp.stack([gathered[:, 0, 2], gathered[:, 1, 1], gathered[:, 2, 0]], axis=1)
    coef = jnp.where(valid[:, :, None, None], coef, 0.0)
    return src.reshape(-1).astype(jnp.int32), coef.reshape(-1).astype(jnp.float32)


def halo_extend(masked, live_rows):
    row_count, lon_count, channels = masked.shape
    lat_total = lax.axis_size("lat")
    lon_total = lax.axis_size("lon")
    lat_up = [(i, (i + 1) % lat_total) for i in range(lat_total)]
    lat_down = [(j, i) for i, j in lat_up]
    lon_up = [(i, (i + 1) % lon_total) for i in range(lon_total)]
    lon_down = [(j, i) for i, j in lon_up]
    last_row = lax.dynamic_slice_in_dim(masked, live_rows - 1, 1, 0)
    from_above = lax.ppermute(last_row, "lat", lat_up)
    from_below = lax.ppermute(masked[0:1], "lat", lat_down)
    rows = jnp.concatenate([from_above, masked, from_below], axis=0)
    from_left = lax.ppermute(rows[:, lon_count - 1 : lon_count], "lon", lon_up)
    from_right = lax.ppermute(rows[:, 0:1], "lon", lon_down)
    lon_pad = round_up(round_up(lon_count, CHUNK) + 2, 16)
    pad = jnp.zeros((row_count + 2, lon_pad - lon_count - 2, channels), masked.dtype)
    return jnp.concatenate([from_left, rows, from_right, pad], axis=1)


def on_device(
    grad_output, band_rows, legendre, quad_weights, spectral_filter, disco_kernel, disco_weight
):
    row_count, lon_count, channels = grad_output.shape
    band_index = lax.axis_index("lat")
    band_total = lax.axis_size("lat")
    lon_index = lax.axis_index("lon")
    point_count = lon_count * lax.axis_size("lon")
    mode_count = legendre.shape[0] * band_total
    chan_share = channels // lax.axis_size("lon")
    slot_ids = jnp.arange(row_count, dtype=jnp.int32)
    live_rows = band_rows[band_index]
    live_slot = slot_ids < live_rows
    masked = jnp.where(live_slot[:, None, None], grad_output, jnp.zeros_like(grad_output))
    trig_table = make_trig(mode_count, point_count)
    portion = lax.all_to_all(masked, "lon", split_axis=2, concat_axis=1, tiled=True)
    spectra = jnp.einsum("rnc,nk->rkc", portion.astype(jnp.float32), trig_table, precision=tripled)
    spectra = spectra.reshape(portion.shape[0], mode_count, 2, portion.shape[2]).astype(
        jnp.bfloat16
    )
    columns = lax.all_to_all(spectra, "lat", split_axis=1, concat_axis=0, tiled=True)
    coefficients = jnp.einsum(
        "mls,smpc->lmpc", legendre, columns.astype(jnp.float32), precision=highest
    )
    filter_slice = lax.dynamic_slice_in_dim(spectral_filter, lon_index * chan_share, chan_share, 2)
    filter_real = filter_slice[0][:, None, :]
    filter_imag = filter_slice[1][:, None, :]
    real_part = coefficients[:, :, 0, :]
    imag_part = coefficients[:, :, 1, :]
    filtered = jnp.stack(
        [
            filter_real * real_part + filter_imag * imag_part,
            filter_real * imag_part - filter_imag * real_part,
        ],
        axis=2,
    )
    returned = jnp.einsum("mls,lmpc->smpc", legendre, filtered, precision=highest)
    returned = (returned * quad_weights[:, None, None, None]).astype(jnp.bfloat16)
    portion = lax.all_to_all(returned, "lat", split_axis=0, concat_axis=1, tiled=True)
    flat_modes = portion.reshape(portion.shape[0], 2 * mode_count, portion.shape[3]).astype(
        jnp.float32
    )
    spectral_rows = jnp.einsum("rkc,nk->rnc", flat_modes, trig_table, precision=tripled).astype(
        jnp.bfloat16
    )
    spectral = lax.all_to_all(spectral_rows, "lon", split_axis=1, concat_axis=2, tiled=True)
    ext = halo_extend(masked, live_rows)
    src_rows, coef = disco_tables(band_rows, disco_kernel, band_index, band_total, row_count)
    weight_flat = disco_weight.reshape(channels, -1)
    disco_full = disco_apply(src_rows, coef, ext, weight_flat, row_count, lon_count)
    disco_term = disco_full[:, :lon_count, :]
    summed = masked.astype(jnp.float32) + disco_term + spectral.astype(jnp.float32)
    return jnp.where(live_slot[:, None, None], summed, 0.0).astype(jnp.bfloat16)


def solution(mesh):
    placed = (P("lat", "lon", None), P(), P("lat", None, None), P(), P(), P(), P())
    return jax.shard_map(
        on_device, mesh=mesh, in_specs=placed, out_specs=P("lat", "lon", None), check_vma=False
    )
```

```python
import ml_dtypes
import numpy as np
import jax
import jax.numpy as jnp
from jax import lax
from jax.experimental import pallas as pl
from jax.experimental.pallas import tpu as pltpu
from jax.sharding import PartitionSpec as P


def make_trig(mode_count, point_count):
    step = next(d for d in range(int(point_count ** 0.5), 0, -1) if point_count % d == 0)
    coarse = np.arange(point_count // step)[:, None] * step
    fine = np.arange(step)[:, None]
    wavenumber = np.arange(mode_count)[None, :]
    coarse_angle = (wavenumber * coarse % point_count) * (2.0 * np.pi / point_count)
    fine_angle = (wavenumber * fine % point_count) * (2.0 * np.pi / point_count)
    scale = point_count ** (-0.5)
    coarse_cos = jnp.asarray((np.cos(coarse_angle) * scale).astype(np.float32))[:, None, :]
    coarse_sin = jnp.asarray((np.sin(coarse_angle) * scale).astype(np.float32))[:, None, :]
    fine_cos = jnp.asarray(np.cos(fine_angle).astype(np.float32))[None, :, :]
    fine_sin = jnp.asarray(np.sin(fine_angle).astype(np.float32))[None, :, :]
    cosine = coarse_cos * fine_cos - coarse_sin * fine_sin
    sine = coarse_sin * fine_cos + coarse_cos * fine_sin
    table = jnp.stack([cosine, -sine], axis=3).reshape(point_count, 2 * mode_count)
    return split_bf16(table)


def split_bf16(values):
    rounded = lax.reduce_precision(values, exponent_bits=8, mantissa_bits=7)
    return rounded.astype(jnp.bfloat16), (values - rounded).astype(jnp.bfloat16)


def dot_split(spec, left_parts, right_parts):
    total = None
    for lp in left_parts:
        for rp in right_parts:
            if lp is not left_parts[0] and rp is not right_parts[0]:
                continue
            term = jnp.einsum(spec, lp, rp, preferred_element_type=jnp.float32)
            total = term if total is None else total + term
    return total


CHUNK = 64


def round_up(value, step):
    return -(-value // step) * step


def disco_body(src_ref, coef_ref, ext_ref, w_ref, out_ref, mix_ref):
    row_total = ext_ref.shape[0]
    slot_total = out_ref.shape[0]
    kinds = w_ref.shape[1] // w_ref.shape[0]
    channels = w_ref.shape[0]
    for r in range(row_total):
        mix_ref[r] = jnp.dot(ext_ref[r], w_ref[...], preferred_element_type=jnp.float32)

    def slot_step(s, carry):
        for c0 in range(0, out_ref.shape[1], CHUNK):
            acc = jnp.zeros((CHUNK, channels), jnp.float32)
            for a_i in range(3):
                row = src_ref[s * 3 + a_i]
                for b_i in range(3):
                    for k in range(kinds):
                        coef = coef_ref[((s * 3 + a_i) * 3 + b_i) * kinds + k]
                        acc = acc + coef * mix_ref[
                            row, pl.ds(c0 + 2 - b_i, CHUNK), pl.ds(k * channels, channels)
                        ]
            out_ref[s, pl.ds(c0, CHUNK), :] = acc
        return carry

    lax.fori_loop(0, slot_total, slot_step, 0)


def disco_apply(src, coef, ext, weight_flat, slot_total, lon_count):
    row_total, lon_pad, channels = ext.shape
    out_rows = round_up(lon_count, CHUNK)
    smem = pltpu.MemorySpace.SMEM if hasattr(pltpu, "MemorySpace") else pltpu.SMEM
    return pl.pallas_call(
        disco_body,
        out_shape=jax.ShapeDtypeStruct((slot_total, out_rows, channels), jnp.float32),
        in_specs=[
            pl.BlockSpec(memory_space=smem),
            pl.BlockSpec(memory_space=smem),
            pl.BlockSpec(memory_space=pltpu.VMEM),
            pl.BlockSpec(memory_space=pltpu.VMEM),
        ],
        out_specs=pl.BlockSpec(memory_space=pltpu.VMEM),
        scratch_shapes=[pltpu.VMEM((row_total, lon_pad, weight_flat.shape[1]), jnp.float32)],
    )(src, coef, ext, weight_flat)


def disco_tables(band_rows, disco_kernel, band_index, band_total, row_count):
    slot_ids = jnp.arange(row_count, dtype=jnp.int32)
    live_rows = band_rows[band_index]
    has_next = slot_ids + 1 < live_rows
    prev_band = jnp.maximum(band_index - 1, 0)
    next_band = jnp.minimum(band_index + 1, band_total - 1)
    base = band_index * row_count
    up_src = jnp.where(slot_ids == 0, 0, slot_ids)
    down_src = jnp.where(has_next, slot_ids + 2, row_count + 1)
    src = jnp.stack([up_src, slot_ids + 1, down_src], axis=1)
    up_row = jnp.where(
        slot_ids == 0, prev_band * row_count + band_rows[prev_band] - 1, base + slot_ids - 1
    )
    down_row = jnp.where(has_next, base + slot_ids + 1, next_band * row_count)
    kernel_row = jnp.stack([up_row, base + slot_ids, down_row], axis=1)
    kernel_row = jnp.clip(kernel_row, 0, disco_kernel.shape[0] - 1)
    up_ok = (slot_ids > 0) | (band_index > 0)
    down_ok = has_next | (band_index < band_total - 1)
    valid = jnp.stack([up_ok, jnp.ones_like(up_ok), down_ok], axis=1)
    gathered = disco_kernel[kernel_row]
    gathered = gathered.reshape(row_count, 3, 3, 3, disco_kernel.shape[2])
    coef = jnp.stack([gathered[:, 0, 2], gathered[:, 1, 1], gathered[:, 2, 0]], axis=1)
    coef = jnp.where(valid[:, :, None, None], coef, 0.0)
    return src.reshape(-1).astype(jnp.int32), coef.reshape(-1).astype(jnp.float32)


def halo_extend(masked, live_rows):
    row_count, lon_count, channels = masked.shape
    lat_total = lax.axis_size("lat")
    lon_total = lax.axis_size("lon")
    lat_up = [(i, (i + 1) % lat_total) for i in range(lat_total)]
    lat_down = [(j, i) for i, j in lat_up]
    lon_up = [(i, (i + 1) % lon_total) for i in range(lon_total)]
    lon_down = [(j, i) for i, j in lon_up]
    last_row = lax.dynamic_slice_in_dim(masked, live_rows - 1, 1, 0)
    from_above = lax.ppermute(last_row, "lat", lat_up)
    from_below = lax.ppermute(masked[0:1], "lat", lat_down)
    rows = jnp.concatenate([from_above, masked, from_below], axis=0)
    from_left = lax.ppermute(rows[:, lon_count - 1 : lon_count], "lon", lon_up)
    from_right = lax.ppermute(rows[:, 0:1], "lon", lon_down)
    lon_pad = round_up(round_up(lon_count, CHUNK) + 2, 16)
    pad = jnp.zeros((row_count + 2, lon_pad - lon_count - 2, channels), masked.dtype)
    return jnp.concatenate([from_left, rows, from_right, pad], axis=1)


def on_device(
    grad_output, band_rows, legendre, quad_weights, spectral_filter, disco_kernel, disco_weight
):
    row_count, lon_count, channels = grad_output.shape
    band_index = lax.axis_index("lat")
    band_total = lax.axis_size("lat")
    lon_index = lax.axis_index("lon")
    point_count = lon_count * lax.axis_size("lon")
    mode_count = legendre.shape[0] * band_total
    chan_share = channels // lax.axis_size("lon")
    slot_ids = jnp.arange(row_count, dtype=jnp.int32)
    live_rows = band_rows[band_index]
    live_slot = slot_ids < live_rows
    masked = jnp.where(live_slot[:, None, None], grad_output, jnp.zeros_like(grad_output))
    trig_parts = make_trig(mode_count, point_count)
    portion = lax.all_to_all(masked, "lon", split_axis=2, concat_axis=1, tiled=True)
    spectra = dot_split("rnc,nk->rkc", (portion,), trig_parts)
    spectra = spectra.reshape(portion.shape[0], mode_count, 2, portion.shape[2]).astype(
        jnp.bfloat16
    )
    columns = lax.all_to_all(spectra, "lat", split_axis=1, concat_axis=0, tiled=True)
    legendre_parts = split_bf16(legendre)
    coefficients = dot_split("mls,smpc->lmpc", legendre_parts, (columns,))
    filter_slice = lax.dynamic_slice_in_dim(spectral_filter, lon_index * chan_share, chan_share, 2)
    filter_real = filter_slice[0][:, None, :]
    filter_imag = filter_slice[1][:, None, :]
    real_part = coefficients[:, :, 0, :]
    imag_part = coefficients[:, :, 1, :]
    filtered = jnp.stack(
        [
            filter_real * real_part + filter_imag * imag_part,
            filter_real * imag_part - filter_imag * real_part,
        ],
        axis=2,
    )
    returned = dot_split("mls,lmpc->smpc", legendre_parts, split_bf16(filtered))
    returned = (returned * quad_weights[:, None, None, None]).astype(jnp.bfloat16)
    portion = lax.all_to_all(returned, "lat", split_axis=0, concat_axis=1, tiled=True)
    flat_modes = portion.reshape(portion.shape[0], 2 * mode_count, portion.shape[3])
    spectral_rows = dot_split("rkc,nk->rnc", (flat_modes,), trig_parts).astype(jnp.bfloat16)
    spectral = lax.all_to_all(spectral_rows, "lon", split_axis=1, concat_axis=2, tiled=True)
    ext = halo_extend(masked, live_rows)
    src_rows, coef = disco_tables(band_rows, disco_kernel, band_index, band_total, row_count)
    weight_flat = disco_weight.reshape(channels, -1)
    disco_full = disco_apply(src_rows, coef, ext, weight_flat, row_count, lon_count)
    disco_term = disco_full[:, :lon_count, :]
    summed = masked.astype(jnp.float32) + disco_term + spectral.astype(jnp.float32)
    return jnp.where(live_slot[:, None, None], summed, 0.0).astype(jnp.bfloat16)


def solution(mesh):
    placed = (P("lat", "lon", None), P(), P("lat", None, None), P(), P(), P(), P())
    return jax.shard_map(
        on_device, mesh=mesh, in_specs=placed, out_specs=P("lat", "lon", None), check_vma=False
    )
```

```python
import ml_dtypes
import numpy as np
import jax
import jax.numpy as jnp
from jax import lax
from jax.experimental import pallas as pl
from jax.experimental.pallas import tpu as pltpu
from jax.sharding import PartitionSpec as P


def make_trig(mode_count, point_count):
    step = next(d for d in range(int(point_count ** 0.5), 0, -1) if point_count % d == 0)
    coarse = np.arange(point_count // step)[:, None] * step
    fine = np.arange(step)[:, None]
    wavenumber = np.arange(mode_count)[None, :]
    coarse_angle = (wavenumber * coarse % point_count) * (2.0 * np.pi / point_count)
    fine_angle = (wavenumber * fine % point_count) * (2.0 * np.pi / point_count)
    scale = point_count ** (-0.5)
    coarse_cos = jnp.asarray((np.cos(coarse_angle) * scale).astype(np.float32))[:, None, :]
    coarse_sin = jnp.asarray((np.sin(coarse_angle) * scale).astype(np.float32))[:, None, :]
    fine_cos = jnp.asarray(np.cos(fine_angle).astype(np.float32))[None, :, :]
    fine_sin = jnp.asarray(np.sin(fine_angle).astype(np.float32))[None, :, :]
    cosine = coarse_cos * fine_cos - coarse_sin * fine_sin
    sine = coarse_sin * fine_cos + coarse_cos * fine_sin
    table = jnp.stack([cosine, -sine], axis=3).reshape(point_count, 2 * mode_count)
    return split_bf16(table)


def split_bf16(values):
    rounded = lax.reduce_precision(values, exponent_bits=8, mantissa_bits=7)
    return rounded.astype(jnp.bfloat16), (values - rounded).astype(jnp.bfloat16)


def dot_split(spec, left_parts, right_parts):
    total = None
    for lp in left_parts:
        for rp in right_parts:
            if lp is not left_parts[0] and rp is not right_parts[0]:
                continue
            term = jnp.einsum(spec, lp, rp, preferred_element_type=jnp.float32)
            total = term if total is None else total + term
    return total


CHUNK = 64


def round_up(value, step):
    return -(-value // step) * step


def disco_body(src_ref, coef_ref, ext_ref, w_ref, out_ref, mix_ref):
    row_total = ext_ref.shape[0]
    slot_total = out_ref.shape[0]
    kinds = w_ref.shape[1] // w_ref.shape[0]
    channels = w_ref.shape[0]
    for r in range(row_total):
        mix_ref[r] = jnp.dot(ext_ref[r], w_ref[...], preferred_element_type=jnp.float32)

    def slot_step(s, carry):
        for c0 in range(0, out_ref.shape[1], CHUNK):
            acc = jnp.zeros((CHUNK, channels), jnp.float32)
            for a_i in range(3):
                row = src_ref[s * 3 + a_i]
                for b_i in range(3):
                    for k in range(kinds):
                        coef = coef_ref[((s * 3 + a_i) * 3 + b_i) * kinds + k]
                        acc = acc + coef * mix_ref[
                            row, pl.ds(c0 + 2 - b_i, CHUNK), pl.ds(k * channels, channels)
                        ]
            out_ref[s, pl.ds(c0, CHUNK), :] = acc
        return carry

    lax.fori_loop(0, slot_total, slot_step, 0)


def disco_apply(src, coef, ext, weight_flat, slot_total, lon_count):
    row_total, lon_pad, channels = ext.shape
    out_rows = round_up(lon_count, CHUNK)
    smem = pltpu.MemorySpace.SMEM if hasattr(pltpu, "MemorySpace") else pltpu.SMEM
    return pl.pallas_call(
        disco_body,
        out_shape=jax.ShapeDtypeStruct((slot_total, out_rows, channels), jnp.float32),
        in_specs=[
            pl.BlockSpec(memory_space=smem),
            pl.BlockSpec(memory_space=smem),
            pl.BlockSpec(memory_space=pltpu.VMEM),
            pl.BlockSpec(memory_space=pltpu.VMEM),
        ],
        out_specs=pl.BlockSpec(memory_space=pltpu.VMEM),
        scratch_shapes=[pltpu.VMEM((row_total, lon_pad, weight_flat.shape[1]), jnp.float32)],
    )(src, coef, ext, weight_flat)


def disco_tables(band_rows, disco_kernel, band_index, band_total, row_count):
    slot_ids = jnp.arange(row_count, dtype=jnp.int32)
    live_rows = band_rows[band_index]
    has_next = slot_ids + 1 < live_rows
    prev_band = jnp.maximum(band_index - 1, 0)
    next_band = jnp.minimum(band_index + 1, band_total - 1)
    base = band_index * row_count
    up_src = jnp.where(slot_ids == 0, 0, slot_ids)
    down_src = jnp.where(has_next, slot_ids + 2, row_count + 1)
    src = jnp.stack([up_src, slot_ids + 1, down_src], axis=1)
    up_row = jnp.where(
        slot_ids == 0, prev_band * row_count + band_rows[prev_band] - 1, base + slot_ids - 1
    )
    down_row = jnp.where(has_next, base + slot_ids + 1, next_band * row_count)
    kernel_row = jnp.stack([up_row, base + slot_ids, down_row], axis=1)
    kernel_row = jnp.clip(kernel_row, 0, disco_kernel.shape[0] - 1)
    up_ok = (slot_ids > 0) | (band_index > 0)
    down_ok = has_next | (band_index < band_total - 1)
    valid = jnp.stack([up_ok, jnp.ones_like(up_ok), down_ok], axis=1)
    gathered = disco_kernel[kernel_row]
    gathered = gathered.reshape(row_count, 3, 3, 3, disco_kernel.shape[2])
    coef = jnp.stack([gathered[:, 0, 2], gathered[:, 1, 1], gathered[:, 2, 0]], axis=1)
    coef = jnp.where(valid[:, :, None, None], coef, 0.0)
    return src.reshape(-1).astype(jnp.int32), coef.reshape(-1).astype(jnp.float32)


def halo_extend(masked, live_rows):
    row_count, lon_count, channels = masked.shape
    lat_total = lax.axis_size("lat")
    lon_total = lax.axis_size("lon")
    lat_up = [(i, (i + 1) % lat_total) for i in range(lat_total)]
    lat_down = [(j, i) for i, j in lat_up]
    lon_up = [(i, (i + 1) % lon_total) for i in range(lon_total)]
    lon_down = [(j, i) for i, j in lon_up]
    last_row = lax.dynamic_slice_in_dim(masked, live_rows - 1, 1, 0)
    from_above = lax.ppermute(last_row, "lat", lat_up)
    from_below = lax.ppermute(masked[0:1], "lat", lat_down)
    rows = jnp.concatenate([from_above, masked, from_below], axis=0)
    from_left = lax.ppermute(rows[:, lon_count - 1 : lon_count], "lon", lon_up)
    from_right = lax.ppermute(rows[:, 0:1], "lon", lon_down)
    lon_pad = round_up(round_up(lon_count, CHUNK) + 2, 16)
    pad = jnp.zeros((row_count + 2, lon_pad - lon_count - 2, channels), masked.dtype)
    return jnp.concatenate([from_left, rows, from_right, pad], axis=1)


def on_device(
    grad_output, band_rows, legendre, quad_weights, spectral_filter, disco_kernel, disco_weight
):
    row_count, lon_count, channels = grad_output.shape
    band_index = lax.axis_index("lat")
    band_total = lax.axis_size("lat")
    lon_index = lax.axis_index("lon")
    point_count = lon_count * lax.axis_size("lon")
    mode_count = legendre.shape[0] * band_total
    chan_share = channels // lax.axis_size("lon")
    slot_ids = jnp.arange(row_count, dtype=jnp.int32)
    live_rows = band_rows[band_index]
    live_slot = slot_ids < live_rows
    masked = jnp.where(live_slot[:, None, None], grad_output, jnp.zeros_like(grad_output))
    trig_parts = make_trig(mode_count, point_count)
    portion = lax.all_to_all(masked, "lon", split_axis=2, concat_axis=1, tiled=True)
    spectra = dot_split("rnc,nk->rkc", (portion,), trig_parts)
    spectra = spectra.reshape(portion.shape[0], mode_count, 2, portion.shape[2]).astype(
        jnp.bfloat16
    )
    columns = lax.all_to_all(spectra, "lat", split_axis=1, concat_axis=0, tiled=True)
    coefficients = jnp.einsum(
        "mls,smpc->lmpc", legendre, columns.astype(jnp.float32), precision=lax.Precision.HIGHEST
    )
    filter_slice = lax.dynamic_slice_in_dim(spectral_filter, lon_index * chan_share, chan_share, 2)
    filter_real = filter_slice[0][:, None, :]
    filter_imag = filter_slice[1][:, None, :]
    real_part = coefficients[:, :, 0, :]
    imag_part = coefficients[:, :, 1, :]
    filtered = jnp.stack(
        [
            filter_real * real_part + filter_imag * imag_part,
            filter_real * imag_part - filter_imag * real_part,
        ],
        axis=2,
    )
    returned = jnp.einsum("mls,lmpc->smpc", legendre, filtered, precision=lax.Precision.HIGHEST)
    returned = (returned * quad_weights[:, None, None, None]).astype(jnp.bfloat16)
    portion = lax.all_to_all(returned, "lat", split_axis=0, concat_axis=1, tiled=True)
    flat_modes = portion.reshape(portion.shape[0], 2 * mode_count, portion.shape[3])
    spectral_rows = dot_split("rkc,nk->rnc", (flat_modes,), trig_parts).astype(jnp.bfloat16)
    spectral = lax.all_to_all(spectral_rows, "lon", split_axis=1, concat_axis=2, tiled=True)
    ext = halo_extend(masked, live_rows)
    src_rows, coef = disco_tables(band_rows, disco_kernel, band_index, band_total, row_count)
    weight_flat = disco_weight.reshape(channels, -1)
    disco_full = disco_apply(src_rows, coef, ext, weight_flat, row_count, lon_count)
    disco_term = disco_full[:, :lon_count, :]
    summed = masked.astype(jnp.float32) + disco_term + spectral.astype(jnp.float32)
    return jnp.where(live_slot[:, None, None], summed, 0.0).astype(jnp.bfloat16)


def solution(mesh):
    placed = (P("lat", "lon", None), P(), P("lat", None, None), P(), P(), P(), P())
    return jax.shard_map(
        on_device, mesh=mesh, in_specs=placed, out_specs=P("lat", "lon", None), check_vma=False
    )
```

```python
import ml_dtypes
import numpy as np
import jax
import jax.numpy as jnp
from jax import lax
from jax.experimental import pallas as pl
from jax.experimental.pallas import tpu as pltpu
from jax.sharding import PartitionSpec as P


def make_trig(mode_count, point_count):
    step = 16 if point_count % 16 == 0 else 1
    coarse = np.arange(point_count // step)[:, None] * step
    fine = np.arange(step)[:, None]
    wavenumber = np.arange(mode_count)[None, :]
    coarse_angle = (wavenumber * coarse % point_count) * (2.0 * np.pi / point_count)
    fine_angle = (wavenumber * fine % point_count) * (2.0 * np.pi / point_count)
    scale = point_count ** (-0.5)
    coarse_cos = jnp.asarray((np.cos(coarse_angle) * scale).astype(np.float32))[:, None, :]
    coarse_sin = jnp.asarray((np.sin(coarse_angle) * scale).astype(np.float32))[:, None, :]
    fine_cos = jnp.asarray(np.cos(fine_angle).astype(np.float32))[None, :, :]
    fine_sin = jnp.asarray(np.sin(fine_angle).astype(np.float32))[None, :, :]
    cosine = coarse_cos * fine_cos - coarse_sin * fine_sin
    minus_sine = -(coarse_sin * fine_cos + coarse_cos * fine_sin)
    return tuple(
        split_bf16(part.reshape(point_count, mode_count)) for part in (cosine, minus_sine)
    )


def split_bf16(values):
    rounded = lax.reduce_precision(values, exponent_bits=8, mantissa_bits=7)
    return rounded.astype(jnp.bfloat16), (values - rounded).astype(jnp.bfloat16)


def dot_split(spec, left_parts, right_parts):
    total = None
    for lp in left_parts:
        for rp in right_parts:
            if lp is not left_parts[0] and rp is not right_parts[0]:
                continue
            term = jnp.einsum(spec, lp, rp, preferred_element_type=jnp.float32)
            total = term if total is None else total + term
    return total


CHUNK = 64


def round_up(value, step):
    return -(-value // step) * step


def disco_body(src_ref, coef_ref, ext_ref, w_ref, out_ref, mix_ref):
    row_total = ext_ref.shape[0]
    slot_total = out_ref.shape[0]
    kinds = w_ref.shape[1] // w_ref.shape[0]
    channels = w_ref.shape[0]
    for r in range(row_total):
        mix_ref[r] = jnp.dot(ext_ref[r], w_ref[...], preferred_element_type=jnp.float32)

    def slot_step(s, carry):
        for c0 in range(0, out_ref.shape[1], CHUNK):
            acc = jnp.zeros((CHUNK, channels), jnp.float32)
            for a_i in range(3):
                row = src_ref[s * 3 + a_i]
                for b_i in range(3):
                    for k in range(kinds):
                        coef = coef_ref[((s * 3 + a_i) * 3 + b_i) * kinds + k]
                        acc = acc + coef * mix_ref[
                            row, pl.ds(c0 + 2 - b_i, CHUNK), pl.ds(k * channels, channels)
                        ]
            out_ref[s, pl.ds(c0, CHUNK), :] = acc
        return carry

    lax.fori_loop(0, slot_total, slot_step, 0)


def disco_apply(src, coef, ext, weight_flat, slot_total, lon_count):
    row_total, lon_pad, channels = ext.shape
    out_rows = round_up(lon_count, CHUNK)
    smem = pltpu.MemorySpace.SMEM if hasattr(pltpu, "MemorySpace") else pltpu.SMEM
    return pl.pallas_call(
        disco_body,
        out_shape=jax.ShapeDtypeStruct((slot_total, out_rows, channels), jnp.float32),
        in_specs=[
            pl.BlockSpec(memory_space=smem),
            pl.BlockSpec(memory_space=smem),
            pl.BlockSpec(memory_space=pltpu.VMEM),
            pl.BlockSpec(memory_space=pltpu.VMEM),
        ],
        out_specs=pl.BlockSpec(memory_space=pltpu.VMEM),
        scratch_shapes=[pltpu.VMEM((row_total, lon_pad, weight_flat.shape[1]), jnp.float32)],
    )(src, coef, ext, weight_flat)


def disco_tables(band_rows, disco_kernel, band_index, band_total, row_count):
    slot_ids = jnp.arange(row_count, dtype=jnp.int32)
    live_rows = band_rows[band_index]
    has_next = slot_ids + 1 < live_rows
    prev_band = jnp.maximum(band_index - 1, 0)
    next_band = jnp.minimum(band_index + 1, band_total - 1)
    base = band_index * row_count
    up_src = jnp.where(slot_ids == 0, 0, slot_ids)
    down_src = jnp.where(has_next, slot_ids + 2, row_count + 1)
    src = jnp.stack([up_src, slot_ids + 1, down_src], axis=1)
    up_row = jnp.where(
        slot_ids == 0, prev_band * row_count + band_rows[prev_band] - 1, base + slot_ids - 1
    )
    down_row = jnp.where(has_next, base + slot_ids + 1, next_band * row_count)
    kernel_row = jnp.stack([up_row, base + slot_ids, down_row], axis=1)
    kernel_row = jnp.clip(kernel_row, 0, disco_kernel.shape[0] - 1)
    up_ok = (slot_ids > 0) | (band_index > 0)
    down_ok = has_next | (band_index < band_total - 1)
    valid = jnp.stack([up_ok, jnp.ones_like(up_ok), down_ok], axis=1)
    gathered = disco_kernel[kernel_row]
    gathered = gathered.reshape(row_count, 3, 3, 3, disco_kernel.shape[2])
    coef = jnp.stack([gathered[:, 0, 2], gathered[:, 1, 1], gathered[:, 2, 0]], axis=1)
    coef = jnp.where(valid[:, :, None, None], coef, 0.0)
    return src.reshape(-1).astype(jnp.int32), coef.reshape(-1).astype(jnp.float32)


def halo_extend(masked, live_rows):
    row_count, lon_count, channels = masked.shape
    lat_total = lax.axis_size("lat")
    lon_total = lax.axis_size("lon")
    lat_up = [(i, (i + 1) % lat_total) for i in range(lat_total)]
    lat_down = [(j, i) for i, j in lat_up]
    lon_up = [(i, (i + 1) % lon_total) for i in range(lon_total)]
    lon_down = [(j, i) for i, j in lon_up]
    last_row = lax.dynamic_slice_in_dim(masked, live_rows - 1, 1, 0)
    from_above = lax.ppermute(last_row, "lat", lat_up)
    from_below = lax.ppermute(masked[0:1], "lat", lat_down)
    rows = jnp.concatenate([from_above, masked, from_below], axis=0)
    from_left = lax.ppermute(rows[:, lon_count - 1 : lon_count], "lon", lon_up)
    from_right = lax.ppermute(rows[:, 0:1], "lon", lon_down)
    lon_pad = round_up(round_up(lon_count, CHUNK) + 2, 16)
    pad = jnp.zeros((row_count + 2, lon_pad - lon_count - 2, channels), masked.dtype)
    return jnp.concatenate([from_left, rows, from_right, pad], axis=1)


def on_device(
    grad_output, band_rows, legendre, quad_weights, spectral_filter, disco_kernel, disco_weight
):
    row_count, lon_count, channels = grad_output.shape
    band_index = lax.axis_index("lat")
    band_total = lax.axis_size("lat")
    lon_index = lax.axis_index("lon")
    point_count = lon_count * lax.axis_size("lon")
    mode_count = legendre.shape[0] * band_total
    chan_share = channels // lax.axis_size("lon")
    slot_ids = jnp.arange(row_count, dtype=jnp.int32)
    live_rows = band_rows[band_index]
    live_slot = slot_ids < live_rows
    masked = jnp.where(live_slot[:, None, None], grad_output, jnp.zeros_like(grad_output))
    trig_parts = make_trig(mode_count, point_count)
    portion = lax.all_to_all(masked, "lon", split_axis=2, concat_axis=1, tiled=True)
    spectra = jnp.stack(
        [dot_split("rnc,nk->rkc", (portion,), parts).astype(jnp.bfloat16) for parts in trig_parts],
        axis=1,
    )
    columns = lax.all_to_all(spectra, "lat", split_axis=2, concat_axis=0, tiled=True)
    legendre_parts = split_bf16(legendre)
    coefficients = dot_split("mls,spmc->lpmc", legendre_parts, (columns,))
    filter_slice = lax.dynamic_slice_in_dim(spectral_filter, lon_index * chan_share, chan_share, 2)
    filter_real = filter_slice[0][:, None, :]
    filter_imag = filter_slice[1][:, None, :]
    real_part = coefficients[:, 0]
    imag_part = coefficients[:, 1]
    filtered = jnp.stack(
        [
            filter_real * real_part + filter_imag * imag_part,
            filter_real * imag_part - filter_imag * real_part,
        ],
        axis=1,
    )
    returned = dot_split("mls,lpmc->spmc", legendre_parts, split_bf16(filtered))
    returned = (returned * quad_weights[:, None, None, None]).astype(jnp.bfloat16)
    portion = lax.all_to_all(returned, "lat", split_axis=0, concat_axis=2, tiled=True)
    spectral_rows = None
    for p, parts in enumerate(trig_parts):
        term = dot_split("rkc,nk->rnc", (portion[:, p],), parts)
        spectral_rows = term if spectral_rows is None else spectral_rows + term
    spectral_rows = spectral_rows.astype(jnp.bfloat16)
    spectral = lax.all_to_all(spectral_rows, "lon", split_axis=1, concat_axis=2, tiled=True)
    ext = halo_extend(masked, live_rows)
    src_rows, coef = disco_tables(band_rows, disco_kernel, band_index, band_total, row_count)
    weight_flat = disco_weight.reshape(channels, -1)
    disco_full = disco_apply(src_rows, coef, ext, weight_flat, row_count, lon_count)
    disco_term = disco_full[:, :lon_count, :]
    summed = masked.astype(jnp.float32) + disco_term + spectral.astype(jnp.float32)
    return jnp.where(live_slot[:, None, None], summed, 0.0).astype(jnp.bfloat16)


def solution(mesh):
    placed = (P("lat", "lon", None), P(), P("lat", None, None), P(), P(), P(), P())
    return jax.shard_map(
        on_device, mesh=mesh, in_specs=placed, out_specs=P("lat", "lon", None), check_vma=False
    )
```

```python
import ml_dtypes
import numpy as np
import jax
import jax.numpy as jnp
from jax import lax
from jax.experimental import pallas as pl
from jax.experimental.pallas import tpu as pltpu
from jax.sharding import PartitionSpec as P


def make_trig(mode_count, point_count):
    step = 16 if point_count % 16 == 0 else 1
    coarse = np.arange(point_count // step)[:, None] * step
    fine = np.arange(step)[:, None]
    wavenumber = np.arange(mode_count)[None, :]
    coarse_angle = (wavenumber * coarse % point_count) * (2.0 * np.pi / point_count)
    fine_angle = (wavenumber * fine % point_count) * (2.0 * np.pi / point_count)
    scale = point_count ** (-0.5)
    coarse_cos = jnp.asarray((np.cos(coarse_angle) * scale).astype(np.float32))[:, None, :]
    coarse_sin = jnp.asarray((np.sin(coarse_angle) * scale).astype(np.float32))[:, None, :]
    fine_cos = jnp.asarray(np.cos(fine_angle).astype(np.float32))[None, :, :]
    fine_sin = jnp.asarray(np.sin(fine_angle).astype(np.float32))[None, :, :]
    cosine = coarse_cos * fine_cos - coarse_sin * fine_sin
    minus_sine = -(coarse_sin * fine_cos + coarse_cos * fine_sin)
    return tuple(
        split_bf16(part.reshape(point_count, mode_count)) for part in (cosine, minus_sine)
    )


def split_bf16(values):
    rounded = lax.reduce_precision(values, exponent_bits=8, mantissa_bits=7)
    return rounded.astype(jnp.bfloat16), (values - rounded).astype(jnp.bfloat16)


def dot_split(spec, left_parts, right_parts):
    total = None
    for lp in left_parts:
        for rp in right_parts:
            if lp is not left_parts[0] and rp is not right_parts[0]:
                continue
            term = jnp.einsum(spec, lp, rp, preferred_element_type=jnp.float32)
            total = term if total is None else total + term
    return total


CHUNK = 64


def round_up(value, step):
    return -(-value // step) * step


def disco_body(src_ref, coef_ref, ext_ref, w_ref, out_ref, mix_ref):
    row_total = ext_ref.shape[0]
    slot_total = out_ref.shape[0]
    kinds = w_ref.shape[1] // w_ref.shape[0]
    channels = w_ref.shape[0]
    for r in range(row_total):
        mix_ref[r] = jnp.dot(ext_ref[r], w_ref[...], preferred_element_type=jnp.float32)

    def slot_step(s, carry):
        for c0 in range(0, out_ref.shape[1], CHUNK):
            acc = jnp.zeros((CHUNK, channels), jnp.float32)
            for a_i in range(3):
                row = src_ref[s * 3 + a_i]
                for b_i in range(3):
                    for k in range(kinds):
                        coef = coef_ref[((s * 3 + a_i) * 3 + b_i) * kinds + k]
                        acc = acc + coef * mix_ref[
                            row, pl.ds(c0 + 2 - b_i, CHUNK), pl.ds(k * channels, channels)
                        ]
            out_ref[s, pl.ds(c0, CHUNK), :] = acc
        return carry

    lax.fori_loop(0, slot_total, slot_step, 0)


def disco_apply(src, coef, ext, weight_flat, slot_total, lon_count):
    row_total, lon_pad, channels = ext.shape
    out_rows = round_up(lon_count, CHUNK)
    smem = pltpu.MemorySpace.SMEM if hasattr(pltpu, "MemorySpace") else pltpu.SMEM
    return pl.pallas_call(
        disco_body,
        out_shape=jax.ShapeDtypeStruct((slot_total, out_rows, channels), jnp.float32),
        in_specs=[
            pl.BlockSpec(memory_space=smem),
            pl.BlockSpec(memory_space=smem),
            pl.BlockSpec(memory_space=pltpu.VMEM),
            pl.BlockSpec(memory_space=pltpu.VMEM),
        ],
        out_specs=pl.BlockSpec(memory_space=pltpu.VMEM),
        scratch_shapes=[pltpu.VMEM((row_total, lon_pad, weight_flat.shape[1]), jnp.float32)],
    )(src, coef, ext, weight_flat)


def disco_tables(band_rows, disco_kernel, band_index, band_total, row_count):
    slot_ids = jnp.arange(row_count, dtype=jnp.int32)
    live_rows = band_rows[band_index]
    has_next = slot_ids + 1 < live_rows
    prev_band = jnp.maximum(band_index - 1, 0)
    next_band = jnp.minimum(band_index + 1, band_total - 1)
    base = band_index * row_count
    up_src = jnp.where(slot_ids == 0, 0, slot_ids)
    down_src = jnp.where(has_next, slot_ids + 2, row_count + 1)
    src = jnp.stack([up_src, slot_ids + 1, down_src], axis=1)
    up_row = jnp.where(
        slot_ids == 0, prev_band * row_count + band_rows[prev_band] - 1, base + slot_ids - 1
    )
    down_row = jnp.where(has_next, base + slot_ids + 1, next_band * row_count)
    kernel_row = jnp.stack([up_row, base + slot_ids, down_row], axis=1)
    kernel_row = jnp.clip(kernel_row, 0, disco_kernel.shape[0] - 1)
    up_ok = (slot_ids > 0) | (band_index > 0)
    down_ok = has_next | (band_index < band_total - 1)
    valid = jnp.stack([up_ok, jnp.ones_like(up_ok), down_ok], axis=1)
    gathered = disco_kernel[kernel_row]
    gathered = gathered.reshape(row_count, 3, 3, 3, disco_kernel.shape[2])
    coef = jnp.stack([gathered[:, 0, 2], gathered[:, 1, 1], gathered[:, 2, 0]], axis=1)
    coef = jnp.where(valid[:, :, None, None], coef, 0.0)
    return src.astype(jnp.int32), coef.reshape(row_count, -1).astype(jnp.float32)


def disco_piece(src_rows, coef, ext, weight_flat, piece, pieces, lon_count):
    share = src_rows.shape[0] // pieces
    first = piece * share
    rows = lax.slice_in_dim(ext, first, first + share + 2, axis=0)
    local_src = (src_rows[first : first + share] - first).reshape(-1)
    local_coef = coef[first : first + share].reshape(-1)
    return disco_apply(local_src, local_coef, rows, weight_flat, share, lon_count)


def halo_extend(masked, live_rows):
    row_count, lon_count, channels = masked.shape
    lat_total = lax.axis_size("lat")
    lon_total = lax.axis_size("lon")
    lat_up = [(i, (i + 1) % lat_total) for i in range(lat_total)]
    lat_down = [(j, i) for i, j in lat_up]
    lon_up = [(i, (i + 1) % lon_total) for i in range(lon_total)]
    lon_down = [(j, i) for i, j in lon_up]
    last_row = lax.dynamic_slice_in_dim(masked, live_rows - 1, 1, 0)
    from_above = lax.ppermute(last_row, "lat", lat_up)
    from_below = lax.ppermute(masked[0:1], "lat", lat_down)
    rows = jnp.concatenate([from_above, masked, from_below], axis=0)
    from_left = lax.ppermute(rows[:, lon_count - 1 : lon_count], "lon", lon_up)
    from_right = lax.ppermute(rows[:, 0:1], "lon", lon_down)
    lon_pad = round_up(round_up(lon_count, CHUNK) + 2, 16)
    pad = jnp.zeros((row_count + 2, lon_pad - lon_count - 2, channels), masked.dtype)
    return jnp.concatenate([from_left, rows, from_right, pad], axis=1)


def on_device(
    grad_output, band_rows, legendre, quad_weights, spectral_filter, disco_kernel, disco_weight
):
    row_count, lon_count, channels = grad_output.shape
    band_index = lax.axis_index("lat")
    band_total = lax.axis_size("lat")
    lon_index = lax.axis_index("lon")
    point_count = lon_count * lax.axis_size("lon")
    mode_count = legendre.shape[0] * band_total
    chan_share = channels // lax.axis_size("lon")
    slot_ids = jnp.arange(row_count, dtype=jnp.int32)
    live_rows = band_rows[band_index]
    live_slot = slot_ids < live_rows
    masked = jnp.where(live_slot[:, None, None], grad_output, jnp.zeros_like(grad_output))
    trig_parts = make_trig(mode_count, point_count)
    portion = lax.all_to_all(masked, "lon", split_axis=2, concat_axis=1, tiled=True)
    spectra = jnp.stack(
        [dot_split("rnc,nk->rkc", (portion,), parts).astype(jnp.bfloat16) for parts in trig_parts],
        axis=1,
    )
    ext = halo_extend(masked, live_rows)
    src_rows, coef = disco_tables(band_rows, disco_kernel, band_index, band_total, row_count)
    weight_flat = disco_weight.reshape(channels, -1)
    pieces = 2 if row_count % 2 == 0 else 1
    disco_parts = []
    spectra, ext_now = lax.optimization_barrier((spectra, ext))
    columns = lax.all_to_all(spectra, "lat", split_axis=2, concat_axis=0, tiled=True)
    disco_parts.append(disco_piece(src_rows, coef, ext_now, weight_flat, 0, pieces, lon_count))
    columns, disco_parts[0] = lax.optimization_barrier((columns, disco_parts[0]))
    legendre_parts = split_bf16(legendre)
    coefficients = dot_split("mls,spmc->lpmc", legendre_parts, (columns,))
    filter_slice = lax.dynamic_slice_in_dim(spectral_filter, lon_index * chan_share, chan_share, 2)
    filter_real = filter_slice[0][:, None, :]
    filter_imag = filter_slice[1][:, None, :]
    real_part = coefficients[:, 0]
    imag_part = coefficients[:, 1]
    filtered = jnp.stack(
        [
            filter_real * real_part + filter_imag * imag_part,
            filter_real * imag_part - filter_imag * real_part,
        ],
        axis=1,
    )
    returned = dot_split("mls,lpmc->spmc", legendre_parts, split_bf16(filtered))
    returned = (returned * quad_weights[:, None, None, None]).astype(jnp.bfloat16)
    returned, ext_now = lax.optimization_barrier((returned, ext))
    portion = lax.all_to_all(returned, "lat", split_axis=0, concat_axis=2, tiled=True)
    for piece in range(1, pieces):
        disco_parts.append(
            disco_piece(src_rows, coef, ext_now, weight_flat, piece, pieces, lon_count)
        )
    portion, disco_parts = lax.optimization_barrier((portion, disco_parts))
    spectral_rows = None
    for p, parts in enumerate(trig_parts):
        term = dot_split("rkc,nk->rnc", (portion[:, p],), parts)
        spectral_rows = term if spectral_rows is None else spectral_rows + term
    spectral_rows = spectral_rows.astype(jnp.bfloat16)
    spectral = lax.all_to_all(spectral_rows, "lon", split_axis=1, concat_axis=2, tiled=True)
    disco_full = jnp.concatenate(disco_parts, axis=0)
    disco_term = disco_full[:, :lon_count, :]
    summed = masked.astype(jnp.float32) + disco_term + spectral.astype(jnp.float32)
    return jnp.where(live_slot[:, None, None], summed, 0.0).astype(jnp.bfloat16)


def solution(mesh):
    placed = (P("lat", "lon", None), P(), P("lat", None, None), P(), P(), P(), P())
    return jax.shard_map(
        on_device, mesh=mesh, in_specs=placed, out_specs=P("lat", "lon", None), check_vma=False
    )
```

```python
import ml_dtypes
import numpy as np
import jax
import jax.numpy as jnp
from jax import lax
from jax.experimental import pallas as pl
from jax.experimental.pallas import tpu as pltpu
from jax.sharding import PartitionSpec as P


def make_trig(mode_count, point_count):
    step = 16 if point_count % 16 == 0 else 1
    coarse = np.arange(point_count // step)[:, None] * step
    fine = np.arange(step)[:, None]
    wavenumber = np.arange(mode_count)[None, :]
    coarse_angle = (wavenumber * coarse % point_count) * (2.0 * np.pi / point_count)
    fine_angle = (wavenumber * fine % point_count) * (2.0 * np.pi / point_count)
    scale = point_count ** (-0.5)
    coarse_cos = jnp.asarray((np.cos(coarse_angle) * scale).astype(np.float32))[:, None, :]
    coarse_sin = jnp.asarray((np.sin(coarse_angle) * scale).astype(np.float32))[:, None, :]
    fine_cos = jnp.asarray(np.cos(fine_angle).astype(np.float32))[None, :, :]
    fine_sin = jnp.asarray(np.sin(fine_angle).astype(np.float32))[None, :, :]
    cosine = coarse_cos * fine_cos - coarse_sin * fine_sin
    minus_sine = -(coarse_sin * fine_cos + coarse_cos * fine_sin)
    return tuple(
        split_bf16(part.reshape(point_count, mode_count)) for part in (cosine, minus_sine)
    )


def split_bf16(values):
    rounded = lax.reduce_precision(values, exponent_bits=8, mantissa_bits=7)
    return rounded.astype(jnp.bfloat16), (values - rounded).astype(jnp.bfloat16)


def dot_split(spec, left_parts, right_parts):
    total = None
    for lp in left_parts:
        for rp in right_parts:
            if lp is not left_parts[0] and rp is not right_parts[0]:
                continue
            term = jnp.einsum(spec, lp, rp, preferred_element_type=jnp.float32)
            total = term if total is None else total + term
    return total


CHUNK = 64


def round_up(value, step):
    return -(-value // step) * step


def disco_body(src_ref, coef_ref, ext_ref, w_ref, out_ref, mix_ref):
    row_total = ext_ref.shape[0]
    slot_total = out_ref.shape[0]
    kinds = w_ref.shape[1] // w_ref.shape[0]
    channels = w_ref.shape[0]
    for r in range(row_total):
        mix_ref[r] = jnp.dot(ext_ref[r], w_ref[...], preferred_element_type=jnp.float32)

    def slot_step(s, carry):
        for c0 in range(0, out_ref.shape[1], CHUNK):
            acc = jnp.zeros((CHUNK, channels), jnp.float32)
            for a_i in range(3):
                row = src_ref[s * 3 + a_i]
                for b_i in range(3):
                    for k in range(kinds):
                        coef = coef_ref[((s * 3 + a_i) * 3 + b_i) * kinds + k]
                        acc = acc + coef * mix_ref[
                            row, pl.ds(c0 + 2 - b_i, CHUNK), pl.ds(k * channels, channels)
                        ]
            out_ref[s, pl.ds(c0, CHUNK), :] = acc
        return carry

    lax.fori_loop(0, slot_total, slot_step, 0)


def disco_apply(src, coef, ext, weight_flat, slot_total, lon_count):
    row_total, lon_pad, channels = ext.shape
    out_rows = round_up(lon_count, CHUNK)
    smem = pltpu.MemorySpace.SMEM if hasattr(pltpu, "MemorySpace") else pltpu.SMEM
    return pl.pallas_call(
        disco_body,
        out_shape=jax.ShapeDtypeStruct((slot_total, out_rows, channels), jnp.float32),
        in_specs=[
            pl.BlockSpec(memory_space=smem),
            pl.BlockSpec(memory_space=smem),
            pl.BlockSpec(memory_space=pltpu.VMEM),
            pl.BlockSpec(memory_space=pltpu.VMEM),
        ],
        out_specs=pl.BlockSpec(memory_space=pltpu.VMEM),
        scratch_shapes=[pltpu.VMEM((row_total, lon_pad, weight_flat.shape[1]), jnp.float32)],
    )(src, coef, ext, weight_flat)


def disco_tables(band_rows, disco_kernel, band_index, band_total, row_count):
    slot_ids = jnp.arange(row_count, dtype=jnp.int32)
    live_rows = band_rows[band_index]
    has_next = slot_ids + 1 < live_rows
    prev_band = jnp.maximum(band_index - 1, 0)
    next_band = jnp.minimum(band_index + 1, band_total - 1)
    base = band_index * row_count
    up_src = jnp.where(slot_ids == 0, 0, slot_ids)
    down_src = jnp.where(has_next, slot_ids + 2, row_count + 1)
    src = jnp.stack([up_src, slot_ids + 1, down_src], axis=1)
    up_row = jnp.where(
        slot_ids == 0, prev_band * row_count + band_rows[prev_band] - 1, base + slot_ids - 1
    )
    down_row = jnp.where(has_next, base + slot_ids + 1, next_band * row_count)
    kernel_row = jnp.stack([up_row, base + slot_ids, down_row], axis=1)
    kernel_row = jnp.clip(kernel_row, 0, disco_kernel.shape[0] - 1)
    up_ok = (slot_ids > 0) | (band_index > 0)
    down_ok = has_next | (band_index < band_total - 1)
    valid = jnp.stack([up_ok, jnp.ones_like(up_ok), down_ok], axis=1)
    gathered = disco_kernel[kernel_row]
    gathered = gathered.reshape(row_count, 3, 3, 3, disco_kernel.shape[2])
    coef = jnp.stack([gathered[:, 0, 2], gathered[:, 1, 1], gathered[:, 2, 0]], axis=1)
    coef = jnp.where(valid[:, :, None, None], coef, 0.0)
    return src.astype(jnp.int32), coef.reshape(row_count, -1).astype(jnp.float32)


def disco_piece(src_rows, coef, ext, weight_flat, piece, pieces, lon_count):
    slot_total = src_rows.shape[0]
    first = piece * slot_total // pieces
    last = (piece + 1) * slot_total // pieces
    rows = lax.slice_in_dim(ext, first, last + 2, axis=0)
    local_src = (src_rows[first:last] - first).reshape(-1)
    local_coef = coef[first:last].reshape(-1)
    return disco_apply(local_src, local_coef, rows, weight_flat, last - first, lon_count)


def halo_extend(masked, live_rows):
    row_count, lon_count, channels = masked.shape
    lat_total = lax.axis_size("lat")
    lon_total = lax.axis_size("lon")
    lat_up = [(i, (i + 1) % lat_total) for i in range(lat_total)]
    lat_down = [(j, i) for i, j in lat_up]
    lon_up = [(i, (i + 1) % lon_total) for i in range(lon_total)]
    lon_down = [(j, i) for i, j in lon_up]
    last_row = lax.dynamic_slice_in_dim(masked, live_rows - 1, 1, 0)
    from_above = lax.ppermute(last_row, "lat", lat_up)
    from_below = lax.ppermute(masked[0:1], "lat", lat_down)
    rows = jnp.concatenate([from_above, masked, from_below], axis=0)
    from_left = lax.ppermute(rows[:, lon_count - 1 : lon_count], "lon", lon_up)
    from_right = lax.ppermute(rows[:, 0:1], "lon", lon_down)
    lon_pad = round_up(round_up(lon_count, CHUNK) + 2, 16)
    pad = jnp.zeros((row_count + 2, lon_pad - lon_count - 2, channels), masked.dtype)
    return jnp.concatenate([from_left, rows, from_right, pad], axis=1)


def on_device(
    grad_output, band_rows, legendre, quad_weights, spectral_filter, disco_kernel, disco_weight
):
    row_count, lon_count, channels = grad_output.shape
    band_index = lax.axis_index("lat")
    band_total = lax.axis_size("lat")
    lon_index = lax.axis_index("lon")
    point_count = lon_count * lax.axis_size("lon")
    mode_count = legendre.shape[0] * band_total
    chan_share = channels // lax.axis_size("lon")
    slot_ids = jnp.arange(row_count, dtype=jnp.int32)
    live_rows = band_rows[band_index]
    live_slot = slot_ids < live_rows
    masked = jnp.where(live_slot[:, None, None], grad_output, jnp.zeros_like(grad_output))
    trig_parts = make_trig(mode_count, point_count)
    portion = lax.all_to_all(masked, "lon", split_axis=2, concat_axis=1, tiled=True)
    spectra = jnp.stack(
        [dot_split("rnc,nk->rkc", (portion,), parts).astype(jnp.bfloat16) for parts in trig_parts],
        axis=1,
    )
    ext = halo_extend(masked, live_rows)
    src_rows, coef = disco_tables(band_rows, disco_kernel, band_index, band_total, row_count)
    weight_flat = disco_weight.reshape(channels, -1)
    pieces = min(3, row_count)
    disco_parts = []
    spectra, ext_now = lax.optimization_barrier((spectra, ext))
    columns = lax.all_to_all(spectra, "lat", split_axis=2, concat_axis=0, tiled=True)
    disco_parts.append(disco_piece(src_rows, coef, ext_now, weight_flat, 0, pieces, lon_count))
    columns, disco_parts[0] = lax.optimization_barrier((columns, disco_parts[0]))
    legendre_parts = split_bf16(legendre)
    coefficients = dot_split("mls,spmc->lpmc", legendre_parts, (columns,))
    filter_slice = lax.dynamic_slice_in_dim(spectral_filter, lon_index * chan_share, chan_share, 2)
    filter_real = filter_slice[0][:, None, :]
    filter_imag = filter_slice[1][:, None, :]
    real_part = coefficients[:, 0]
    imag_part = coefficients[:, 1]
    filtered = jnp.stack(
        [
            filter_real * real_part + filter_imag * imag_part,
            filter_real * imag_part - filter_imag * real_part,
        ],
        axis=1,
    )
    returned = dot_split("mls,lpmc->spmc", legendre_parts, split_bf16(filtered))
    returned = (returned * quad_weights[:, None, None, None]).astype(jnp.bfloat16)
    returned, ext_now = lax.optimization_barrier((returned, ext))
    portion = lax.all_to_all(returned, "lat", split_axis=0, concat_axis=2, tiled=True)
    disco_parts.append(disco_piece(src_rows, coef, ext_now, weight_flat, 1, pieces, lon_count))
    portion, disco_parts = lax.optimization_barrier((portion, disco_parts))
    spectral_rows = None
    for p, parts in enumerate(trig_parts):
        term = dot_split("rkc,nk->rnc", (portion[:, p],), parts)
        spectral_rows = term if spectral_rows is None else spectral_rows + term
    spectral_rows = spectral_rows.astype(jnp.bfloat16)
    spectral_rows, ext_now = lax.optimization_barrier((spectral_rows, ext))
    spectral = lax.all_to_all(spectral_rows, "lon", split_axis=1, concat_axis=2, tiled=True)
    for piece in range(2, pieces):
        disco_parts.append(
            disco_piece(src_rows, coef, ext_now, weight_flat, piece, pieces, lon_count)
        )
    spectral, disco_parts = lax.optimization_barrier((spectral, disco_parts))
    disco_full = jnp.concatenate(disco_parts, axis=0)
    disco_term = disco_full[:, :lon_count, :]
    summed = masked.astype(jnp.float32) + disco_term + spectral.astype(jnp.float32)
    return jnp.where(live_slot[:, None, None], summed, 0.0).astype(jnp.bfloat16)


def solution(mesh):
    placed = (P("lat", "lon", None), P(), P("lat", None, None), P(), P(), P(), P())
    return jax.shard_map(
        on_device, mesh=mesh, in_specs=placed, out_specs=P("lat", "lon", None), check_vma=False
    )
```

```python
import ml_dtypes
import numpy as np
import jax
import jax.numpy as jnp
from jax import lax
from jax.experimental import pallas as pl
from jax.experimental.pallas import tpu as pltpu
from jax.sharding import PartitionSpec as P


def make_trig(mode_count, point_count):
    step = 16 if point_count % 16 == 0 else 1
    coarse = np.arange(point_count // step)[:, None] * step
    fine = np.arange(step)[:, None]
    wavenumber = np.arange(mode_count)[None, :]
    coarse_angle = (wavenumber * coarse % point_count) * (2.0 * np.pi / point_count)
    fine_angle = (wavenumber * fine % point_count) * (2.0 * np.pi / point_count)
    scale = point_count ** (-0.5)
    coarse_cos = jnp.asarray((np.cos(coarse_angle) * scale).astype(np.float32))[:, None, :]
    coarse_sin = jnp.asarray((np.sin(coarse_angle) * scale).astype(np.float32))[:, None, :]
    fine_cos = jnp.asarray(np.cos(fine_angle).astype(np.float32))[None, :, :]
    fine_sin = jnp.asarray(np.sin(fine_angle).astype(np.float32))[None, :, :]
    cosine = coarse_cos * fine_cos - coarse_sin * fine_sin
    minus_sine = -(coarse_sin * fine_cos + coarse_cos * fine_sin)
    return tuple(
        split_bf16(part.reshape(point_count, mode_count)) for part in (cosine, minus_sine)
    )


def split_bf16(values):
    rounded = lax.reduce_precision(values, exponent_bits=8, mantissa_bits=7)
    return rounded.astype(jnp.bfloat16), (values - rounded).astype(jnp.bfloat16)


def dot_split(spec, left_parts, right_parts):
    total = None
    for lp in left_parts:
        for rp in right_parts:
            if lp is not left_parts[0] and rp is not right_parts[0]:
                continue
            term = jnp.einsum(spec, lp, rp, preferred_element_type=jnp.float32)
            total = term if total is None else total + term
    return total


CHUNK = 64


def round_up(value, step):
    return -(-value // step) * step


def disco_body(src_ref, coef_ref, ext_ref, w_ref, out_ref, mix_ref):
    row_total = ext_ref.shape[0]
    slot_total = out_ref.shape[0]
    kinds = w_ref.shape[1] // w_ref.shape[0]
    channels = w_ref.shape[0]
    for r in range(row_total):
        mix_ref[r] = jnp.dot(ext_ref[r], w_ref[...], preferred_element_type=jnp.float32)

    def slot_step(s, carry):
        for c0 in range(0, out_ref.shape[1], CHUNK):
            acc = jnp.zeros((CHUNK, channels), jnp.float32)
            for a_i in range(3):
                row = src_ref[s * 3 + a_i]
                for b_i in range(3):
                    for k in range(kinds):
                        coef = coef_ref[((s * 3 + a_i) * 3 + b_i) * kinds + k]
                        acc = acc + coef * mix_ref[
                            row, pl.ds(c0 + 2 - b_i, CHUNK), pl.ds(k * channels, channels)
                        ]
            out_ref[s, pl.ds(c0, CHUNK), :] = acc
        return carry

    lax.fori_loop(0, slot_total, slot_step, 0)


def disco_apply(src, coef, ext, weight_flat, slot_total, lon_count):
    row_total, lon_pad, channels = ext.shape
    out_rows = round_up(lon_count, CHUNK)
    smem = pltpu.MemorySpace.SMEM if hasattr(pltpu, "MemorySpace") else pltpu.SMEM
    return pl.pallas_call(
        disco_body,
        out_shape=jax.ShapeDtypeStruct((slot_total, out_rows, channels), jnp.float32),
        in_specs=[
            pl.BlockSpec(memory_space=smem),
            pl.BlockSpec(memory_space=smem),
            pl.BlockSpec(memory_space=pltpu.VMEM),
            pl.BlockSpec(memory_space=pltpu.VMEM),
        ],
        out_specs=pl.BlockSpec(memory_space=pltpu.VMEM),
        scratch_shapes=[pltpu.VMEM((row_total, lon_pad, weight_flat.shape[1]), jnp.float32)],
    )(src, coef, ext, weight_flat)


def disco_tables(band_rows, disco_kernel, band_index, band_total, row_count):
    slot_ids = jnp.arange(row_count, dtype=jnp.int32)
    live_rows = band_rows[band_index]
    has_next = slot_ids + 1 < live_rows
    prev_band = jnp.maximum(band_index - 1, 0)
    next_band = jnp.minimum(band_index + 1, band_total - 1)
    base = band_index * row_count
    up_src = jnp.where(slot_ids == 0, 0, slot_ids)
    down_src = jnp.where(has_next, slot_ids + 2, row_count + 1)
    src = jnp.stack([up_src, slot_ids + 1, down_src], axis=1)
    up_row = jnp.where(
        slot_ids == 0, prev_band * row_count + band_rows[prev_band] - 1, base + slot_ids - 1
    )
    down_row = jnp.where(has_next, base + slot_ids + 1, next_band * row_count)
    kernel_row = jnp.stack([up_row, base + slot_ids, down_row], axis=1)
    kernel_row = jnp.clip(kernel_row, 0, disco_kernel.shape[0] - 1)
    up_ok = (slot_ids > 0) | (band_index > 0)
    down_ok = has_next | (band_index < band_total - 1)
    valid = jnp.stack([up_ok, jnp.ones_like(up_ok), down_ok], axis=1)
    gathered = disco_kernel[kernel_row]
    gathered = gathered.reshape(row_count, 3, 3, 3, disco_kernel.shape[2])
    coef = jnp.stack([gathered[:, 0, 2], gathered[:, 1, 1], gathered[:, 2, 0]], axis=1)
    coef = jnp.where(valid[:, :, None, None], coef, 0.0)
    return src.astype(jnp.int32), coef.reshape(row_count, -1).astype(jnp.float32)


def disco_piece(src_rows, coef, ext, weight_flat, piece, pieces, lon_count):
    slot_total = src_rows.shape[0]
    first = piece * slot_total // pieces
    last = (piece + 1) * slot_total // pieces
    rows = lax.slice_in_dim(ext, first, last + 2, axis=0)
    local_src = (src_rows[first:last] - first).reshape(-1)
    local_coef = coef[first:last].reshape(-1)
    return disco_apply(local_src, local_coef, rows, weight_flat, last - first, lon_count)


def halo_extend(masked, live_rows):
    row_count, lon_count, channels = masked.shape
    lat_total = lax.axis_size("lat")
    lon_total = lax.axis_size("lon")
    lat_up = [(i, (i + 1) % lat_total) for i in range(lat_total)]
    lat_down = [(j, i) for i, j in lat_up]
    lon_up = [(i, (i + 1) % lon_total) for i in range(lon_total)]
    lon_down = [(j, i) for i, j in lon_up]
    last_row = lax.dynamic_slice_in_dim(masked, live_rows - 1, 1, 0)
    from_above = lax.ppermute(last_row, "lat", lat_up)
    from_below = lax.ppermute(masked[0:1], "lat", lat_down)
    rows = jnp.concatenate([from_above, masked, from_below], axis=0)
    from_left = lax.ppermute(rows[:, lon_count - 1 : lon_count], "lon", lon_up)
    from_right = lax.ppermute(rows[:, 0:1], "lon", lon_down)
    lon_pad = round_up(round_up(lon_count, CHUNK) + 2, 16)
    pad = jnp.zeros((row_count + 2, lon_pad - lon_count - 2, channels), masked.dtype)
    return jnp.concatenate([from_left, rows, from_right, pad], axis=1)


def spectral_by_channels(
    masked, legendre, quad_weights, spectral_filter, trig_parts, ext, disco_work
):
    channels = masked.shape[2]
    lon_index = lax.axis_index("lon")
    chan_share = channels // lax.axis_size("lon")
    disco_parts = []
    portion = lax.all_to_all(masked, "lon", split_axis=2, concat_axis=1, tiled=True)
    spectra = jnp.stack(
        [dot_split("rnc,nk->rkc", (portion,), parts).astype(jnp.bfloat16) for parts in trig_parts],
        axis=1,
    )
    spectra, ext_now = lax.optimization_barrier((spectra, ext))
    columns = lax.all_to_all(spectra, "lat", split_axis=2, concat_axis=0, tiled=True)
    disco_parts.append(disco_work(ext_now, 0))
    columns, disco_parts[0] = lax.optimization_barrier((columns, disco_parts[0]))
    legendre_parts = split_bf16(legendre)
    coefficients = dot_split("mls,spmc->lpmc", legendre_parts, (columns,))
    filter_slice = lax.dynamic_slice_in_dim(spectral_filter, lon_index * chan_share, chan_share, 2)
    filter_real = filter_slice[0][:, None, :]
    filter_imag = filter_slice[1][:, None, :]
    real_part = coefficients[:, 0]
    imag_part = coefficients[:, 1]
    filtered = jnp.stack(
        [
            filter_real * real_part + filter_imag * imag_part,
            filter_real * imag_part - filter_imag * real_part,
        ],
        axis=1,
    )
    returned = dot_split("mls,lpmc->spmc", legendre_parts, split_bf16(filtered))
    returned = (returned * quad_weights[:, None, None, None]).astype(jnp.bfloat16)
    returned, ext_now = lax.optimization_barrier((returned, ext))
    portion = lax.all_to_all(returned, "lat", split_axis=0, concat_axis=2, tiled=True)
    disco_parts.append(disco_work(ext_now, 1))
    portion, disco_parts = lax.optimization_barrier((portion, disco_parts))
    spectral_rows = None
    for p, parts in enumerate(trig_parts):
        term = dot_split("rkc,nk->rnc", (portion[:, p],), parts)
        spectral_rows = term if spectral_rows is None else spectral_rows + term
    spectral_rows = spectral_rows.astype(jnp.bfloat16)
    spectral_rows, ext_now = lax.optimization_barrier((spectral_rows, ext))
    spectral = lax.all_to_all(spectral_rows, "lon", split_axis=1, concat_axis=2, tiled=True)
    disco_parts.append(disco_work(ext_now, 2))
    spectral, disco_parts = lax.optimization_barrier((spectral, disco_parts))
    return spectral, disco_parts


def filter_modes(coefficients, spectral_filter):
    filter_real = spectral_filter[0][:, None, :]
    filter_imag = spectral_filter[1][:, None, :]
    real_part = coefficients[:, 0]
    imag_part = coefficients[:, 1]
    return jnp.stack(
        [
            filter_real * real_part + filter_imag * imag_part,
            filter_real * imag_part - filter_imag * real_part,
        ],
        axis=1,
    )


def spectral_by_modes(masked, legendre, quad_weights, spectral_filter, trig_parts, ext, disco_work):
    both = ("lat", "lon")
    lon_total = lax.axis_size("lon")
    mode_share = legendre.shape[0] // lon_total
    disco_parts = []
    portion = lax.all_to_all(masked, "lon", split_axis=0, concat_axis=1, tiled=True)
    spectra = jnp.stack(
        [dot_split("rnc,nk->rkc", (portion,), parts).astype(jnp.bfloat16) for parts in trig_parts],
        axis=1,
    )
    spectra, ext_now = lax.optimization_barrier((spectra, ext))
    columns = lax.all_to_all(spectra, both, split_axis=2, concat_axis=0, tiled=True)
    disco_parts.append(disco_work(ext_now, 0))
    columns, disco_parts[0] = lax.optimization_barrier((columns, disco_parts[0]))
    own_legendre = lax.dynamic_slice_in_dim(
        legendre, lax.axis_index("lon") * mode_share, mode_share, 0
    )
    legendre_parts = split_bf16(own_legendre)
    coefficients = dot_split("mls,spmc->lpmc", legendre_parts, (columns,))
    filtered = filter_modes(coefficients, spectral_filter)
    returned = dot_split("mls,lpmc->spmc", legendre_parts, split_bf16(filtered))
    returned = (returned * quad_weights[:, None, None, None]).astype(jnp.bfloat16)
    returned, ext_now = lax.optimization_barrier((returned, ext))
    portion = lax.all_to_all(returned, both, split_axis=0, concat_axis=2, tiled=True)
    disco_parts.append(disco_work(ext_now, 1))
    portion, disco_parts = lax.optimization_barrier((portion, disco_parts))
    spectral_rows = None
    for p, parts in enumerate(trig_parts):
        term = dot_split("rkc,nk->rnc", (portion[:, p],), parts)
        spectral_rows = term if spectral_rows is None else spectral_rows + term
    spectral_rows = spectral_rows.astype(jnp.bfloat16)
    spectral_rows, ext_now = lax.optimization_barrier((spectral_rows, ext))
    spectral = lax.all_to_all(spectral_rows, "lon", split_axis=1, concat_axis=0, tiled=True)
    disco_parts.append(disco_work(ext_now, 2))
    spectral, disco_parts = lax.optimization_barrier((spectral, disco_parts))
    return spectral, disco_parts


def on_device(
    grad_output, band_rows, legendre, quad_weights, spectral_filter, disco_kernel, disco_weight
):
    row_count, lon_count, channels = grad_output.shape
    band_index = lax.axis_index("lat")
    band_total = lax.axis_size("lat")
    lon_total = lax.axis_size("lon")
    point_count = lon_count * lon_total
    mode_count = legendre.shape[0] * band_total
    slot_ids = jnp.arange(row_count, dtype=jnp.int32)
    live_rows = band_rows[band_index]
    live_slot = slot_ids < live_rows
    masked = jnp.where(live_slot[:, None, None], grad_output, jnp.zeros_like(grad_output))
    trig_parts = make_trig(mode_count, point_count)
    ext = halo_extend(masked, live_rows)
    src_rows, coef = disco_tables(band_rows, disco_kernel, band_index, band_total, row_count)
    weight_flat = disco_weight.reshape(channels, -1)
    pieces = min(3, row_count)

    def disco_work(ext_now, piece):
        return disco_piece(src_rows, coef, ext_now, weight_flat, piece, pieces, lon_count)

    by_modes = legendre.shape[0] % lon_total == 0 and row_count % lon_total == 0
    path = spectral_by_modes if by_modes else spectral_by_channels
    spectral, disco_parts = path(
        masked, legendre, quad_weights, spectral_filter, trig_parts, ext, disco_work
    )
    disco_full = jnp.concatenate(disco_parts, axis=0)
    disco_term = disco_full[:, :lon_count, :]
    summed = masked.astype(jnp.float32) + disco_term + spectral.astype(jnp.float32)
    return jnp.where(live_slot[:, None, None], summed, 0.0).astype(jnp.bfloat16)


def solution(mesh):
    placed = (P("lat", "lon", None), P(), P("lat", None, None), P(), P(), P(), P())
    return jax.shard_map(
        on_device, mesh=mesh, in_specs=placed, out_specs=P("lat", "lon", None), check_vma=False
    )
```

```python
import functools

import ml_dtypes
import numpy as np
import jax
import jax.numpy as jnp
from jax import lax
from jax.experimental import pallas as pl
from jax.experimental.pallas import tpu as pltpu
from jax.sharding import PartitionSpec as P


def make_trig(mode_count, point_count):
    step = 16 if point_count % 16 == 0 else 1
    coarse = np.arange(point_count // step)[:, None] * step
    fine = np.arange(step)[:, None]
    wavenumber = np.arange(mode_count)[None, :]
    coarse_angle = (wavenumber * coarse % point_count) * (2.0 * np.pi / point_count)
    fine_angle = (wavenumber * fine % point_count) * (2.0 * np.pi / point_count)
    scale = point_count ** (-0.5)
    coarse_cos = jnp.asarray((np.cos(coarse_angle) * scale).astype(np.float32))[:, None, :]
    coarse_sin = jnp.asarray((np.sin(coarse_angle) * scale).astype(np.float32))[:, None, :]
    fine_cos = jnp.asarray(np.cos(fine_angle).astype(np.float32))[None, :, :]
    fine_sin = jnp.asarray(np.sin(fine_angle).astype(np.float32))[None, :, :]
    cosine = coarse_cos * fine_cos - coarse_sin * fine_sin
    minus_sine = -(coarse_sin * fine_cos + coarse_cos * fine_sin)
    return tuple(
        split_bf16(part.reshape(point_count, mode_count)) for part in (cosine, minus_sine)
    )


def split_bf16(values):
    rounded = lax.reduce_precision(values, exponent_bits=8, mantissa_bits=7)
    return rounded.astype(jnp.bfloat16), (values - rounded).astype(jnp.bfloat16)


def dot_split(spec, left_parts, right_parts):
    total = None
    for lp in left_parts:
        for rp in right_parts:
            if lp is not left_parts[0] and rp is not right_parts[0]:
                continue
            term = jnp.einsum(spec, lp, rp, preferred_element_type=jnp.float32)
            total = term if total is None else total + term
    return total


CHUNK = 64


def round_up(value, step):
    return -(-value // step) * step


def disco_body(first, last, src_ref, coef_ref, ext_ref, w_ref, out_ref, mix_ref):
    kinds = w_ref.shape[1] // w_ref.shape[0]
    channels = w_ref.shape[0]
    for r in range(last - first + 2):
        mix_ref[r] = jnp.dot(ext_ref[first + r], w_ref[...], preferred_element_type=jnp.float32)

    def slot_step(s, carry):
        for c0 in range(0, out_ref.shape[1], CHUNK):
            acc = jnp.zeros((CHUNK, channels), jnp.float32)
            for a_i in range(3):
                row = src_ref[(first + s) * 3 + a_i] - first
                for b_i in range(3):
                    for k in range(kinds):
                        coef = coef_ref[(((first + s) * 3 + a_i) * 3 + b_i) * kinds + k]
                        acc = acc + coef * mix_ref[
                            row, pl.ds(c0 + 2 - b_i, CHUNK), pl.ds(k * channels, channels)
                        ]
            out_ref[s, pl.ds(c0, CHUNK), :] = acc
        return carry

    lax.fori_loop(0, last - first, slot_step, 0)


def disco_piece(src_rows, coef, ext, weight_flat, piece, pieces, lon_count):
    slot_total = ext.shape[0] - 2
    first = piece * slot_total // pieces
    last = (piece + 1) * slot_total // pieces
    lon_pad, channels = ext.shape[1:]
    out_rows = round_up(lon_count, CHUNK)
    smem = pltpu.MemorySpace.SMEM if hasattr(pltpu, "MemorySpace") else pltpu.SMEM
    return pl.pallas_call(
        functools.partial(disco_body, first, last),
        out_shape=jax.ShapeDtypeStruct((last - first, out_rows, channels), jnp.float32),
        in_specs=[
            pl.BlockSpec(memory_space=smem),
            pl.BlockSpec(memory_space=smem),
            pl.BlockSpec(memory_space=pltpu.VMEM),
            pl.BlockSpec(memory_space=pltpu.VMEM),
        ],
        out_specs=pl.BlockSpec(memory_space=pltpu.VMEM),
        scratch_shapes=[pltpu.VMEM((last - first + 2, lon_pad, weight_flat.shape[1]), jnp.float32)],
    )(src_rows, coef, ext, weight_flat)


def disco_tables(band_rows, disco_kernel, band_index, band_total, row_count):
    slot_ids = jnp.arange(row_count, dtype=jnp.int32)
    live_rows = band_rows[band_index]
    has_next = slot_ids + 1 < live_rows
    prev_band = jnp.maximum(band_index - 1, 0)
    next_band = jnp.minimum(band_index + 1, band_total - 1)
    base = band_index * row_count
    up_src = jnp.where(slot_ids == 0, 0, slot_ids)
    down_src = jnp.where(has_next, slot_ids + 2, row_count + 1)
    src = jnp.stack([up_src, slot_ids + 1, down_src], axis=1)
    up_row = jnp.where(
        slot_ids == 0, prev_band * row_count + band_rows[prev_band] - 1, base + slot_ids - 1
    )
    down_row = jnp.where(has_next, base + slot_ids + 1, next_band * row_count)
    kernel_row = jnp.stack([up_row, base + slot_ids, down_row], axis=1)
    kernel_row = jnp.clip(kernel_row, 0, disco_kernel.shape[0] - 1)
    up_ok = (slot_ids > 0) | (band_index > 0)
    down_ok = has_next | (band_index < band_total - 1)
    valid = jnp.stack([up_ok, jnp.ones_like(up_ok), down_ok], axis=1)
    gathered = disco_kernel[kernel_row]
    gathered = gathered.reshape(row_count, 3, 3, 3, disco_kernel.shape[2])
    coef = jnp.stack([gathered[:, 0, 2], gathered[:, 1, 1], gathered[:, 2, 0]], axis=1)
    coef = jnp.where(valid[:, :, None, None], coef, 0.0)
    return src.reshape(-1).astype(jnp.int32), coef.reshape(-1).astype(jnp.float32)


def halo_extend(masked, live_rows):
    row_count, lon_count, channels = masked.shape
    lat_total = lax.axis_size("lat")
    lon_total = lax.axis_size("lon")
    lat_up = [(i, (i + 1) % lat_total) for i in range(lat_total)]
    lat_down = [(j, i) for i, j in lat_up]
    lon_up = [(i, (i + 1) % lon_total) for i in range(lon_total)]
    lon_down = [(j, i) for i, j in lon_up]
    last_row = lax.dynamic_slice_in_dim(masked, live_rows - 1, 1, 0)
    from_above = lax.ppermute(last_row, "lat", lat_up)
    from_below = lax.ppermute(masked[0:1], "lat", lat_down)
    rows = jnp.concatenate([from_above, masked, from_below], axis=0)
    from_left = lax.ppermute(rows[:, lon_count - 1 : lon_count], "lon", lon_up)
    from_right = lax.ppermute(rows[:, 0:1], "lon", lon_down)
    lon_pad = round_up(round_up(lon_count, CHUNK) + 2, 16)
    pad = jnp.zeros((row_count + 2, lon_pad - lon_count - 2, channels), masked.dtype)
    return jnp.concatenate([from_left, rows, from_right, pad], axis=1)


def spectral_by_channels(
    masked, legendre, quad_weights, spectral_filter, trig_parts, ext, disco_work
):
    channels = masked.shape[2]
    lon_index = lax.axis_index("lon")
    chan_share = channels // lax.axis_size("lon")
    disco_parts = []
    portion = lax.all_to_all(masked, "lon", split_axis=2, concat_axis=1, tiled=True)
    spectra = jnp.stack(
        [dot_split("rnc,nk->rkc", (portion,), parts).astype(jnp.bfloat16) for parts in trig_parts],
        axis=1,
    )
    spectra, ext_now = lax.optimization_barrier((spectra, ext))
    columns = lax.all_to_all(spectra, "lat", split_axis=2, concat_axis=0, tiled=True)
    disco_parts.append(disco_work(ext_now, 0))
    columns, disco_parts[0] = lax.optimization_barrier((columns, disco_parts[0]))
    legendre_parts = split_bf16(legendre)
    coefficients = dot_split("mls,spmc->lpmc", legendre_parts, (columns,))
    filter_slice = lax.dynamic_slice_in_dim(spectral_filter, lon_index * chan_share, chan_share, 2)
    filter_real = filter_slice[0][:, None, :]
    filter_imag = filter_slice[1][:, None, :]
    real_part = coefficients[:, 0]
    imag_part = coefficients[:, 1]
    filtered = jnp.stack(
        [
            filter_real * real_part + filter_imag * imag_part,
            filter_real * imag_part - filter_imag * real_part,
        ],
        axis=1,
    )
    returned = dot_split("mls,lpmc->spmc", legendre_parts, split_bf16(filtered))
    returned = (returned * quad_weights[:, None, None, None]).astype(jnp.bfloat16)
    returned, ext_now = lax.optimization_barrier((returned, ext))
    portion = lax.all_to_all(returned, "lat", split_axis=0, concat_axis=2, tiled=True)
    disco_parts.append(disco_work(ext_now, 1))
    portion, disco_parts = lax.optimization_barrier((portion, disco_parts))
    spectral_rows = None
    for p, parts in enumerate(trig_parts):
        term = dot_split("rkc,nk->rnc", (portion[:, p],), parts)
        spectral_rows = term if spectral_rows is None else spectral_rows + term
    spectral_rows = spectral_rows.astype(jnp.bfloat16)
    spectral_rows, ext_now = lax.optimization_barrier((spectral_rows, ext))
    spectral = lax.all_to_all(spectral_rows, "lon", split_axis=1, concat_axis=2, tiled=True)
    disco_parts.append(disco_work(ext_now, 2))
    spectral, disco_parts = lax.optimization_barrier((spectral, disco_parts))
    return spectral, disco_parts


def filter_modes(coefficients, spectral_filter):
    filter_real = spectral_filter[0][:, None, :]
    filter_imag = spectral_filter[1][:, None, :]
    real_part = coefficients[:, 0]
    imag_part = coefficients[:, 1]
    return jnp.stack(
        [
            filter_real * real_part + filter_imag * imag_part,
            filter_real * imag_part - filter_imag * real_part,
        ],
        axis=1,
    )


def spectral_by_modes(masked, legendre, quad_weights, spectral_filter, trig_parts, ext, disco_work):
    both = ("lat", "lon")
    lon_total = lax.axis_size("lon")
    mode_share = legendre.shape[0] // lon_total
    disco_parts = []
    portion = lax.all_to_all(masked, "lon", split_axis=0, concat_axis=1, tiled=True)
    spectra = jnp.stack(
        [dot_split("rnc,nk->rkc", (portion,), parts).astype(jnp.bfloat16) for parts in trig_parts],
        axis=1,
    )
    spectra, ext_now = lax.optimization_barrier((spectra, ext))
    columns = lax.all_to_all(spectra, both, split_axis=2, concat_axis=0, tiled=True)
    disco_parts.append(disco_work(ext_now, 0))
    columns, disco_parts[0] = lax.optimization_barrier((columns, disco_parts[0]))
    own_legendre = lax.dynamic_slice_in_dim(
        legendre, lax.axis_index("lon") * mode_share, mode_share, 0
    )
    legendre_parts = split_bf16(own_legendre)
    coefficients = dot_split("mls,spmc->lpmc", legendre_parts, (columns,))
    filtered = filter_modes(coefficients, spectral_filter)
    returned = dot_split("mls,lpmc->spmc", legendre_parts, split_bf16(filtered))
    returned = (returned * quad_weights[:, None, None, None]).astype(jnp.bfloat16)
    returned, ext_now = lax.optimization_barrier((returned, ext))
    portion = lax.all_to_all(returned, both, split_axis=0, concat_axis=2, tiled=True)
    disco_parts.append(disco_work(ext_now, 1))
    portion, disco_parts = lax.optimization_barrier((portion, disco_parts))
    spectral_rows = None
    for p, parts in enumerate(trig_parts):
        term = dot_split("rkc,nk->rnc", (portion[:, p],), parts)
        spectral_rows = term if spectral_rows is None else spectral_rows + term
    spectral_rows = spectral_rows.astype(jnp.bfloat16)
    spectral_rows, ext_now = lax.optimization_barrier((spectral_rows, ext))
    spectral = lax.all_to_all(spectral_rows, "lon", split_axis=1, concat_axis=0, tiled=True)
    disco_parts.append(disco_work(ext_now, 2))
    spectral, disco_parts = lax.optimization_barrier((spectral, disco_parts))
    return spectral, disco_parts


def on_device(
    grad_output, band_rows, legendre, quad_weights, spectral_filter, disco_kernel, disco_weight
):
    row_count, lon_count, channels = grad_output.shape
    band_index = lax.axis_index("lat")
    band_total = lax.axis_size("lat")
    lon_total = lax.axis_size("lon")
    point_count = lon_count * lon_total
    mode_count = legendre.shape[0] * band_total
    slot_ids = jnp.arange(row_count, dtype=jnp.int32)
    live_rows = band_rows[band_index]
    live_slot = slot_ids < live_rows
    masked = jnp.where(live_slot[:, None, None], grad_output, jnp.zeros_like(grad_output))
    trig_parts = make_trig(mode_count, point_count)
    ext = halo_extend(masked, live_rows)
    src_rows, coef = disco_tables(band_rows, disco_kernel, band_index, band_total, row_count)
    weight_flat = disco_weight.reshape(channels, -1)
    pieces = min(3, row_count)

    def disco_work(ext_now, piece):
        return disco_piece(src_rows, coef, ext_now, weight_flat, piece, pieces, lon_count)

    by_modes = legendre.shape[0] % lon_total == 0 and row_count % lon_total == 0
    path = spectral_by_modes if by_modes else spectral_by_channels
    spectral, disco_parts = path(
        masked, legendre, quad_weights, spectral_filter, trig_parts, ext, disco_work
    )
    disco_full = jnp.concatenate(disco_parts, axis=0)
    disco_term = disco_full[:, :lon_count, :]
    summed = masked.astype(jnp.float32) + disco_term + spectral.astype(jnp.float32)
    return jnp.where(live_slot[:, None, None], summed, 0.0).astype(jnp.bfloat16)


def solution(mesh):
    placed = (P("lat", "lon", None), P(), P("lat", None, None), P(), P(), P(), P())
    return jax.shard_map(
        on_device, mesh=mesh, in_specs=placed, out_specs=P("lat", "lon", None), check_vma=False
    )
```

```python
import functools

import ml_dtypes
import numpy as np
import jax
import jax.numpy as jnp
from jax import lax
from jax.experimental import pallas as pl
from jax.experimental.pallas import tpu as pltpu
from jax.sharding import PartitionSpec as P


def make_trig(mode_count, point_count):
    step = 16 if point_count % 16 == 0 else 1
    coarse = np.arange(point_count // step)[:, None] * step
    fine = np.arange(step)[:, None]
    wavenumber = np.arange(mode_count)[None, :]
    coarse_angle = (wavenumber * coarse % point_count) * (2.0 * np.pi / point_count)
    fine_angle = (wavenumber * fine % point_count) * (2.0 * np.pi / point_count)
    scale = point_count ** (-0.5)
    coarse_cos = jnp.asarray((np.cos(coarse_angle) * scale).astype(np.float32))[:, None, :]
    coarse_sin = jnp.asarray((np.sin(coarse_angle) * scale).astype(np.float32))[:, None, :]
    fine_cos = jnp.asarray(np.cos(fine_angle).astype(np.float32))[None, :, :]
    fine_sin = jnp.asarray(np.sin(fine_angle).astype(np.float32))[None, :, :]
    cosine = coarse_cos * fine_cos - coarse_sin * fine_sin
    minus_sine = -(coarse_sin * fine_cos + coarse_cos * fine_sin)
    return tuple(
        split_bf16(part.reshape(point_count, mode_count)) for part in (cosine, minus_sine)
    )


def split_bf16(values):
    rounded = lax.reduce_precision(values, exponent_bits=8, mantissa_bits=7)
    return rounded.astype(jnp.bfloat16), (values - rounded).astype(jnp.bfloat16)


def dot_split(spec, left_parts, right_parts):
    total = None
    for lp in left_parts:
        for rp in right_parts:
            if lp is not left_parts[0] and rp is not right_parts[0]:
                continue
            term = jnp.einsum(spec, lp, rp, preferred_element_type=jnp.float32)
            total = term if total is None else total + term
    return total


CHUNK = 64


def round_up(value, step):
    return -(-value // step) * step


def disco_body(first, last, src_ref, coef_ref, ext_ref, w_ref, out_ref, mix_ref):
    kinds = w_ref.shape[1] // w_ref.shape[0]
    channels = w_ref.shape[0]
    for r in range(last - first + 2):
        mix_ref[r] = jnp.dot(ext_ref[first + r], w_ref[...], preferred_element_type=jnp.float32)

    def slot_step(s, carry):
        for c0 in range(0, out_ref.shape[1], CHUNK):
            acc = jnp.zeros((CHUNK, channels), jnp.float32)
            for a_i in range(3):
                row = src_ref[(first + s) * 3 + a_i] - first
                for b_i in range(3):
                    for k in range(kinds):
                        coef = coef_ref[(((first + s) * 3 + a_i) * 3 + b_i) * kinds + k]
                        acc = acc + coef * mix_ref[
                            row, pl.ds(c0 + 2 - b_i, CHUNK), pl.ds(k * channels, channels)
                        ]
            out_ref[s, pl.ds(c0, CHUNK), :] = acc
        return carry

    lax.fori_loop(0, last - first, slot_step, 0)


def disco_piece(src_rows, coef, ext, weight_flat, piece, pieces, lon_count):
    slot_total = ext.shape[0] - 2
    first = piece * slot_total // pieces
    last = (piece + 1) * slot_total // pieces
    lon_pad, channels = ext.shape[1:]
    out_rows = round_up(lon_count, CHUNK)
    smem = pltpu.MemorySpace.SMEM if hasattr(pltpu, "MemorySpace") else pltpu.SMEM
    return pl.pallas_call(
        functools.partial(disco_body, first, last),
        out_shape=jax.ShapeDtypeStruct((last - first, out_rows, channels), jnp.float32),
        in_specs=[
            pl.BlockSpec(memory_space=smem),
            pl.BlockSpec(memory_space=smem),
            pl.BlockSpec(memory_space=pltpu.VMEM),
            pl.BlockSpec(memory_space=pltpu.VMEM),
        ],
        out_specs=pl.BlockSpec(memory_space=pltpu.VMEM),
        scratch_shapes=[pltpu.VMEM((last - first + 2, lon_pad, weight_flat.shape[1]), jnp.float32)],
    )(src_rows, coef, ext, weight_flat)


def disco_tables(band_rows, disco_kernel, band_index, band_total, row_count):
    slot_ids = jnp.arange(row_count, dtype=jnp.int32)
    live_rows = band_rows[band_index]
    has_next = slot_ids + 1 < live_rows
    prev_band = jnp.maximum(band_index - 1, 0)
    next_band = jnp.minimum(band_index + 1, band_total - 1)
    base = band_index * row_count
    up_src = jnp.where(slot_ids == 0, 0, slot_ids)
    down_src = jnp.where(has_next, slot_ids + 2, row_count + 1)
    src = jnp.stack([up_src, slot_ids + 1, down_src], axis=1)
    up_row = jnp.where(
        slot_ids == 0, prev_band * row_count + band_rows[prev_band] - 1, base + slot_ids - 1
    )
    down_row = jnp.where(has_next, base + slot_ids + 1, next_band * row_count)
    kernel_row = jnp.stack([up_row, base + slot_ids, down_row], axis=1)
    kernel_row = jnp.clip(kernel_row, 0, disco_kernel.shape[0] - 1)
    up_ok = (slot_ids > 0) | (band_index > 0)
    down_ok = has_next | (band_index < band_total - 1)
    valid = jnp.stack([up_ok, jnp.ones_like(up_ok), down_ok], axis=1)
    gathered = disco_kernel[kernel_row]
    gathered = gathered.reshape(row_count, 3, 3, 3, disco_kernel.shape[2])
    coef = jnp.stack([gathered[:, 0, 2], gathered[:, 1, 1], gathered[:, 2, 0]], axis=1)
    coef = jnp.where(valid[:, :, None, None], coef, 0.0)
    return src.reshape(-1).astype(jnp.int32), coef.reshape(-1).astype(jnp.float32)


def halo_extend(masked, live_rows):
    row_count, lon_count, channels = masked.shape
    lat_total = lax.axis_size("lat")
    lon_total = lax.axis_size("lon")
    lat_up = [(i, (i + 1) % lat_total) for i in range(lat_total)]
    lat_down = [(j, i) for i, j in lat_up]
    lon_up = [(i, (i + 1) % lon_total) for i in range(lon_total)]
    lon_down = [(j, i) for i, j in lon_up]
    last_row = lax.dynamic_slice_in_dim(masked, live_rows - 1, 1, 0)
    from_above = lax.ppermute(last_row, "lat", lat_up)
    from_below = lax.ppermute(masked[0:1], "lat", lat_down)
    rows = jnp.concatenate([from_above, masked, from_below], axis=0)
    from_left = lax.ppermute(rows[:, lon_count - 1 : lon_count], "lon", lon_up)
    from_right = lax.ppermute(rows[:, 0:1], "lon", lon_down)
    lon_pad = round_up(round_up(lon_count, CHUNK) + 2, 16)
    pad = jnp.zeros((row_count + 2, lon_pad - lon_count - 2, channels), masked.dtype)
    return jnp.concatenate([from_left, rows, from_right, pad], axis=1)


def spectral_by_channels(
    masked, legendre, quad_weights, spectral_filter, trig_parts, ext, disco_work
):
    channels = masked.shape[2]
    lon_index = lax.axis_index("lon")
    chan_share = channels // lax.axis_size("lon")
    disco_parts = []
    portion = lax.all_to_all(masked, "lon", split_axis=2, concat_axis=1, tiled=True)
    spectra = jnp.stack(
        [dot_split("rnc,nk->rkc", (portion,), parts).astype(jnp.bfloat16) for parts in trig_parts],
        axis=1,
    )
    spectra, ext_now = lax.optimization_barrier((spectra, ext))
    columns = lax.all_to_all(spectra, "lat", split_axis=2, concat_axis=0, tiled=True)
    disco_parts.append(disco_work(ext_now, 0))
    columns, disco_parts[0] = lax.optimization_barrier((columns, disco_parts[0]))
    legendre_parts = split_bf16(legendre)
    coefficients = dot_split("mls,spmc->lpmc", legendre_parts, (columns,))
    filter_slice = lax.dynamic_slice_in_dim(spectral_filter, lon_index * chan_share, chan_share, 2)
    filter_real = filter_slice[0][:, None, :]
    filter_imag = filter_slice[1][:, None, :]
    real_part = coefficients[:, 0]
    imag_part = coefficients[:, 1]
    filtered = jnp.stack(
        [
            filter_real * real_part + filter_imag * imag_part,
            filter_real * imag_part - filter_imag * real_part,
        ],
        axis=1,
    )
    returned = dot_split("mls,lpmc->spmc", legendre_parts, split_bf16(filtered))
    returned = (returned * quad_weights[:, None, None, None]).astype(jnp.bfloat16)
    returned, ext_now = lax.optimization_barrier((returned, ext))
    portion = lax.all_to_all(returned, "lat", split_axis=0, concat_axis=2, tiled=True)
    disco_parts.append(disco_work(ext_now, 1))
    portion, disco_parts = lax.optimization_barrier((portion, disco_parts))
    spectral_rows = None
    for p, parts in enumerate(trig_parts):
        term = dot_split("rkc,nk->rnc", (portion[:, p],), parts)
        spectral_rows = term if spectral_rows is None else spectral_rows + term
    spectral_rows = spectral_rows.astype(jnp.bfloat16)
    spectral_rows, ext_now = lax.optimization_barrier((spectral_rows, ext))
    spectral = lax.all_to_all(spectral_rows, "lon", split_axis=1, concat_axis=2, tiled=True)
    disco_parts.append(disco_work(ext_now, 2))
    spectral, disco_parts = lax.optimization_barrier((spectral, disco_parts))
    return spectral, disco_parts


def filter_modes(coefficients, spectral_filter):
    filter_real = spectral_filter[0][:, None, :]
    filter_imag = spectral_filter[1][:, None, :]
    real_part = coefficients[:, 0]
    imag_part = coefficients[:, 1]
    return jnp.stack(
        [
            filter_real * real_part + filter_imag * imag_part,
            filter_real * imag_part - filter_imag * real_part,
        ],
        axis=1,
    )


def spectral_by_modes(masked, legendre, quad_weights, spectral_filter, trig_parts, ext, disco_work):
    both = ("lat", "lon")
    lon_total = lax.axis_size("lon")
    mode_share = legendre.shape[0] // lon_total
    disco_parts = []
    portion = lax.all_to_all(masked, "lon", split_axis=0, concat_axis=1, tiled=True)
    spectra = jnp.stack(
        [dot_split("rnc,nk->rkc", (portion,), parts).astype(jnp.bfloat16) for parts in trig_parts],
        axis=1,
    )
    spectra, ext_now = lax.optimization_barrier((spectra, ext))
    columns = lax.all_to_all(spectra, both, split_axis=2, concat_axis=0, tiled=True)
    disco_parts.append(disco_work(ext_now, 0))
    columns, disco_parts[0] = lax.optimization_barrier((columns, disco_parts[0]))
    own_legendre = lax.dynamic_slice_in_dim(
        legendre, lax.axis_index("lon") * mode_share, mode_share, 0
    )
    legendre_parts = split_bf16(own_legendre)
    coefficients = dot_split("mls,spmc->lpmc", legendre_parts, (columns,))
    filtered = filter_modes(coefficients, spectral_filter)
    returned = dot_split("mls,lpmc->spmc", legendre_parts, split_bf16(filtered))
    returned = (returned * quad_weights[:, None, None, None]).astype(jnp.bfloat16)
    returned, ext_now = lax.optimization_barrier((returned, ext))
    portion = lax.all_to_all(returned, both, split_axis=0, concat_axis=2, tiled=True)
    disco_parts.append(disco_work(ext_now, 1))
    portion, disco_parts = lax.optimization_barrier((portion, disco_parts))
    portion, ext_now = lax.optimization_barrier((portion, ext))
    gathered = lax.all_gather(portion, "lon", axis=0, tiled=True)
    disco_parts.append(disco_work(ext_now, 2))
    gathered, disco_parts = lax.optimization_barrier((gathered, disco_parts))
    lon_count = masked.shape[1]
    lon_index = lax.axis_index("lon")
    spectral = None
    for p, parts in enumerate(trig_parts):
        own = tuple(
            lax.dynamic_slice_in_dim(part, lon_index * lon_count, lon_count, 0) for part in parts
        )
        term = dot_split("rkc,nk->rnc", (gathered[:, p],), own)
        spectral = term if spectral is None else spectral + term
    spectral = spectral.astype(jnp.bfloat16)
    return spectral, disco_parts


def on_device(
    grad_output, band_rows, legendre, quad_weights, spectral_filter, disco_kernel, disco_weight
):
    row_count, lon_count, channels = grad_output.shape
    band_index = lax.axis_index("lat")
    band_total = lax.axis_size("lat")
    lon_total = lax.axis_size("lon")
    point_count = lon_count * lon_total
    mode_count = legendre.shape[0] * band_total
    slot_ids = jnp.arange(row_count, dtype=jnp.int32)
    live_rows = band_rows[band_index]
    live_slot = slot_ids < live_rows
    masked = jnp.where(live_slot[:, None, None], grad_output, jnp.zeros_like(grad_output))
    trig_parts = make_trig(mode_count, point_count)
    ext = halo_extend(masked, live_rows)
    src_rows, coef = disco_tables(band_rows, disco_kernel, band_index, band_total, row_count)
    weight_flat = disco_weight.reshape(channels, -1)
    pieces = min(3, row_count)

    def disco_work(ext_now, piece):
        return disco_piece(src_rows, coef, ext_now, weight_flat, piece, pieces, lon_count)

    by_modes = legendre.shape[0] % lon_total == 0 and row_count % lon_total == 0
    path = spectral_by_modes if by_modes else spectral_by_channels
    spectral, disco_parts = path(
        masked, legendre, quad_weights, spectral_filter, trig_parts, ext, disco_work
    )
    disco_full = jnp.concatenate(disco_parts, axis=0)
    disco_term = disco_full[:, :lon_count, :]
    summed = masked.astype(jnp.float32) + disco_term + spectral.astype(jnp.float32)
    return jnp.where(live_slot[:, None, None], summed, 0.0).astype(jnp.bfloat16)


def solution(mesh):
    placed = (P("lat", "lon", None), P(), P("lat", None, None), P(), P(), P(), P())
    return jax.shard_map(
        on_device, mesh=mesh, in_specs=placed, out_specs=P("lat", "lon", None), check_vma=False
    )
```

```python
import functools

import ml_dtypes
import numpy as np
import jax
import jax.numpy as jnp
from jax import lax
from jax.experimental import pallas as pl
from jax.experimental.pallas import tpu as pltpu
from jax.sharding import PartitionSpec as P


def make_trig(mode_count, point_count):
    step = 16 if point_count % 16 == 0 else 1
    coarse = np.arange(point_count // step)[:, None] * step
    fine = np.arange(step)[:, None]
    wavenumber = np.arange(mode_count)[None, :]
    coarse_angle = (wavenumber * coarse % point_count) * (2.0 * np.pi / point_count)
    fine_angle = (wavenumber * fine % point_count) * (2.0 * np.pi / point_count)
    scale = point_count ** (-0.5)
    coarse_cos = jnp.asarray((np.cos(coarse_angle) * scale).astype(np.float32))[:, None, :]
    coarse_sin = jnp.asarray((np.sin(coarse_angle) * scale).astype(np.float32))[:, None, :]
    fine_cos = jnp.asarray(np.cos(fine_angle).astype(np.float32))[None, :, :]
    fine_sin = jnp.asarray(np.sin(fine_angle).astype(np.float32))[None, :, :]
    cosine = coarse_cos * fine_cos - coarse_sin * fine_sin
    minus_sine = -(coarse_sin * fine_cos + coarse_cos * fine_sin)
    return tuple(
        split_bf16(part.reshape(point_count, mode_count)) for part in (cosine, minus_sine)
    )


def split_bf16(values):
    rounded = lax.reduce_precision(values, exponent_bits=8, mantissa_bits=7)
    return rounded.astype(jnp.bfloat16), (values - rounded).astype(jnp.bfloat16)


def dot_split(spec, left_parts, right_parts):
    total = None
    for lp in left_parts:
        for rp in right_parts:
            if lp is not left_parts[0] and rp is not right_parts[0]:
                continue
            term = jnp.einsum(spec, lp, rp, preferred_element_type=jnp.float32)
            total = term if total is None else total + term
    return total


CHUNK = 64


def round_up(value, step):
    return -(-value // step) * step


def disco_body(first, last, src_ref, coef_ref, ext_ref, w_ref, out_ref, mix_ref):
    kinds = w_ref.shape[1] // w_ref.shape[0]
    channels = w_ref.shape[0]
    for r in range(last - first + 2):
        mix_ref[r] = jnp.dot(ext_ref[first + r], w_ref[...], preferred_element_type=jnp.float32)

    def slot_step(s, carry):
        for c0 in range(0, out_ref.shape[1], CHUNK):
            acc = jnp.zeros((CHUNK, channels), jnp.float32)
            for a_i in range(3):
                row = src_ref[(first + s) * 3 + a_i] - first
                for b_i in range(3):
                    for k in range(kinds):
                        coef = coef_ref[(((first + s) * 3 + a_i) * 3 + b_i) * kinds + k]
                        acc = acc + coef * mix_ref[
                            row, pl.ds(c0 + 2 - b_i, CHUNK), pl.ds(k * channels, channels)
                        ]
            out_ref[s, pl.ds(c0, CHUNK), :] = acc
        return carry

    lax.fori_loop(0, last - first, slot_step, 0)


def disco_piece(src_rows, coef, ext, weight_flat, piece, pieces, lon_count):
    slot_total = ext.shape[0] - 2
    first = piece * slot_total // pieces
    last = (piece + 1) * slot_total // pieces
    lon_pad, channels = ext.shape[1:]
    out_rows = round_up(lon_count, CHUNK)
    smem = pltpu.MemorySpace.SMEM if hasattr(pltpu, "MemorySpace") else pltpu.SMEM
    return pl.pallas_call(
        functools.partial(disco_body, first, last),
        out_shape=jax.ShapeDtypeStruct((last - first, out_rows, channels), jnp.float32),
        in_specs=[
            pl.BlockSpec(memory_space=smem),
            pl.BlockSpec(memory_space=smem),
            pl.BlockSpec(memory_space=pltpu.VMEM),
            pl.BlockSpec(memory_space=pltpu.VMEM),
        ],
        out_specs=pl.BlockSpec(memory_space=pltpu.VMEM),
        scratch_shapes=[pltpu.VMEM((last - first + 2, lon_pad, weight_flat.shape[1]), jnp.float32)],
    )(src_rows, coef, ext, weight_flat)


def disco_tables(band_rows, disco_kernel, band_index, band_total, row_count):
    slot_ids = jnp.arange(row_count, dtype=jnp.int32)
    live_rows = band_rows[band_index]
    has_next = slot_ids + 1 < live_rows
    prev_band = jnp.maximum(band_index - 1, 0)
    next_band = jnp.minimum(band_index + 1, band_total - 1)
    base = band_index * row_count
    up_src = jnp.where(slot_ids == 0, 0, slot_ids)
    down_src = jnp.where(has_next, slot_ids + 2, row_count + 1)
    src = jnp.stack([up_src, slot_ids + 1, down_src], axis=1)
    up_row = jnp.where(
        slot_ids == 0, prev_band * row_count + band_rows[prev_band] - 1, base + slot_ids - 1
    )
    down_row = jnp.where(has_next, base + slot_ids + 1, next_band * row_count)
    kernel_row = jnp.stack([up_row, base + slot_ids, down_row], axis=1)
    kernel_row = jnp.clip(kernel_row, 0, disco_kernel.shape[0] - 1)
    up_ok = (slot_ids > 0) | (band_index > 0)
    down_ok = has_next | (band_index < band_total - 1)
    valid = jnp.stack([up_ok, jnp.ones_like(up_ok), down_ok], axis=1)
    gathered = disco_kernel[kernel_row]
    gathered = gathered.reshape(row_count, 3, 3, 3, disco_kernel.shape[2])
    coef = jnp.stack([gathered[:, 0, 2], gathered[:, 1, 1], gathered[:, 2, 0]], axis=1)
    coef = jnp.where(valid[:, :, None, None], coef, 0.0)
    return src.reshape(-1).astype(jnp.int32), coef.reshape(-1).astype(jnp.float32)


def lat_extend(block, live_rows):
    lat_total = lax.axis_size("lat")
    lat_up = [(i, (i + 1) % lat_total) for i in range(lat_total)]
    lat_down = [(j, i) for i, j in lat_up]
    last_row = lax.dynamic_slice_in_dim(block, live_rows - 1, 1, 0)
    from_above = lax.ppermute(last_row, "lat", lat_up)
    from_below = lax.ppermute(block[0:1], "lat", lat_down)
    return jnp.concatenate([from_above, block, from_below], axis=0)


def pad_lon(rows, lon_count):
    lon_pad = round_up(round_up(lon_count, CHUNK) + 2, 16)
    pad = jnp.zeros((rows.shape[0], lon_pad - rows.shape[1], rows.shape[2]), rows.dtype)
    return jnp.concatenate([rows, pad], axis=1)


def halo_extend(masked, live_rows):
    row_count, lon_count, channels = masked.shape
    lat_total = lax.axis_size("lat")
    lon_total = lax.axis_size("lon")
    lat_up = [(i, (i + 1) % lat_total) for i in range(lat_total)]
    lat_down = [(j, i) for i, j in lat_up]
    lon_up = [(i, (i + 1) % lon_total) for i in range(lon_total)]
    lon_down = [(j, i) for i, j in lon_up]
    last_row = lax.dynamic_slice_in_dim(masked, live_rows - 1, 1, 0)
    from_above = lax.ppermute(last_row, "lat", lat_up)
    from_below = lax.ppermute(masked[0:1], "lat", lat_down)
    rows = jnp.concatenate([from_above, masked, from_below], axis=0)
    from_left = lax.ppermute(rows[:, lon_count - 1 : lon_count], "lon", lon_up)
    from_right = lax.ppermute(rows[:, 0:1], "lon", lon_down)
    lon_pad = round_up(round_up(lon_count, CHUNK) + 2, 16)
    pad = jnp.zeros((row_count + 2, lon_pad - lon_count - 2, channels), masked.dtype)
    return jnp.concatenate([from_left, rows, from_right, pad], axis=1)


def spectral_by_channels(
    masked, legendre, quad_weights, spectral_filter, trig_parts, live_rows, disco_work
):
    ext = halo_extend(masked, live_rows)
    channels = masked.shape[2]
    lon_index = lax.axis_index("lon")
    chan_share = channels // lax.axis_size("lon")
    disco_parts = []
    portion = lax.all_to_all(masked, "lon", split_axis=2, concat_axis=1, tiled=True)
    spectra = jnp.stack(
        [dot_split("rnc,nk->rkc", (portion,), parts).astype(jnp.bfloat16) for parts in trig_parts],
        axis=1,
    )
    spectra, ext_now = lax.optimization_barrier((spectra, ext))
    columns = lax.all_to_all(spectra, "lat", split_axis=2, concat_axis=0, tiled=True)
    disco_parts.append(disco_work(ext_now, 0))
    columns, disco_parts[0] = lax.optimization_barrier((columns, disco_parts[0]))
    legendre_parts = split_bf16(legendre)
    coefficients = dot_split("mls,spmc->lpmc", legendre_parts, (columns,))
    filter_slice = lax.dynamic_slice_in_dim(spectral_filter, lon_index * chan_share, chan_share, 2)
    filter_real = filter_slice[0][:, None, :]
    filter_imag = filter_slice[1][:, None, :]
    real_part = coefficients[:, 0]
    imag_part = coefficients[:, 1]
    filtered = jnp.stack(
        [
            filter_real * real_part + filter_imag * imag_part,
            filter_real * imag_part - filter_imag * real_part,
        ],
        axis=1,
    )
    returned = dot_split("mls,lpmc->spmc", legendre_parts, split_bf16(filtered))
    returned = (returned * quad_weights[:, None, None, None]).astype(jnp.bfloat16)
    returned, ext_now = lax.optimization_barrier((returned, ext))
    portion = lax.all_to_all(returned, "lat", split_axis=0, concat_axis=2, tiled=True)
    disco_parts.append(disco_work(ext_now, 1))
    portion, disco_parts = lax.optimization_barrier((portion, disco_parts))
    spectral_rows = None
    for p, parts in enumerate(trig_parts):
        term = dot_split("rkc,nk->rnc", (portion[:, p],), parts)
        spectral_rows = term if spectral_rows is None else spectral_rows + term
    spectral_rows = spectral_rows.astype(jnp.bfloat16)
    spectral_rows, ext_now = lax.optimization_barrier((spectral_rows, ext))
    spectral = lax.all_to_all(spectral_rows, "lon", split_axis=1, concat_axis=2, tiled=True)
    disco_parts.append(disco_work(ext_now, 2))
    spectral, disco_parts = lax.optimization_barrier((spectral, disco_parts))
    return spectral, disco_parts


def filter_modes(coefficients, spectral_filter):
    filter_real = spectral_filter[0][:, None, :]
    filter_imag = spectral_filter[1][:, None, :]
    real_part = coefficients[:, 0]
    imag_part = coefficients[:, 1]
    return jnp.stack(
        [
            filter_real * real_part + filter_imag * imag_part,
            filter_real * imag_part - filter_imag * real_part,
        ],
        axis=1,
    )


def spectral_by_modes(
    masked, legendre, quad_weights, spectral_filter, trig_parts, live_rows, disco_work
):
    both = ("lat", "lon")
    lon_total = lax.axis_size("lon")
    mode_share = legendre.shape[0] // lon_total
    row_count, lon_count, channels = masked.shape
    share = row_count // lon_total
    body = masked.reshape(lon_total, share * lon_count, channels)
    edges = jnp.concatenate([masked[:, 0], masked[:, lon_count - 1]], axis=0)
    edges = jnp.broadcast_to(edges[None], (lon_total, 2 * row_count, channels))
    received = lax.all_to_all(
        jnp.concatenate([body, edges], axis=1), "lon", split_axis=0, concat_axis=0, tiled=True
    )
    portion = received[:, : share * lon_count].reshape(lon_total, share, lon_count, channels)
    portion = portion.transpose(1, 0, 2, 3).reshape(share, lon_total * lon_count, channels)
    edge_block = received[:, share * lon_count :]
    lon_index = lax.axis_index("lon")
    left = lax.dynamic_index_in_dim(edge_block, (lon_index - 1) % lon_total, 0, keepdims=False)
    right = lax.dynamic_index_in_dim(edge_block, (lon_index + 1) % lon_total, 0, keepdims=False)
    own = jnp.concatenate([left[row_count:, None], masked, right[:row_count, None]], axis=1)
    ext = pad_lon(lat_extend(own, live_rows), lon_count)
    disco_parts = []
    spectra = jnp.stack(
        [dot_split("rnc,nk->rkc", (portion,), parts).astype(jnp.bfloat16) for parts in trig_parts],
        axis=1,
    )
    spectra, ext_now = lax.optimization_barrier((spectra, ext))
    columns = lax.all_to_all(spectra, both, split_axis=2, concat_axis=0, tiled=True)
    disco_parts.append(disco_work(ext_now, 0))
    columns, disco_parts[0] = lax.optimization_barrier((columns, disco_parts[0]))
    own_legendre = lax.dynamic_slice_in_dim(
        legendre, lax.axis_index("lon") * mode_share, mode_share, 0
    )
    legendre_parts = split_bf16(own_legendre)
    coefficients = dot_split("mls,spmc->lpmc", legendre_parts, (columns,))
    filtered = filter_modes(coefficients, spectral_filter)
    returned = dot_split("mls,lpmc->spmc", legendre_parts, split_bf16(filtered))
    returned = (returned * quad_weights[:, None, None, None]).astype(jnp.bfloat16)
    returned, ext_now = lax.optimization_barrier((returned, ext))
    portion = lax.all_to_all(returned, both, split_axis=0, concat_axis=2, tiled=True)
    disco_parts.append(disco_work(ext_now, 1))
    portion, disco_parts = lax.optimization_barrier((portion, disco_parts))
    spectral_rows = None
    for p, parts in enumerate(trig_parts):
        term = dot_split("rkc,nk->rnc", (portion[:, p],), parts)
        spectral_rows = term if spectral_rows is None else spectral_rows + term
    spectral_rows = spectral_rows.astype(jnp.bfloat16)
    spectral_rows, ext_now = lax.optimization_barrier((spectral_rows, ext))
    spectral = lax.all_to_all(spectral_rows, "lon", split_axis=1, concat_axis=0, tiled=True)
    disco_parts.append(disco_work(ext_now, 2))
    spectral, disco_parts = lax.optimization_barrier((spectral, disco_parts))
    return spectral, disco_parts


def on_device(
    grad_output, band_rows, legendre, quad_weights, spectral_filter, disco_kernel, disco_weight
):
    row_count, lon_count, channels = grad_output.shape
    band_index = lax.axis_index("lat")
    band_total = lax.axis_size("lat")
    lon_total = lax.axis_size("lon")
    point_count = lon_count * lon_total
    mode_count = legendre.shape[0] * band_total
    slot_ids = jnp.arange(row_count, dtype=jnp.int32)
    live_rows = band_rows[band_index]
    live_slot = slot_ids < live_rows
    masked = jnp.where(live_slot[:, None, None], grad_output, jnp.zeros_like(grad_output))
    trig_parts = make_trig(mode_count, point_count)
    src_rows, coef = disco_tables(band_rows, disco_kernel, band_index, band_total, row_count)
    weight_flat = disco_weight.reshape(channels, -1)
    pieces = min(3, row_count)

    def disco_work(ext_now, piece):
        return disco_piece(src_rows, coef, ext_now, weight_flat, piece, pieces, lon_count)

    by_modes = legendre.shape[0] % lon_total == 0 and row_count % lon_total == 0
    path = spectral_by_modes if by_modes else spectral_by_channels
    spectral, disco_parts = path(
        masked, legendre, quad_weights, spectral_filter, trig_parts, live_rows, disco_work
    )
    disco_full = jnp.concatenate(disco_parts, axis=0)
    disco_term = disco_full[:, :lon_count, :]
    summed = masked.astype(jnp.float32) + disco_term + spectral.astype(jnp.float32)
    return jnp.where(live_slot[:, None, None], summed, 0.0).astype(jnp.bfloat16)


def solution(mesh):
    placed = (P("lat", "lon", None), P(), P("lat", None, None), P(), P(), P(), P())
    return jax.shard_map(
        on_device, mesh=mesh, in_specs=placed, out_specs=P("lat", "lon", None), check_vma=False
    )
```

```python
import functools

import ml_dtypes
import numpy as np
import jax
import jax.numpy as jnp
from jax import lax
from jax.experimental import pallas as pl
from jax.experimental.pallas import tpu as pltpu
from jax.sharding import PartitionSpec as P


def make_trig(mode_count, point_count):
    step = 16 if point_count % 16 == 0 else 1
    coarse = np.arange(point_count // step)[:, None] * step
    fine = np.arange(step)[:, None]
    wavenumber = np.arange(mode_count)[None, :]
    coarse_angle = (wavenumber * coarse % point_count) * (2.0 * np.pi / point_count)
    fine_angle = (wavenumber * fine % point_count) * (2.0 * np.pi / point_count)
    scale = point_count ** (-0.5)
    coarse_cos = jnp.asarray((np.cos(coarse_angle) * scale).astype(np.float32))[:, None, :]
    coarse_sin = jnp.asarray((np.sin(coarse_angle) * scale).astype(np.float32))[:, None, :]
    fine_cos = jnp.asarray(np.cos(fine_angle).astype(np.float32))[None, :, :]
    fine_sin = jnp.asarray(np.sin(fine_angle).astype(np.float32))[None, :, :]
    cosine = coarse_cos * fine_cos - coarse_sin * fine_sin
    minus_sine = -(coarse_sin * fine_cos + coarse_cos * fine_sin)
    return tuple(
        split_bf16(part.reshape(point_count, mode_count)) for part in (cosine, minus_sine)
    )


def split_bf16(values):
    rounded = lax.reduce_precision(values, exponent_bits=8, mantissa_bits=7)
    return rounded.astype(jnp.bfloat16), (values - rounded).astype(jnp.bfloat16)


def dot_split(spec, left_parts, right_parts):
    total = None
    for lp in left_parts:
        for rp in right_parts:
            if lp is not left_parts[0] and rp is not right_parts[0]:
                continue
            term = jnp.einsum(spec, lp, rp, preferred_element_type=jnp.float32)
            total = term if total is None else total + term
    return total


CHUNK = 64


def round_up(value, step):
    return -(-value // step) * step


def disco_body(first, last, src_ref, coef_ref, ext_ref, w_ref, out_ref, mix_ref):
    kinds = w_ref.shape[1] // w_ref.shape[0]
    channels = w_ref.shape[0]
    for r in range(last - first + 2):
        mix_ref[r] = jnp.dot(ext_ref[first + r], w_ref[...], preferred_element_type=jnp.float32)

    def slot_step(s, carry):
        for c0 in range(0, out_ref.shape[1], CHUNK):
            acc = jnp.zeros((CHUNK, channels), jnp.float32)
            for a_i in range(3):
                row = src_ref[(first + s) * 3 + a_i] - first
                for b_i in range(3):
                    for k in range(kinds):
                        coef = coef_ref[(((first + s) * 3 + a_i) * 3 + b_i) * kinds + k]
                        acc = acc + coef * mix_ref[
                            row, pl.ds(c0 + 2 - b_i, CHUNK), pl.ds(k * channels, channels)
                        ]
            out_ref[s, pl.ds(c0, CHUNK), :] = acc
        return carry

    lax.fori_loop(0, last - first, slot_step, 0)


def disco_piece(src_rows, coef, ext, weight_flat, piece, pieces, lon_count):
    slot_total = ext.shape[0] - 2
    first = piece * slot_total // pieces
    last = (piece + 1) * slot_total // pieces
    lon_pad, channels = ext.shape[1:]
    out_rows = round_up(lon_count, CHUNK)
    smem = pltpu.MemorySpace.SMEM if hasattr(pltpu, "MemorySpace") else pltpu.SMEM
    return pl.pallas_call(
        functools.partial(disco_body, first, last),
        out_shape=jax.ShapeDtypeStruct((last - first, out_rows, channels), jnp.float32),
        in_specs=[
            pl.BlockSpec(memory_space=smem),
            pl.BlockSpec(memory_space=smem),
            pl.BlockSpec(memory_space=pltpu.VMEM),
            pl.BlockSpec(memory_space=pltpu.VMEM),
        ],
        out_specs=pl.BlockSpec(memory_space=pltpu.VMEM),
        scratch_shapes=[pltpu.VMEM((last - first + 2, lon_pad, weight_flat.shape[1]), jnp.float32)],
    )(src_rows, coef, ext, weight_flat)


def disco_tables(band_rows, disco_kernel, band_index, band_total, row_count):
    slot_ids = jnp.arange(row_count, dtype=jnp.int32)
    live_rows = band_rows[band_index]
    has_next = slot_ids + 1 < live_rows
    prev_band = jnp.maximum(band_index - 1, 0)
    next_band = jnp.minimum(band_index + 1, band_total - 1)
    base = band_index * row_count
    up_src = jnp.where(slot_ids == 0, 0, slot_ids)
    down_src = jnp.where(has_next, slot_ids + 2, row_count + 1)
    src = jnp.stack([up_src, slot_ids + 1, down_src], axis=1)
    up_row = jnp.where(
        slot_ids == 0, prev_band * row_count + band_rows[prev_band] - 1, base + slot_ids - 1
    )
    down_row = jnp.where(has_next, base + slot_ids + 1, next_band * row_count)
    kernel_row = jnp.stack([up_row, base + slot_ids, down_row], axis=1)
    kernel_row = jnp.clip(kernel_row, 0, disco_kernel.shape[0] - 1)
    up_ok = (slot_ids > 0) | (band_index > 0)
    down_ok = has_next | (band_index < band_total - 1)
    valid = jnp.stack([up_ok, jnp.ones_like(up_ok), down_ok], axis=1)
    gathered = disco_kernel[kernel_row]
    gathered = gathered.reshape(row_count, 3, 3, 3, disco_kernel.shape[2])
    coef = jnp.stack([gathered[:, 0, 2], gathered[:, 1, 1], gathered[:, 2, 0]], axis=1)
    coef = jnp.where(valid[:, :, None, None], coef, 0.0)
    return src.reshape(-1).astype(jnp.int32), coef.reshape(-1).astype(jnp.float32)


def lat_extend(block, live_rows):
    lat_total = lax.axis_size("lat")
    lat_up = [(i, (i + 1) % lat_total) for i in range(lat_total)]
    lat_down = [(j, i) for i, j in lat_up]
    last_row = lax.dynamic_slice_in_dim(block, live_rows - 1, 1, 0)
    from_above = lax.ppermute(last_row, "lat", lat_up)
    from_below = lax.ppermute(block[0:1], "lat", lat_down)
    return jnp.concatenate([from_above, block, from_below], axis=0)


def pad_lon(rows, lon_count):
    lon_pad = round_up(round_up(lon_count, CHUNK) + 2, 16)
    pad = jnp.zeros((rows.shape[0], lon_pad - rows.shape[1], rows.shape[2]), rows.dtype)
    return jnp.concatenate([rows, pad], axis=1)


def halo_extend(masked, live_rows):
    row_count, lon_count, channels = masked.shape
    lat_total = lax.axis_size("lat")
    lon_total = lax.axis_size("lon")
    lat_up = [(i, (i + 1) % lat_total) for i in range(lat_total)]
    lat_down = [(j, i) for i, j in lat_up]
    lon_up = [(i, (i + 1) % lon_total) for i in range(lon_total)]
    lon_down = [(j, i) for i, j in lon_up]
    last_row = lax.dynamic_slice_in_dim(masked, live_rows - 1, 1, 0)
    from_above = lax.ppermute(last_row, "lat", lat_up)
    from_below = lax.ppermute(masked[0:1], "lat", lat_down)
    rows = jnp.concatenate([from_above, masked, from_below], axis=0)
    from_left = lax.ppermute(rows[:, lon_count - 1 : lon_count], "lon", lon_up)
    from_right = lax.ppermute(rows[:, 0:1], "lon", lon_down)
    lon_pad = round_up(round_up(lon_count, CHUNK) + 2, 16)
    pad = jnp.zeros((row_count + 2, lon_pad - lon_count - 2, channels), masked.dtype)
    return jnp.concatenate([from_left, rows, from_right, pad], axis=1)


def spectral_by_channels(
    masked, legendre, quad_weights, spectral_filter, trig_parts, live_rows, disco_work, prep
):
    ext = halo_extend(masked, live_rows)
    channels = masked.shape[2]
    lon_index = lax.axis_index("lon")
    chan_share = channels // lax.axis_size("lon")
    disco_parts = []
    portion = lax.all_to_all(masked, "lon", split_axis=2, concat_axis=1, tiled=True)
    spectra = jnp.stack(
        [dot_split("rnc,nk->rkc", (portion,), parts).astype(jnp.bfloat16) for parts in trig_parts],
        axis=1,
    )
    spectra, ext_now = lax.optimization_barrier((spectra, ext))
    columns = lax.all_to_all(spectra, "lat", split_axis=2, concat_axis=0, tiled=True)
    disco_parts.append(disco_work(ext_now, 0, prep))
    columns, disco_parts[0] = lax.optimization_barrier((columns, disco_parts[0]))
    legendre_parts = split_bf16(legendre)
    coefficients = dot_split("mls,spmc->lpmc", legendre_parts, (columns,))
    filter_slice = lax.dynamic_slice_in_dim(spectral_filter, lon_index * chan_share, chan_share, 2)
    filter_real = filter_slice[0][:, None, :]
    filter_imag = filter_slice[1][:, None, :]
    real_part = coefficients[:, 0]
    imag_part = coefficients[:, 1]
    filtered = jnp.stack(
        [
            filter_real * real_part + filter_imag * imag_part,
            filter_real * imag_part - filter_imag * real_part,
        ],
        axis=1,
    )
    returned = dot_split("mls,lpmc->spmc", legendre_parts, split_bf16(filtered))
    returned = (returned * quad_weights[:, None, None, None]).astype(jnp.bfloat16)
    returned, ext_now = lax.optimization_barrier((returned, ext))
    portion = lax.all_to_all(returned, "lat", split_axis=0, concat_axis=2, tiled=True)
    disco_parts.append(disco_work(ext_now, 1, prep))
    portion, disco_parts = lax.optimization_barrier((portion, disco_parts))
    spectral_rows = None
    for p, parts in enumerate(trig_parts):
        term = dot_split("rkc,nk->rnc", (portion[:, p],), parts)
        spectral_rows = term if spectral_rows is None else spectral_rows + term
    spectral_rows = spectral_rows.astype(jnp.bfloat16)
    spectral_rows, ext_now = lax.optimization_barrier((spectral_rows, ext))
    spectral = lax.all_to_all(spectral_rows, "lon", split_axis=1, concat_axis=2, tiled=True)
    disco_parts.append(disco_work(ext_now, 2, prep))
    spectral, disco_parts = lax.optimization_barrier((spectral, disco_parts))
    return spectral, disco_parts


def filter_modes(coefficients, spectral_filter):
    filter_real = spectral_filter[0][:, None, :]
    filter_imag = spectral_filter[1][:, None, :]
    real_part = coefficients[:, 0]
    imag_part = coefficients[:, 1]
    return jnp.stack(
        [
            filter_real * real_part + filter_imag * imag_part,
            filter_real * imag_part - filter_imag * real_part,
        ],
        axis=1,
    )


def spectral_by_modes(
    masked, legendre, quad_weights, spectral_filter, trig_parts, live_rows, disco_work, prep
):
    both = ("lat", "lon")
    lon_total = lax.axis_size("lon")
    mode_share = legendre.shape[0] // lon_total
    row_count, lon_count, channels = masked.shape
    share = row_count // lon_total
    body = masked.reshape(lon_total, share * lon_count, channels)
    edges = jnp.concatenate([masked[:, 0], masked[:, lon_count - 1]], axis=0)
    edges = jnp.broadcast_to(edges[None], (lon_total, 2 * row_count, channels))
    received = lax.all_to_all(
        jnp.concatenate([body, edges], axis=1), "lon", split_axis=0, concat_axis=0, tiled=True
    )
    own_legendre = lax.dynamic_slice_in_dim(
        legendre, lax.axis_index("lon") * mode_share, mode_share, 0
    )
    legendre_parts = split_bf16(own_legendre)
    received, legendre_parts, prep = lax.optimization_barrier((received, legendre_parts, prep))
    portion = received[:, : share * lon_count].reshape(lon_total, share, lon_count, channels)
    portion = portion.transpose(1, 0, 2, 3).reshape(share, lon_total * lon_count, channels)
    edge_block = received[:, share * lon_count :]
    lon_index = lax.axis_index("lon")
    left = lax.dynamic_index_in_dim(edge_block, (lon_index - 1) % lon_total, 0, keepdims=False)
    right = lax.dynamic_index_in_dim(edge_block, (lon_index + 1) % lon_total, 0, keepdims=False)
    own = jnp.concatenate([left[row_count:, None], masked, right[:row_count, None]], axis=1)
    ext = pad_lon(lat_extend(own, live_rows), lon_count)
    disco_parts = []
    spectra = jnp.stack(
        [dot_split("rnc,nk->rkc", (portion,), parts).astype(jnp.bfloat16) for parts in trig_parts],
        axis=1,
    )
    spectra, ext_now = lax.optimization_barrier((spectra, ext))
    columns = lax.all_to_all(spectra, both, split_axis=2, concat_axis=0, tiled=True)
    disco_parts.append(disco_work(ext_now, 0, prep))
    columns, disco_parts[0] = lax.optimization_barrier((columns, disco_parts[0]))
    coefficients = dot_split("mls,spmc->lpmc", legendre_parts, (columns,))
    filtered = filter_modes(coefficients, spectral_filter)
    returned = dot_split("mls,lpmc->spmc", legendre_parts, split_bf16(filtered))
    returned = (returned * quad_weights[:, None, None, None]).astype(jnp.bfloat16)
    returned, ext_now = lax.optimization_barrier((returned, ext))
    portion = lax.all_to_all(returned, both, split_axis=0, concat_axis=2, tiled=True)
    disco_parts.append(disco_work(ext_now, 1, prep))
    portion, disco_parts = lax.optimization_barrier((portion, disco_parts))
    spectral_rows = None
    for p, parts in enumerate(trig_parts):
        term = dot_split("rkc,nk->rnc", (portion[:, p],), parts)
        spectral_rows = term if spectral_rows is None else spectral_rows + term
    spectral_rows = spectral_rows.astype(jnp.bfloat16)
    spectral_rows, ext_now = lax.optimization_barrier((spectral_rows, ext))
    spectral = lax.all_to_all(spectral_rows, "lon", split_axis=1, concat_axis=0, tiled=True)
    disco_parts.append(disco_work(ext_now, 2, prep))
    spectral, disco_parts = lax.optimization_barrier((spectral, disco_parts))
    return spectral, disco_parts


def on_device(
    grad_output, band_rows, legendre, quad_weights, spectral_filter, disco_kernel, disco_weight
):
    row_count, lon_count, channels = grad_output.shape
    band_index = lax.axis_index("lat")
    band_total = lax.axis_size("lat")
    lon_total = lax.axis_size("lon")
    point_count = lon_count * lon_total
    mode_count = legendre.shape[0] * band_total
    slot_ids = jnp.arange(row_count, dtype=jnp.int32)
    live_rows = band_rows[band_index]
    live_slot = slot_ids < live_rows
    masked = jnp.where(live_slot[:, None, None], grad_output, jnp.zeros_like(grad_output))
    trig_parts = make_trig(mode_count, point_count)
    src_rows, coef = disco_tables(band_rows, disco_kernel, band_index, band_total, row_count)
    weight_flat = disco_weight.reshape(channels, -1)
    pieces = min(3, row_count)

    def disco_work(ext_now, piece, prep):
        return disco_piece(prep[0], prep[1], ext_now, prep[2], piece, pieces, lon_count)

    by_modes = legendre.shape[0] % lon_total == 0 and row_count % lon_total == 0
    path = spectral_by_modes if by_modes else spectral_by_channels
    spectral, disco_parts = path(
        masked,
        legendre,
        quad_weights,
        spectral_filter,
        trig_parts,
        live_rows,
        disco_work,
        (src_rows, coef, weight_flat),
    )
    disco_full = jnp.concatenate(disco_parts, axis=0)
    disco_term = disco_full[:, :lon_count, :]
    summed = masked.astype(jnp.float32) + disco_term + spectral.astype(jnp.float32)
    return jnp.where(live_slot[:, None, None], summed, 0.0).astype(jnp.bfloat16)


def solution(mesh):
    placed = (P("lat", "lon", None), P(), P("lat", None, None), P(), P(), P(), P())
    return jax.shard_map(
        on_device, mesh=mesh, in_specs=placed, out_specs=P("lat", "lon", None), check_vma=False
    )
```

```python
import functools

import ml_dtypes
import numpy as np
import jax
import jax.numpy as jnp
from jax import lax
from jax.experimental import pallas as pl
from jax.experimental.pallas import tpu as pltpu
from jax.sharding import PartitionSpec as P


def make_trig(mode_count, point_count):
    step = 16 if point_count % 16 == 0 else 1
    coarse = np.arange(point_count // step)[:, None] * step
    fine = np.arange(step)[:, None]
    wavenumber = np.arange(mode_count)[None, :]
    coarse_angle = (wavenumber * coarse % point_count) * (2.0 * np.pi / point_count)
    fine_angle = (wavenumber * fine % point_count) * (2.0 * np.pi / point_count)
    scale = point_count ** (-0.5)
    coarse_cos = jnp.asarray((np.cos(coarse_angle) * scale).astype(np.float32))[:, None, :]
    coarse_sin = jnp.asarray((np.sin(coarse_angle) * scale).astype(np.float32))[:, None, :]
    fine_cos = jnp.asarray(np.cos(fine_angle).astype(np.float32))[None, :, :]
    fine_sin = jnp.asarray(np.sin(fine_angle).astype(np.float32))[None, :, :]
    cosine = coarse_cos * fine_cos - coarse_sin * fine_sin
    minus_sine = -(coarse_sin * fine_cos + coarse_cos * fine_sin)
    return tuple(
        split_bf16(part.reshape(point_count, mode_count)) for part in (cosine, minus_sine)
    )


def split_bf16(values):
    rounded = lax.reduce_precision(values, exponent_bits=8, mantissa_bits=7)
    return rounded.astype(jnp.bfloat16), (values - rounded).astype(jnp.bfloat16)


def dot_split(spec, left_parts, right_parts):
    total = None
    for lp in left_parts:
        for rp in right_parts:
            if lp is not left_parts[0] and rp is not right_parts[0]:
                continue
            term = jnp.einsum(spec, lp, rp, preferred_element_type=jnp.float32)
            total = term if total is None else total + term
    return total


CHUNK = 64


def round_up(value, step):
    return -(-value // step) * step


def disco_body(first, last, src_ref, coef_ref, ext_ref, w_ref, out_ref, mix_ref):
    kinds = w_ref.shape[1] // w_ref.shape[0]
    channels = w_ref.shape[0]
    for r in range(last - first + 2):
        mix_ref[r] = jnp.dot(ext_ref[first + r], w_ref[...], preferred_element_type=jnp.float32)

    def slot_step(s, carry):
        for c0 in range(0, out_ref.shape[1], CHUNK):
            acc = jnp.zeros((CHUNK, channels), jnp.float32)
            for a_i in range(3):
                row = src_ref[(first + s) * 3 + a_i] - first
                for b_i in range(3):
                    for k in range(kinds):
                        coef = coef_ref[(((first + s) * 3 + a_i) * 3 + b_i) * kinds + k]
                        acc = acc + coef * mix_ref[
                            row, pl.ds(c0 + 2 - b_i, CHUNK), pl.ds(k * channels, channels)
                        ]
            out_ref[s, pl.ds(c0, CHUNK), :] = acc
        return carry

    lax.fori_loop(0, last - first, slot_step, 0)


def disco_piece(src_rows, coef, ext, weight_flat, piece, pieces, lon_count):
    slot_total = ext.shape[0] - 2
    first = piece * slot_total // pieces
    last = (piece + 1) * slot_total // pieces
    lon_pad, channels = ext.shape[1:]
    out_rows = round_up(lon_count, CHUNK)
    smem = pltpu.MemorySpace.SMEM if hasattr(pltpu, "MemorySpace") else pltpu.SMEM
    return pl.pallas_call(
        functools.partial(disco_body, first, last),
        out_shape=jax.ShapeDtypeStruct((last - first, out_rows, channels), jnp.float32),
        in_specs=[
            pl.BlockSpec(memory_space=smem),
            pl.BlockSpec(memory_space=smem),
            pl.BlockSpec(memory_space=pltpu.VMEM),
            pl.BlockSpec(memory_space=pltpu.VMEM),
        ],
        out_specs=pl.BlockSpec(memory_space=pltpu.VMEM),
        scratch_shapes=[pltpu.VMEM((last - first + 2, lon_pad, weight_flat.shape[1]), jnp.float32)],
    )(src_rows, coef, ext, weight_flat)


def disco_tables(band_rows, disco_kernel, band_index, band_total, row_count):
    slot_ids = jnp.arange(row_count, dtype=jnp.int32)
    live_rows = band_rows[band_index]
    has_next = slot_ids + 1 < live_rows
    prev_band = jnp.maximum(band_index - 1, 0)
    next_band = jnp.minimum(band_index + 1, band_total - 1)
    base = band_index * row_count
    up_src = jnp.where(slot_ids == 0, 0, slot_ids)
    down_src = jnp.where(has_next, slot_ids + 2, row_count + 1)
    src = jnp.stack([up_src, slot_ids + 1, down_src], axis=1)
    up_row = jnp.where(
        slot_ids == 0, prev_band * row_count + band_rows[prev_band] - 1, base + slot_ids - 1
    )
    down_row = jnp.where(has_next, base + slot_ids + 1, next_band * row_count)
    kernel_row = jnp.stack([up_row, base + slot_ids, down_row], axis=1)
    kernel_row = jnp.clip(kernel_row, 0, disco_kernel.shape[0] - 1)
    up_ok = (slot_ids > 0) | (band_index > 0)
    down_ok = has_next | (band_index < band_total - 1)
    valid = jnp.stack([up_ok, jnp.ones_like(up_ok), down_ok], axis=1)
    gathered = disco_kernel[kernel_row]
    gathered = gathered.reshape(row_count, 3, 3, 3, disco_kernel.shape[2])
    coef = jnp.stack([gathered[:, 0, 2], gathered[:, 1, 1], gathered[:, 2, 0]], axis=1)
    coef = jnp.where(valid[:, :, None, None], coef, 0.0)
    return src.reshape(-1).astype(jnp.int32), coef.reshape(-1).astype(jnp.float32)


def lat_extend(block, live_rows):
    lat_total = lax.axis_size("lat")
    lat_up = [(i, (i + 1) % lat_total) for i in range(lat_total)]
    lat_down = [(j, i) for i, j in lat_up]
    last_row = lax.dynamic_slice_in_dim(block, live_rows - 1, 1, 0)
    from_above = lax.ppermute(last_row, "lat", lat_up)
    from_below = lax.ppermute(block[0:1], "lat", lat_down)
    return jnp.concatenate([from_above, block, from_below], axis=0)


def pad_lon(rows, lon_count):
    lon_pad = round_up(round_up(lon_count, CHUNK) + 2, 16)
    pad = jnp.zeros((rows.shape[0], lon_pad - rows.shape[1], rows.shape[2]), rows.dtype)
    return jnp.concatenate([rows, pad], axis=1)


def halo_extend(masked, live_rows):
    row_count, lon_count, channels = masked.shape
    lat_total = lax.axis_size("lat")
    lon_total = lax.axis_size("lon")
    lat_up = [(i, (i + 1) % lat_total) for i in range(lat_total)]
    lat_down = [(j, i) for i, j in lat_up]
    lon_up = [(i, (i + 1) % lon_total) for i in range(lon_total)]
    lon_down = [(j, i) for i, j in lon_up]
    last_row = lax.dynamic_slice_in_dim(masked, live_rows - 1, 1, 0)
    from_above = lax.ppermute(last_row, "lat", lat_up)
    from_below = lax.ppermute(masked[0:1], "lat", lat_down)
    rows = jnp.concatenate([from_above, masked, from_below], axis=0)
    from_left = lax.ppermute(rows[:, lon_count - 1 : lon_count], "lon", lon_up)
    from_right = lax.ppermute(rows[:, 0:1], "lon", lon_down)
    lon_pad = round_up(round_up(lon_count, CHUNK) + 2, 16)
    pad = jnp.zeros((row_count + 2, lon_pad - lon_count - 2, channels), masked.dtype)
    return jnp.concatenate([from_left, rows, from_right, pad], axis=1)


def spectral_by_channels(
    masked, legendre, quad_weights, spectral_filter, trig_parts, live_rows, disco_work, prep
):
    ext = halo_extend(masked, live_rows)
    channels = masked.shape[2]
    lon_index = lax.axis_index("lon")
    chan_share = channels // lax.axis_size("lon")
    disco_parts = []
    portion = lax.all_to_all(masked, "lon", split_axis=2, concat_axis=1, tiled=True)
    spectra = jnp.stack(
        [dot_split("rnc,nk->rkc", (portion,), parts).astype(jnp.bfloat16) for parts in trig_parts],
        axis=1,
    )
    spectra, ext_now = lax.optimization_barrier((spectra, ext))
    columns = lax.all_to_all(spectra, "lat", split_axis=2, concat_axis=0, tiled=True)
    disco_parts.append(disco_work(ext_now, 0, prep))
    columns, disco_parts[0] = lax.optimization_barrier((columns, disco_parts[0]))
    legendre_parts = split_bf16(legendre)
    coefficients = dot_split("mls,spmc->lpmc", legendre_parts, (columns,))
    filter_slice = lax.dynamic_slice_in_dim(spectral_filter, lon_index * chan_share, chan_share, 2)
    filter_real = filter_slice[0][:, None, :]
    filter_imag = filter_slice[1][:, None, :]
    real_part = coefficients[:, 0]
    imag_part = coefficients[:, 1]
    filtered = jnp.stack(
        [
            filter_real * real_part + filter_imag * imag_part,
            filter_real * imag_part - filter_imag * real_part,
        ],
        axis=1,
    )
    returned = dot_split("mls,lpmc->spmc", legendre_parts, split_bf16(filtered))
    returned = (returned * quad_weights[:, None, None, None]).astype(jnp.bfloat16)
    returned, ext_now = lax.optimization_barrier((returned, ext))
    portion = lax.all_to_all(returned, "lat", split_axis=0, concat_axis=2, tiled=True)
    disco_parts.append(disco_work(ext_now, 1, prep))
    portion, disco_parts = lax.optimization_barrier((portion, disco_parts))
    spectral_rows = None
    for p, parts in enumerate(trig_parts):
        term = dot_split("rkc,nk->rnc", (portion[:, p],), parts)
        spectral_rows = term if spectral_rows is None else spectral_rows + term
    spectral_rows = spectral_rows.astype(jnp.bfloat16)
    spectral_rows, ext_now = lax.optimization_barrier((spectral_rows, ext))
    spectral = lax.all_to_all(spectral_rows, "lon", split_axis=1, concat_axis=2, tiled=True)
    disco_parts.append(disco_work(ext_now, 2, prep))
    spectral, disco_parts = lax.optimization_barrier((spectral, disco_parts))
    return spectral, disco_parts


def filter_modes(coefficients, spectral_filter):
    filter_real = spectral_filter[0][:, None, :]
    filter_imag = spectral_filter[1][:, None, :]
    real_part = coefficients[:, 0]
    imag_part = coefficients[:, 1]
    return jnp.stack(
        [
            filter_real * real_part + filter_imag * imag_part,
            filter_real * imag_part - filter_imag * real_part,
        ],
        axis=1,
    )


def spectral_by_modes(
    masked, legendre, quad_weights, spectral_filter, trig_parts, live_rows, disco_work, prep
):
    both = ("lat", "lon")
    lon_total = lax.axis_size("lon")
    mode_share = legendre.shape[0] // lon_total
    row_count, lon_count, channels = masked.shape
    share = row_count // lon_total
    body = masked.reshape(lon_total, share * lon_count, channels)
    edges = jnp.concatenate([masked[:, 0], masked[:, lon_count - 1]], axis=0)
    edges = jnp.broadcast_to(edges[None], (lon_total, 2 * row_count, channels))
    received = lax.all_to_all(
        jnp.concatenate([body, edges], axis=1), "lon", split_axis=0, concat_axis=0, tiled=True
    )
    own_legendre = lax.dynamic_slice_in_dim(
        legendre, lax.axis_index("lon") * mode_share, mode_share, 0
    )
    legendre_parts = split_bf16(own_legendre)
    received, legendre_parts, prep = lax.optimization_barrier((received, legendre_parts, prep))
    portion = received[:, : share * lon_count].reshape(lon_total, share, lon_count, channels)
    portion = portion.transpose(1, 0, 2, 3).reshape(share, lon_total * lon_count, channels)
    edge_block = received[:, share * lon_count :]
    lon_index = lax.axis_index("lon")
    left = lax.dynamic_index_in_dim(edge_block, (lon_index - 1) % lon_total, 0, keepdims=False)
    right = lax.dynamic_index_in_dim(edge_block, (lon_index + 1) % lon_total, 0, keepdims=False)
    own = jnp.concatenate([left[row_count:, None], masked, right[:row_count, None]], axis=1)
    disco_parts = []
    spectra = jnp.stack(
        [dot_split("rnc,nk->rkc", (portion,), parts).astype(jnp.bfloat16) for parts in trig_parts],
        axis=1,
    )
    spectra, own = lax.optimization_barrier((spectra, own))
    ext = pad_lon(lat_extend(own, live_rows), lon_count)
    ext_now = ext
    columns = lax.all_to_all(spectra, both, split_axis=2, concat_axis=0, tiled=True)
    disco_parts.append(disco_work(ext_now, 0, prep))
    columns, disco_parts[0] = lax.optimization_barrier((columns, disco_parts[0]))
    coefficients = dot_split("mls,spmc->lpmc", legendre_parts, (columns,))
    filtered = filter_modes(coefficients, spectral_filter)
    returned = dot_split("mls,lpmc->spmc", legendre_parts, split_bf16(filtered))
    returned = (returned * quad_weights[:, None, None, None]).astype(jnp.bfloat16)
    returned, ext_now = lax.optimization_barrier((returned, ext))
    portion = lax.all_to_all(returned, both, split_axis=0, concat_axis=2, tiled=True)
    disco_parts.append(disco_work(ext_now, 1, prep))
    portion, disco_parts = lax.optimization_barrier((portion, disco_parts))
    spectral_rows = None
    for p, parts in enumerate(trig_parts):
        term = dot_split("rkc,nk->rnc", (portion[:, p],), parts)
        spectral_rows = term if spectral_rows is None else spectral_rows + term
    spectral_rows = spectral_rows.astype(jnp.bfloat16)
    spectral_rows, ext_now = lax.optimization_barrier((spectral_rows, ext))
    spectral = lax.all_to_all(spectral_rows, "lon", split_axis=1, concat_axis=0, tiled=True)
    disco_parts.append(disco_work(ext_now, 2, prep))
    spectral, disco_parts = lax.optimization_barrier((spectral, disco_parts))
    return spectral, disco_parts


def on_device(
    grad_output, band_rows, legendre, quad_weights, spectral_filter, disco_kernel, disco_weight
):
    row_count, lon_count, channels = grad_output.shape
    band_index = lax.axis_index("lat")
    band_total = lax.axis_size("lat")
    lon_total = lax.axis_size("lon")
    point_count = lon_count * lon_total
    mode_count = legendre.shape[0] * band_total
    slot_ids = jnp.arange(row_count, dtype=jnp.int32)
    live_rows = band_rows[band_index]
    live_slot = slot_ids < live_rows
    masked = jnp.where(live_slot[:, None, None], grad_output, jnp.zeros_like(grad_output))
    trig_parts = make_trig(mode_count, point_count)
    src_rows, coef = disco_tables(band_rows, disco_kernel, band_index, band_total, row_count)
    weight_flat = disco_weight.reshape(channels, -1)
    pieces = min(3, row_count)

    def disco_work(ext_now, piece, prep):
        return disco_piece(prep[0], prep[1], ext_now, prep[2], piece, pieces, lon_count)

    by_modes = legendre.shape[0] % lon_total == 0 and row_count % lon_total == 0
    path = spectral_by_modes if by_modes else spectral_by_channels
    spectral, disco_parts = path(
        masked,
        legendre,
        quad_weights,
        spectral_filter,
        trig_parts,
        live_rows,
        disco_work,
        (src_rows, coef, weight_flat),
    )
    disco_full = jnp.concatenate(disco_parts, axis=0)
    disco_term = disco_full[:, :lon_count, :]
    summed = masked.astype(jnp.float32) + disco_term + spectral.astype(jnp.float32)
    return jnp.where(live_slot[:, None, None], summed, 0.0).astype(jnp.bfloat16)


def solution(mesh):
    placed = (P("lat", "lon", None), P(), P("lat", None, None), P(), P(), P(), P())
    return jax.shard_map(
        on_device, mesh=mesh, in_specs=placed, out_specs=P("lat", "lon", None), check_vma=False
    )
```

```python
import functools

import ml_dtypes
import numpy as np
import jax
import jax.numpy as jnp
from jax import lax
from jax.experimental import pallas as pl
from jax.experimental.pallas import tpu as pltpu
from jax.sharding import PartitionSpec as P


def make_trig(mode_count, point_count):
    step = 16 if point_count % 16 == 0 else 1
    coarse = np.arange(point_count // step)[:, None] * step
    fine = np.arange(step)[:, None]
    wavenumber = np.arange(mode_count)[None, :]
    coarse_angle = (wavenumber * coarse % point_count) * (2.0 * np.pi / point_count)
    fine_angle = (wavenumber * fine % point_count) * (2.0 * np.pi / point_count)
    scale = point_count ** (-0.5)
    coarse_cos = jnp.asarray((np.cos(coarse_angle) * scale).astype(np.float32))[:, None, :]
    coarse_sin = jnp.asarray((np.sin(coarse_angle) * scale).astype(np.float32))[:, None, :]
    fine_cos = jnp.asarray(np.cos(fine_angle).astype(np.float32))[None, :, :]
    fine_sin = jnp.asarray(np.sin(fine_angle).astype(np.float32))[None, :, :]
    cosine = coarse_cos * fine_cos - coarse_sin * fine_sin
    minus_sine = -(coarse_sin * fine_cos + coarse_cos * fine_sin)
    return tuple(
        split_bf16(part.reshape(point_count, mode_count)) for part in (cosine, minus_sine)
    )


def split_bf16(values):
    rounded = lax.reduce_precision(values, exponent_bits=8, mantissa_bits=7)
    return rounded.astype(jnp.bfloat16), (values - rounded).astype(jnp.bfloat16)


def dot_split(spec, left_parts, right_parts):
    total = None
    for lp in left_parts:
        for rp in right_parts:
            if lp is not left_parts[0] and rp is not right_parts[0]:
                continue
            term = jnp.einsum(spec, lp, rp, preferred_element_type=jnp.float32)
            total = term if total is None else total + term
    return total


CHUNK = 64


def round_up(value, step):
    return -(-value // step) * step


def disco_body(first, last, src_ref, coef_ref, ext_ref, w_ref, out_ref, mix_ref):
    kinds = w_ref.shape[1] // w_ref.shape[0]
    channels = w_ref.shape[0]
    for r in range(last - first + 2):
        mix_ref[r] = jnp.dot(ext_ref[first + r], w_ref[...], preferred_element_type=jnp.float32)

    def slot_step(s, carry):
        for c0 in range(0, out_ref.shape[1], CHUNK):
            acc = jnp.zeros((CHUNK, channels), jnp.float32)
            for a_i in range(3):
                row = src_ref[(first + s) * 3 + a_i] - first
                for b_i in range(3):
                    for k in range(kinds):
                        coef = coef_ref[(((first + s) * 3 + a_i) * 3 + b_i) * kinds + k]
                        acc = acc + coef * mix_ref[
                            row, pl.ds(c0 + 2 - b_i, CHUNK), pl.ds(k * channels, channels)
                        ]
            out_ref[s, pl.ds(c0, CHUNK), :] = acc
        return carry

    lax.fori_loop(0, last - first, slot_step, 0)


def disco_piece(src_rows, coef, ext, weight_flat, piece, pieces, lon_count):
    slot_total = ext.shape[0] - 2
    bounds = [i * slot_total // pieces for i in range(pieces + 1)]
    if pieces == 3 and slot_total >= 8:
        bounds = [0, slot_total // 8, slot_total // 2, slot_total]
    first, last = bounds[piece], bounds[piece + 1]
    lon_pad, channels = ext.shape[1:]
    out_rows = round_up(lon_count, CHUNK)
    smem = pltpu.MemorySpace.SMEM if hasattr(pltpu, "MemorySpace") else pltpu.SMEM
    return pl.pallas_call(
        functools.partial(disco_body, first, last),
        out_shape=jax.ShapeDtypeStruct((last - first, out_rows, channels), jnp.float32),
        in_specs=[
            pl.BlockSpec(memory_space=smem),
            pl.BlockSpec(memory_space=smem),
            pl.BlockSpec(memory_space=pltpu.VMEM),
            pl.BlockSpec(memory_space=pltpu.VMEM),
        ],
        out_specs=pl.BlockSpec(memory_space=pltpu.VMEM),
        scratch_shapes=[pltpu.VMEM((last - first + 2, lon_pad, weight_flat.shape[1]), jnp.float32)],
    )(src_rows, coef, ext, weight_flat)


def disco_tables(band_rows, disco_kernel, band_index, band_total, row_count):
    slot_ids = jnp.arange(row_count, dtype=jnp.int32)
    live_rows = band_rows[band_index]
    has_next = slot_ids + 1 < live_rows
    prev_band = jnp.maximum(band_index - 1, 0)
    next_band = jnp.minimum(band_index + 1, band_total - 1)
    base = band_index * row_count
    up_src = jnp.where(slot_ids == 0, 0, slot_ids)
    down_src = jnp.where(has_next, slot_ids + 2, row_count + 1)
    src = jnp.stack([up_src, slot_ids + 1, down_src], axis=1)
    up_row = jnp.where(
        slot_ids == 0, prev_band * row_count + band_rows[prev_band] - 1, base + slot_ids - 1
    )
    down_row = jnp.where(has_next, base + slot_ids + 1, next_band * row_count)
    kernel_row = jnp.stack([up_row, base + slot_ids, down_row], axis=1)
    kernel_row = jnp.clip(kernel_row, 0, disco_kernel.shape[0] - 1)
    up_ok = (slot_ids > 0) | (band_index > 0)
    down_ok = has_next | (band_index < band_total - 1)
    valid = jnp.stack([up_ok, jnp.ones_like(up_ok), down_ok], axis=1)
    gathered = disco_kernel[kernel_row]
    gathered = gathered.reshape(row_count, 3, 3, 3, disco_kernel.shape[2])
    coef = jnp.stack([gathered[:, 0, 2], gathered[:, 1, 1], gathered[:, 2, 0]], axis=1)
    coef = jnp.where(valid[:, :, None, None], coef, 0.0)
    return src.reshape(-1).astype(jnp.int32), coef.reshape(-1).astype(jnp.float32)


def lat_extend(block, live_rows):
    lat_total = lax.axis_size("lat")
    lat_up = [(i, (i + 1) % lat_total) for i in range(lat_total)]
    lat_down = [(j, i) for i, j in lat_up]
    last_row = lax.dynamic_slice_in_dim(block, live_rows - 1, 1, 0)
    from_above = lax.ppermute(last_row, "lat", lat_up)
    from_below = lax.ppermute(block[0:1], "lat", lat_down)
    return jnp.concatenate([from_above, block, from_below], axis=0)


def pad_lon(rows, lon_count):
    lon_pad = round_up(round_up(lon_count, CHUNK) + 2, 16)
    pad = jnp.zeros((rows.shape[0], lon_pad - rows.shape[1], rows.shape[2]), rows.dtype)
    return jnp.concatenate([rows, pad], axis=1)


def halo_extend(masked, live_rows):
    row_count, lon_count, channels = masked.shape
    lat_total = lax.axis_size("lat")
    lon_total = lax.axis_size("lon")
    lat_up = [(i, (i + 1) % lat_total) for i in range(lat_total)]
    lat_down = [(j, i) for i, j in lat_up]
    lon_up = [(i, (i + 1) % lon_total) for i in range(lon_total)]
    lon_down = [(j, i) for i, j in lon_up]
    last_row = lax.dynamic_slice_in_dim(masked, live_rows - 1, 1, 0)
    from_above = lax.ppermute(last_row, "lat", lat_up)
    from_below = lax.ppermute(masked[0:1], "lat", lat_down)
    rows = jnp.concatenate([from_above, masked, from_below], axis=0)
    from_left = lax.ppermute(rows[:, lon_count - 1 : lon_count], "lon", lon_up)
    from_right = lax.ppermute(rows[:, 0:1], "lon", lon_down)
    lon_pad = round_up(round_up(lon_count, CHUNK) + 2, 16)
    pad = jnp.zeros((row_count + 2, lon_pad - lon_count - 2, channels), masked.dtype)
    return jnp.concatenate([from_left, rows, from_right, pad], axis=1)


def spectral_by_channels(
    masked, legendre, quad_weights, spectral_filter, trig_parts, live_rows, disco_work, prep
):
    ext = halo_extend(masked, live_rows)
    channels = masked.shape[2]
    lon_index = lax.axis_index("lon")
    chan_share = channels // lax.axis_size("lon")
    disco_parts = []
    portion = lax.all_to_all(masked, "lon", split_axis=2, concat_axis=1, tiled=True)
    spectra = jnp.stack(
        [dot_split("rnc,nk->rkc", (portion,), parts).astype(jnp.bfloat16) for parts in trig_parts],
        axis=1,
    )
    spectra, ext_now = lax.optimization_barrier((spectra, ext))
    columns = lax.all_to_all(spectra, "lat", split_axis=2, concat_axis=0, tiled=True)
    disco_parts.append(disco_work(ext_now, 0, prep))
    columns, disco_parts[0] = lax.optimization_barrier((columns, disco_parts[0]))
    legendre_parts = split_bf16(legendre)
    coefficients = dot_split("mls,spmc->lpmc", legendre_parts, (columns,))
    filter_slice = lax.dynamic_slice_in_dim(spectral_filter, lon_index * chan_share, chan_share, 2)
    filter_real = filter_slice[0][:, None, :]
    filter_imag = filter_slice[1][:, None, :]
    real_part = coefficients[:, 0]
    imag_part = coefficients[:, 1]
    filtered = jnp.stack(
        [
            filter_real * real_part + filter_imag * imag_part,
            filter_real * imag_part - filter_imag * real_part,
        ],
        axis=1,
    )
    returned = dot_split("mls,lpmc->spmc", legendre_parts, split_bf16(filtered))
    returned = (returned * quad_weights[:, None, None, None]).astype(jnp.bfloat16)
    returned, ext_now = lax.optimization_barrier((returned, ext))
    portion = lax.all_to_all(returned, "lat", split_axis=0, concat_axis=2, tiled=True)
    disco_parts.append(disco_work(ext_now, 1, prep))
    portion, disco_parts = lax.optimization_barrier((portion, disco_parts))
    spectral_rows = None
    for p, parts in enumerate(trig_parts):
        term = dot_split("rkc,nk->rnc", (portion[:, p],), parts)
        spectral_rows = term if spectral_rows is None else spectral_rows + term
    spectral_rows = spectral_rows.astype(jnp.bfloat16)
    spectral_rows, ext_now = lax.optimization_barrier((spectral_rows, ext))
    spectral = lax.all_to_all(spectral_rows, "lon", split_axis=1, concat_axis=2, tiled=True)
    disco_parts.append(disco_work(ext_now, 2, prep))
    spectral, disco_parts = lax.optimization_barrier((spectral, disco_parts))
    return spectral, disco_parts


def filter_modes(coefficients, spectral_filter):
    filter_real = spectral_filter[0][:, None, :]
    filter_imag = spectral_filter[1][:, None, :]
    real_part = coefficients[:, 0]
    imag_part = coefficients[:, 1]
    return jnp.stack(
        [
            filter_real * real_part + filter_imag * imag_part,
            filter_real * imag_part - filter_imag * real_part,
        ],
        axis=1,
    )


def spectral_by_modes(
    masked, legendre, quad_weights, spectral_filter, trig_parts, live_rows, disco_work, prep
):
    both = ("lat", "lon")
    lon_total = lax.axis_size("lon")
    mode_share = legendre.shape[0] // lon_total
    row_count, lon_count, channels = masked.shape
    share = row_count // lon_total
    body = masked.reshape(lon_total, share * lon_count, channels)
    edges = jnp.concatenate([masked[:, 0], masked[:, lon_count - 1]], axis=0)
    edges = jnp.broadcast_to(edges[None], (lon_total, 2 * row_count, channels))
    received = lax.all_to_all(
        jnp.concatenate([body, edges], axis=1), "lon", split_axis=0, concat_axis=0, tiled=True
    )
    own_legendre = lax.dynamic_slice_in_dim(
        legendre, lax.axis_index("lon") * mode_share, mode_share, 0
    )
    legendre_parts = split_bf16(own_legendre)
    received, legendre_parts, prep = lax.optimization_barrier((received, legendre_parts, prep))
    portion = received[:, : share * lon_count].reshape(lon_total, share, lon_count, channels)
    portion = portion.transpose(1, 0, 2, 3).reshape(share, lon_total * lon_count, channels)
    edge_block = received[:, share * lon_count :]
    lon_index = lax.axis_index("lon")
    left = lax.dynamic_index_in_dim(edge_block, (lon_index - 1) % lon_total, 0, keepdims=False)
    right = lax.dynamic_index_in_dim(edge_block, (lon_index + 1) % lon_total, 0, keepdims=False)
    own = jnp.concatenate([left[row_count:, None], masked, right[:row_count, None]], axis=1)
    disco_parts = []
    spectra = jnp.stack(
        [dot_split("rnc,nk->rkc", (portion,), parts).astype(jnp.bfloat16) for parts in trig_parts],
        axis=1,
    )
    spectra, own = lax.optimization_barrier((spectra, own))
    ext = pad_lon(lat_extend(own, live_rows), lon_count)
    ext_now = ext
    columns = lax.all_to_all(spectra, both, split_axis=2, concat_axis=0, tiled=True)
    disco_parts.append(disco_work(ext_now, 0, prep))
    columns, disco_parts[0] = lax.optimization_barrier((columns, disco_parts[0]))
    coefficients = dot_split("mls,spmc->lpmc", legendre_parts, (columns,))
    filtered = filter_modes(coefficients, spectral_filter)
    returned = dot_split("mls,lpmc->spmc", legendre_parts, split_bf16(filtered))
    returned = (returned * quad_weights[:, None, None, None]).astype(jnp.bfloat16)
    returned, ext_now = lax.optimization_barrier((returned, ext))
    portion = lax.all_to_all(returned, both, split_axis=0, concat_axis=2, tiled=True)
    disco_parts.append(disco_work(ext_now, 1, prep))
    portion, disco_parts = lax.optimization_barrier((portion, disco_parts))
    spectral_rows = None
    for p, parts in enumerate(trig_parts):
        term = dot_split("rkc,nk->rnc", (portion[:, p],), parts)
        spectral_rows = term if spectral_rows is None else spectral_rows + term
    spectral_rows = spectral_rows.astype(jnp.bfloat16)
    spectral_rows, ext_now = lax.optimization_barrier((spectral_rows, ext))
    spectral = lax.all_to_all(spectral_rows, "lon", split_axis=1, concat_axis=0, tiled=True)
    disco_parts.append(disco_work(ext_now, 2, prep))
    spectral, disco_parts = lax.optimization_barrier((spectral, disco_parts))
    return spectral, disco_parts


def on_device(
    grad_output, band_rows, legendre, quad_weights, spectral_filter, disco_kernel, disco_weight
):
    row_count, lon_count, channels = grad_output.shape
    band_index = lax.axis_index("lat")
    band_total = lax.axis_size("lat")
    lon_total = lax.axis_size("lon")
    point_count = lon_count * lon_total
    mode_count = legendre.shape[0] * band_total
    slot_ids = jnp.arange(row_count, dtype=jnp.int32)
    live_rows = band_rows[band_index]
    live_slot = slot_ids < live_rows
    masked = jnp.where(live_slot[:, None, None], grad_output, jnp.zeros_like(grad_output))
    trig_parts = make_trig(mode_count, point_count)
    src_rows, coef = disco_tables(band_rows, disco_kernel, band_index, band_total, row_count)
    weight_flat = disco_weight.reshape(channels, -1)
    pieces = min(3, row_count)

    def disco_work(ext_now, piece, prep):
        return disco_piece(prep[0], prep[1], ext_now, prep[2], piece, pieces, lon_count)

    by_modes = legendre.shape[0] % lon_total == 0 and row_count % lon_total == 0
    path = spectral_by_modes if by_modes else spectral_by_channels
    spectral, disco_parts = path(
        masked,
        legendre,
        quad_weights,
        spectral_filter,
        trig_parts,
        live_rows,
        disco_work,
        (src_rows, coef, weight_flat),
    )
    disco_full = jnp.concatenate(disco_parts, axis=0)
    disco_term = disco_full[:, :lon_count, :]
    summed = masked.astype(jnp.float32) + disco_term + spectral.astype(jnp.float32)
    return jnp.where(live_slot[:, None, None], summed, 0.0).astype(jnp.bfloat16)


def solution(mesh):
    placed = (P("lat", "lon", None), P(), P("lat", None, None), P(), P(), P(), P())
    return jax.shard_map(
        on_device, mesh=mesh, in_specs=placed, out_specs=P("lat", "lon", None), check_vma=False
    )
```

```python
import functools

import ml_dtypes
import numpy as np
import jax
import jax.numpy as jnp
from jax import lax
from jax.experimental import pallas as pl
from jax.experimental.pallas import tpu as pltpu
from jax.sharding import PartitionSpec as P


def make_trig(mode_count, point_count):
    step = 16 if point_count % 16 == 0 else 1
    coarse = np.arange(point_count // step)[:, None] * step
    fine = np.arange(step)[:, None]
    wavenumber = np.arange(mode_count)[None, :]
    coarse_angle = (wavenumber * coarse % point_count) * (2.0 * np.pi / point_count)
    fine_angle = (wavenumber * fine % point_count) * (2.0 * np.pi / point_count)
    scale = point_count ** (-0.5)
    coarse_cos = jnp.asarray((np.cos(coarse_angle) * scale).astype(np.float32))[:, None, :]
    coarse_sin = jnp.asarray((np.sin(coarse_angle) * scale).astype(np.float32))[:, None, :]
    fine_cos = jnp.asarray(np.cos(fine_angle).astype(np.float32))[None, :, :]
    fine_sin = jnp.asarray(np.sin(fine_angle).astype(np.float32))[None, :, :]
    cosine = coarse_cos * fine_cos - coarse_sin * fine_sin
    minus_sine = -(coarse_sin * fine_cos + coarse_cos * fine_sin)
    return tuple(
        split_bf16(part.reshape(point_count, mode_count)) for part in (cosine, minus_sine)
    )


def split_bf16(values):
    rounded = lax.reduce_precision(values, exponent_bits=8, mantissa_bits=7)
    return rounded.astype(jnp.bfloat16), (values - rounded).astype(jnp.bfloat16)


def dot_split(spec, left_parts, right_parts):
    total = None
    for lp in left_parts:
        for rp in right_parts:
            if lp is not left_parts[0] and rp is not right_parts[0]:
                continue
            term = jnp.einsum(spec, lp, rp, preferred_element_type=jnp.float32)
            total = term if total is None else total + term
    return total


CHUNK = 64


def round_up(value, step):
    return -(-value // step) * step


def disco_body(first, last, src_ref, coef_ref, ext_ref, w_ref, out_ref, mix_ref):
    kinds = w_ref.shape[1] // w_ref.shape[0]
    channels = w_ref.shape[0]
    for r in range(last - first + 2):
        mix_ref[r] = jnp.dot(ext_ref[first + r], w_ref[...], preferred_element_type=jnp.float32)

    def slot_step(s, carry):
        for c0 in range(0, out_ref.shape[1], CHUNK):
            acc = jnp.zeros((CHUNK, channels), jnp.float32)
            for a_i in range(3):
                row = src_ref[(first + s) * 3 + a_i] - first
                for b_i in range(3):
                    for k in range(kinds):
                        coef = coef_ref[(((first + s) * 3 + a_i) * 3 + b_i) * kinds + k]
                        acc = acc + coef * mix_ref[
                            row, pl.ds(c0 + 2 - b_i, CHUNK), pl.ds(k * channels, channels)
                        ]
            out_ref[s, pl.ds(c0, CHUNK), :] = acc
        return carry

    lax.fori_loop(0, last - first, slot_step, 0)


def disco_piece(src_rows, coef, ext, weight_flat, piece, pieces, lon_count):
    slot_total = ext.shape[0] - 2
    bounds = [i * slot_total // pieces for i in range(pieces + 1)]
    if pieces == 3 and slot_total >= 8:
        bounds = [0, slot_total // 8, slot_total // 2, slot_total]
    first, last = bounds[piece], bounds[piece + 1]
    lon_pad, channels = ext.shape[1:]
    out_rows = round_up(lon_count, CHUNK)
    smem = pltpu.MemorySpace.SMEM if hasattr(pltpu, "MemorySpace") else pltpu.SMEM
    return pl.pallas_call(
        functools.partial(disco_body, first, last),
        out_shape=jax.ShapeDtypeStruct((last - first, out_rows, channels), jnp.float32),
        in_specs=[
            pl.BlockSpec(memory_space=smem),
            pl.BlockSpec(memory_space=smem),
            pl.BlockSpec(memory_space=pltpu.VMEM),
            pl.BlockSpec(memory_space=pltpu.VMEM),
        ],
        out_specs=pl.BlockSpec(memory_space=pltpu.VMEM),
        scratch_shapes=[pltpu.VMEM((last - first + 2, lon_pad, weight_flat.shape[1]), jnp.float32)],
    )(src_rows, coef, ext, weight_flat)


def disco_tables(band_rows, disco_kernel, band_index, band_total, row_count):
    slot_ids = jnp.arange(row_count, dtype=jnp.int32)
    live_rows = band_rows[band_index]
    has_next = slot_ids + 1 < live_rows
    prev_band = jnp.maximum(band_index - 1, 0)
    next_band = jnp.minimum(band_index + 1, band_total - 1)
    base = band_index * row_count
    up_src = jnp.where(slot_ids == 0, 0, slot_ids)
    down_src = jnp.where(has_next, slot_ids + 2, row_count + 1)
    src = jnp.stack([up_src, slot_ids + 1, down_src], axis=1)
    up_row = jnp.where(
        slot_ids == 0, prev_band * row_count + band_rows[prev_band] - 1, base + slot_ids - 1
    )
    down_row = jnp.where(has_next, base + slot_ids + 1, next_band * row_count)
    kernel_row = jnp.stack([up_row, base + slot_ids, down_row], axis=1)
    kernel_row = jnp.clip(kernel_row, 0, disco_kernel.shape[0] - 1)
    up_ok = (slot_ids > 0) | (band_index > 0)
    down_ok = has_next | (band_index < band_total - 1)
    valid = jnp.stack([up_ok, jnp.ones_like(up_ok), down_ok], axis=1)
    gathered = disco_kernel[kernel_row]
    gathered = gathered.reshape(row_count, 3, 3, 3, disco_kernel.shape[2])
    coef = jnp.stack([gathered[:, 0, 2], gathered[:, 1, 1], gathered[:, 2, 0]], axis=1)
    coef = jnp.where(valid[:, :, None, None], coef, 0.0)
    return src.reshape(-1).astype(jnp.int32), coef.reshape(-1).astype(jnp.float32)


def lat_extend(block, live_rows):
    lat_total = lax.axis_size("lat")
    lat_up = [(i, (i + 1) % lat_total) for i in range(lat_total)]
    lat_down = [(j, i) for i, j in lat_up]
    last_row = lax.dynamic_slice_in_dim(block, live_rows - 1, 1, 0)
    from_above = lax.ppermute(last_row, "lat", lat_up)
    from_below = lax.ppermute(block[0:1], "lat", lat_down)
    return jnp.concatenate([from_above, block, from_below], axis=0)


def pad_lon(rows, lon_count):
    lon_pad = round_up(round_up(lon_count, CHUNK) + 2, 16)
    pad = jnp.zeros((rows.shape[0], lon_pad - rows.shape[1], rows.shape[2]), rows.dtype)
    return jnp.concatenate([rows, pad], axis=1)


def halo_extend(masked, live_rows):
    row_count, lon_count, channels = masked.shape
    lat_total = lax.axis_size("lat")
    lon_total = lax.axis_size("lon")
    lat_up = [(i, (i + 1) % lat_total) for i in range(lat_total)]
    lat_down = [(j, i) for i, j in lat_up]
    lon_up = [(i, (i + 1) % lon_total) for i in range(lon_total)]
    lon_down = [(j, i) for i, j in lon_up]
    last_row = lax.dynamic_slice_in_dim(masked, live_rows - 1, 1, 0)
    from_above = lax.ppermute(last_row, "lat", lat_up)
    from_below = lax.ppermute(masked[0:1], "lat", lat_down)
    rows = jnp.concatenate([from_above, masked, from_below], axis=0)
    from_left = lax.ppermute(rows[:, lon_count - 1 : lon_count], "lon", lon_up)
    from_right = lax.ppermute(rows[:, 0:1], "lon", lon_down)
    lon_pad = round_up(round_up(lon_count, CHUNK) + 2, 16)
    pad = jnp.zeros((row_count + 2, lon_pad - lon_count - 2, channels), masked.dtype)
    return jnp.concatenate([from_left, rows, from_right, pad], axis=1)


def spectral_by_channels(
    masked, legendre, quad_weights, spectral_filter, trig_parts, live_rows, disco_work, prep, raw
):
    ext = halo_extend(masked, live_rows)
    channels = masked.shape[2]
    lon_index = lax.axis_index("lon")
    chan_share = channels // lax.axis_size("lon")
    disco_parts = []
    portion = lax.all_to_all(masked, "lon", split_axis=2, concat_axis=1, tiled=True)
    spectra = jnp.stack(
        [dot_split("rnc,nk->rkc", (portion,), parts).astype(jnp.bfloat16) for parts in trig_parts],
        axis=1,
    )
    spectra, ext_now = lax.optimization_barrier((spectra, ext))
    columns = lax.all_to_all(spectra, "lat", split_axis=2, concat_axis=0, tiled=True)
    disco_parts.append(disco_work(ext_now, 0, prep))
    columns, disco_parts[0] = lax.optimization_barrier((columns, disco_parts[0]))
    legendre_parts = split_bf16(legendre)
    coefficients = dot_split("mls,spmc->lpmc", legendre_parts, (columns,))
    filter_slice = lax.dynamic_slice_in_dim(spectral_filter, lon_index * chan_share, chan_share, 2)
    filter_real = filter_slice[0][:, None, :]
    filter_imag = filter_slice[1][:, None, :]
    real_part = coefficients[:, 0]
    imag_part = coefficients[:, 1]
    filtered = jnp.stack(
        [
            filter_real * real_part + filter_imag * imag_part,
            filter_real * imag_part - filter_imag * real_part,
        ],
        axis=1,
    )
    returned = dot_split("mls,lpmc->spmc", legendre_parts, split_bf16(filtered))
    returned = (returned * quad_weights[:, None, None, None]).astype(jnp.bfloat16)
    returned, ext_now = lax.optimization_barrier((returned, ext))
    portion = lax.all_to_all(returned, "lat", split_axis=0, concat_axis=2, tiled=True)
    disco_parts.append(disco_work(ext_now, 1, prep))
    portion, disco_parts = lax.optimization_barrier((portion, disco_parts))
    spectral_rows = None
    for p, parts in enumerate(trig_parts):
        term = dot_split("rkc,nk->rnc", (portion[:, p],), parts)
        spectral_rows = term if spectral_rows is None else spectral_rows + term
    spectral_rows = spectral_rows.astype(jnp.bfloat16)
    spectral_rows, ext_now = lax.optimization_barrier((spectral_rows, ext))
    spectral = lax.all_to_all(spectral_rows, "lon", split_axis=1, concat_axis=2, tiled=True)
    disco_parts.append(disco_work(ext_now, 2, prep))
    spectral, disco_parts = lax.optimization_barrier((spectral, disco_parts))
    return spectral, disco_parts


def filter_modes(coefficients, spectral_filter):
    filter_real = spectral_filter[0][:, None, :]
    filter_imag = spectral_filter[1][:, None, :]
    real_part = coefficients[:, 0]
    imag_part = coefficients[:, 1]
    return jnp.stack(
        [
            filter_real * real_part + filter_imag * imag_part,
            filter_real * imag_part - filter_imag * real_part,
        ],
        axis=1,
    )


def spectral_by_modes(
    masked, legendre, quad_weights, spectral_filter, trig_parts, live_rows, disco_work, prep, raw
):
    both = ("lat", "lon")
    lon_total = lax.axis_size("lon")
    mode_share = legendre.shape[0] // lon_total
    row_count, lon_count, channels = masked.shape
    share = row_count // lon_total
    body = raw.reshape(lon_total, share * lon_count, channels)
    edges = jnp.concatenate([raw[:, 0], raw[:, lon_count - 1]], axis=0)
    edges = jnp.broadcast_to(edges[None], (lon_total, 2 * row_count, channels))
    received = lax.all_to_all(
        jnp.concatenate([body, edges], axis=1), "lon", split_axis=0, concat_axis=0, tiled=True
    )
    own_legendre = lax.dynamic_slice_in_dim(
        legendre, lax.axis_index("lon") * mode_share, mode_share, 0
    )
    legendre_parts = split_bf16(own_legendre)
    received, legendre_parts, prep = lax.optimization_barrier((received, legendre_parts, prep))
    portion = received[:, : share * lon_count].reshape(lon_total, share, lon_count, channels)
    portion = portion.transpose(1, 0, 2, 3).reshape(share, lon_total * lon_count, channels)
    portion_live = lax.axis_index("lon") * share + jnp.arange(share) < live_rows
    portion = jnp.where(portion_live[:, None, None], portion, jnp.zeros_like(portion))
    edge_block = received[:, share * lon_count :]
    lon_index = lax.axis_index("lon")
    left = lax.dynamic_index_in_dim(edge_block, (lon_index - 1) % lon_total, 0, keepdims=False)
    right = lax.dynamic_index_in_dim(edge_block, (lon_index + 1) % lon_total, 0, keepdims=False)
    own = jnp.concatenate([left[row_count:, None], masked, right[:row_count, None]], axis=1)
    disco_parts = []
    spectra = jnp.stack(
        [dot_split("rnc,nk->rkc", (portion,), parts).astype(jnp.bfloat16) for parts in trig_parts],
        axis=1,
    )
    spectra, own = lax.optimization_barrier((spectra, own))
    ext = pad_lon(lat_extend(own, live_rows), lon_count)
    ext_now = ext
    columns = lax.all_to_all(spectra, both, split_axis=2, concat_axis=0, tiled=True)
    disco_parts.append(disco_work(ext_now, 0, prep))
    columns, disco_parts[0] = lax.optimization_barrier((columns, disco_parts[0]))
    coefficients = dot_split("mls,spmc->lpmc", legendre_parts, (columns,))
    filtered = filter_modes(coefficients, spectral_filter)
    returned = dot_split("mls,lpmc->spmc", legendre_parts, split_bf16(filtered))
    returned = (returned * quad_weights[:, None, None, None]).astype(jnp.bfloat16)
    returned, ext_now = lax.optimization_barrier((returned, ext))
    portion = lax.all_to_all(returned, both, split_axis=0, concat_axis=2, tiled=True)
    disco_parts.append(disco_work(ext_now, 1, prep))
    portion, disco_parts = lax.optimization_barrier((portion, disco_parts))
    spectral_rows = None
    for p, parts in enumerate(trig_parts):
        term = dot_split("rkc,nk->rnc", (portion[:, p],), parts)
        spectral_rows = term if spectral_rows is None else spectral_rows + term
    spectral_rows = spectral_rows.astype(jnp.bfloat16)
    spectral_rows, ext_now = lax.optimization_barrier((spectral_rows, ext))
    spectral = lax.all_to_all(spectral_rows, "lon", split_axis=1, concat_axis=0, tiled=True)
    disco_parts.append(disco_work(ext_now, 2, prep))
    spectral, disco_parts = lax.optimization_barrier((spectral, disco_parts))
    return spectral, disco_parts


def on_device(
    grad_output, band_rows, legendre, quad_weights, spectral_filter, disco_kernel, disco_weight
):
    row_count, lon_count, channels = grad_output.shape
    band_index = lax.axis_index("lat")
    band_total = lax.axis_size("lat")
    lon_total = lax.axis_size("lon")
    point_count = lon_count * lon_total
    mode_count = legendre.shape[0] * band_total
    slot_ids = jnp.arange(row_count, dtype=jnp.int32)
    live_rows = band_rows[band_index]
    live_slot = slot_ids < live_rows
    masked = jnp.where(live_slot[:, None, None], grad_output, jnp.zeros_like(grad_output))
    trig_parts = make_trig(mode_count, point_count)
    src_rows, coef = disco_tables(band_rows, disco_kernel, band_index, band_total, row_count)
    weight_flat = disco_weight.reshape(channels, -1)
    pieces = min(3, row_count)

    def disco_work(ext_now, piece, prep):
        return disco_piece(prep[0], prep[1], ext_now, prep[2], piece, pieces, lon_count)

    by_modes = legendre.shape[0] % lon_total == 0 and row_count % lon_total == 0
    path = spectral_by_modes if by_modes else spectral_by_channels
    spectral, disco_parts = path(
        masked,
        legendre,
        quad_weights,
        spectral_filter,
        trig_parts,
        live_rows,
        disco_work,
        (src_rows, coef, weight_flat),
        grad_output,
    )
    disco_full = jnp.concatenate(disco_parts, axis=0)
    disco_term = disco_full[:, :lon_count, :]
    summed = masked.astype(jnp.float32) + disco_term + spectral.astype(jnp.float32)
    return jnp.where(live_slot[:, None, None], summed, 0.0).astype(jnp.bfloat16)


def solution(mesh):
    placed = (P("lat", "lon", None), P(), P("lat", None, None), P(), P(), P(), P())
    return jax.shard_map(
        on_device, mesh=mesh, in_specs=placed, out_specs=P("lat", "lon", None), check_vma=False
    )
```

```python
import functools

import ml_dtypes
import numpy as np
import jax
import jax.numpy as jnp
from jax import lax
from jax.experimental import pallas as pl
from jax.experimental.pallas import tpu as pltpu
from jax.sharding import PartitionSpec as P


def make_trig(mode_count, point_count):
    step = 16 if point_count % 16 == 0 else 1
    coarse = np.arange(point_count // step)[:, None] * step
    fine = np.arange(step)[:, None]
    wavenumber = np.arange(mode_count)[None, :]
    coarse_angle = (wavenumber * coarse % point_count) * (2.0 * np.pi / point_count)
    fine_angle = (wavenumber * fine % point_count) * (2.0 * np.pi / point_count)
    scale = point_count ** (-0.5)
    coarse_cos = jnp.asarray((np.cos(coarse_angle) * scale).astype(np.float32))[:, None, :]
    coarse_sin = jnp.asarray((np.sin(coarse_angle) * scale).astype(np.float32))[:, None, :]
    fine_cos = jnp.asarray(np.cos(fine_angle).astype(np.float32))[None, :, :]
    fine_sin = jnp.asarray(np.sin(fine_angle).astype(np.float32))[None, :, :]
    cosine = coarse_cos * fine_cos - coarse_sin * fine_sin
    minus_sine = -(coarse_sin * fine_cos + coarse_cos * fine_sin)
    return tuple(
        split_bf16(part.reshape(point_count, mode_count)) for part in (cosine, minus_sine)
    )


def split_bf16(values):
    rounded = lax.reduce_precision(values, exponent_bits=8, mantissa_bits=7)
    return rounded.astype(jnp.bfloat16), (values - rounded).astype(jnp.bfloat16)


def dot_split(spec, left_parts, right_parts):
    total = None
    for lp in left_parts:
        for rp in right_parts:
            if lp is not left_parts[0] and rp is not right_parts[0]:
                continue
            term = jnp.einsum(spec, lp, rp, preferred_element_type=jnp.float32)
            total = term if total is None else total + term
    return total


CHUNK = 64


def round_up(value, step):
    return -(-value // step) * step


def disco_body(first, last, src_ref, coef_ref, ext_ref, w_ref, out_ref, mix_ref):
    kinds = w_ref.shape[1] // w_ref.shape[0]
    channels = w_ref.shape[0]
    span = last - first + 2
    below = ext_ref.shape[0] - 1
    for r in range(span):
        mix_ref[r] = jnp.dot(ext_ref[first + r], w_ref[...], preferred_element_type=jnp.float32)
    mix_ref[span] = jnp.dot(ext_ref[below], w_ref[...], preferred_element_type=jnp.float32)

    def slot_step(s, carry):
        for c0 in range(0, out_ref.shape[1], CHUNK):
            acc = jnp.zeros((CHUNK, channels), jnp.float32)
            for a_i in range(3):
                source = src_ref[(first + s) * 3 + a_i]
                row = jnp.where(source == below, span, source - first)
                for b_i in range(3):
                    for k in range(kinds):
                        coef = coef_ref[(((first + s) * 3 + a_i) * 3 + b_i) * kinds + k]
                        acc = acc + coef * mix_ref[
                            row, pl.ds(c0 + 2 - b_i, CHUNK), pl.ds(k * channels, channels)
                        ]
            out_ref[s, pl.ds(c0, CHUNK), :] = acc
        return carry

    lax.fori_loop(0, last - first, slot_step, 0)


def disco_piece(src_rows, coef, ext, weight_flat, piece, pieces, lon_count):
    slot_total = ext.shape[0] - 2
    bounds = [i * slot_total // pieces for i in range(pieces + 1)]
    if pieces == 3 and slot_total >= 8:
        bounds = [0, slot_total // 8, slot_total // 2, slot_total]
    first, last = bounds[piece], bounds[piece + 1]
    lon_pad, channels = ext.shape[1:]
    out_rows = round_up(lon_count, CHUNK)
    smem = pltpu.MemorySpace.SMEM if hasattr(pltpu, "MemorySpace") else pltpu.SMEM
    return pl.pallas_call(
        functools.partial(disco_body, first, last),
        out_shape=jax.ShapeDtypeStruct((last - first, out_rows, channels), jnp.float32),
        in_specs=[
            pl.BlockSpec(memory_space=smem),
            pl.BlockSpec(memory_space=smem),
            pl.BlockSpec(memory_space=pltpu.VMEM),
            pl.BlockSpec(memory_space=pltpu.VMEM),
        ],
        out_specs=pl.BlockSpec(memory_space=pltpu.VMEM),
        scratch_shapes=[pltpu.VMEM((last - first + 3, lon_pad, weight_flat.shape[1]), jnp.float32)],
    )(src_rows, coef, ext, weight_flat)


def disco_tables(band_rows, disco_kernel, band_index, band_total, row_count):
    slot_ids = jnp.arange(row_count, dtype=jnp.int32)
    live_rows = band_rows[band_index]
    has_next = slot_ids + 1 < live_rows
    prev_band = jnp.maximum(band_index - 1, 0)
    next_band = jnp.minimum(band_index + 1, band_total - 1)
    base = band_index * row_count
    up_src = jnp.where(slot_ids == 0, 0, slot_ids)
    down_src = jnp.where(has_next, slot_ids + 2, row_count + 1)
    src = jnp.stack([up_src, slot_ids + 1, down_src], axis=1)
    up_row = jnp.where(
        slot_ids == 0, prev_band * row_count + band_rows[prev_band] - 1, base + slot_ids - 1
    )
    down_row = jnp.where(has_next, base + slot_ids + 1, next_band * row_count)
    kernel_row = jnp.stack([up_row, base + slot_ids, down_row], axis=1)
    kernel_row = jnp.clip(kernel_row, 0, disco_kernel.shape[0] - 1)
    up_ok = (slot_ids > 0) | (band_index > 0)
    down_ok = has_next | (band_index < band_total - 1)
    valid = jnp.stack([up_ok, jnp.ones_like(up_ok), down_ok], axis=1)
    gathered = disco_kernel[kernel_row]
    gathered = gathered.reshape(row_count, 3, 3, 3, disco_kernel.shape[2])
    coef = jnp.stack([gathered[:, 0, 2], gathered[:, 1, 1], gathered[:, 2, 0]], axis=1)
    coef = jnp.where(valid[:, :, None, None], coef, 0.0)
    return src.reshape(-1).astype(jnp.int32), coef.reshape(-1).astype(jnp.float32)


def lat_extend(block, live_rows):
    lat_total = lax.axis_size("lat")
    lat_up = [(i, (i + 1) % lat_total) for i in range(lat_total)]
    lat_down = [(j, i) for i, j in lat_up]
    last_row = lax.dynamic_slice_in_dim(block, live_rows - 1, 1, 0)
    from_above = lax.ppermute(last_row, "lat", lat_up)
    from_below = lax.ppermute(block[0:1], "lat", lat_down)
    return jnp.concatenate([from_above, block, from_below], axis=0)


def pad_lon(rows, lon_count):
    lon_pad = round_up(round_up(lon_count, CHUNK) + 2, 16)
    pad = jnp.zeros((rows.shape[0], lon_pad - rows.shape[1], rows.shape[2]), rows.dtype)
    return jnp.concatenate([rows, pad], axis=1)


def halo_extend(masked, live_rows):
    row_count, lon_count, channels = masked.shape
    lat_total = lax.axis_size("lat")
    lon_total = lax.axis_size("lon")
    lat_up = [(i, (i + 1) % lat_total) for i in range(lat_total)]
    lat_down = [(j, i) for i, j in lat_up]
    lon_up = [(i, (i + 1) % lon_total) for i in range(lon_total)]
    lon_down = [(j, i) for i, j in lon_up]
    last_row = lax.dynamic_slice_in_dim(masked, live_rows - 1, 1, 0)
    from_above = lax.ppermute(last_row, "lat", lat_up)
    from_below = lax.ppermute(masked[0:1], "lat", lat_down)
    rows = jnp.concatenate([from_above, masked, from_below], axis=0)
    from_left = lax.ppermute(rows[:, lon_count - 1 : lon_count], "lon", lon_up)
    from_right = lax.ppermute(rows[:, 0:1], "lon", lon_down)
    lon_pad = round_up(round_up(lon_count, CHUNK) + 2, 16)
    pad = jnp.zeros((row_count + 2, lon_pad - lon_count - 2, channels), masked.dtype)
    return jnp.concatenate([from_left, rows, from_right, pad], axis=1)


def spectral_by_channels(
    masked, legendre, quad_weights, spectral_filter, trig_parts, live_rows, disco_work, prep, raw
):
    ext = halo_extend(masked, live_rows)
    channels = masked.shape[2]
    lon_index = lax.axis_index("lon")
    chan_share = channels // lax.axis_size("lon")
    disco_parts = []
    portion = lax.all_to_all(masked, "lon", split_axis=2, concat_axis=1, tiled=True)
    spectra = jnp.stack(
        [dot_split("rnc,nk->rkc", (portion,), parts).astype(jnp.bfloat16) for parts in trig_parts],
        axis=1,
    )
    spectra, ext_now = lax.optimization_barrier((spectra, ext))
    columns = lax.all_to_all(spectra, "lat", split_axis=2, concat_axis=0, tiled=True)
    disco_parts.append(disco_work(ext_now, 0, prep))
    columns, disco_parts[0] = lax.optimization_barrier((columns, disco_parts[0]))
    legendre_parts = split_bf16(legendre)
    coefficients = dot_split("mls,spmc->lpmc", legendre_parts, (columns,))
    filter_slice = lax.dynamic_slice_in_dim(spectral_filter, lon_index * chan_share, chan_share, 2)
    filter_real = filter_slice[0][:, None, :]
    filter_imag = filter_slice[1][:, None, :]
    real_part = coefficients[:, 0]
    imag_part = coefficients[:, 1]
    filtered = jnp.stack(
        [
            filter_real * real_part + filter_imag * imag_part,
            filter_real * imag_part - filter_imag * real_part,
        ],
        axis=1,
    )
    returned = dot_split("mls,lpmc->spmc", legendre_parts, split_bf16(filtered))
    returned = (returned * quad_weights[:, None, None, None]).astype(jnp.bfloat16)
    returned, ext_now = lax.optimization_barrier((returned, ext))
    portion = lax.all_to_all(returned, "lat", split_axis=0, concat_axis=2, tiled=True)
    disco_parts.append(disco_work(ext_now, 1, prep))
    portion, disco_parts = lax.optimization_barrier((portion, disco_parts))
    spectral_rows = None
    for p, parts in enumerate(trig_parts):
        term = dot_split("rkc,nk->rnc", (portion[:, p],), parts)
        spectral_rows = term if spectral_rows is None else spectral_rows + term
    spectral_rows = spectral_rows.astype(jnp.bfloat16)
    spectral_rows, ext_now = lax.optimization_barrier((spectral_rows, ext))
    spectral = lax.all_to_all(spectral_rows, "lon", split_axis=1, concat_axis=2, tiled=True)
    disco_parts.append(disco_work(ext_now, 2, prep))
    spectral, disco_parts = lax.optimization_barrier((spectral, disco_parts))
    return spectral, disco_parts


def filter_modes(coefficients, spectral_filter):
    filter_real = spectral_filter[0][:, None, :]
    filter_imag = spectral_filter[1][:, None, :]
    real_part = coefficients[:, 0]
    imag_part = coefficients[:, 1]
    return jnp.stack(
        [
            filter_real * real_part + filter_imag * imag_part,
            filter_real * imag_part - filter_imag * real_part,
        ],
        axis=1,
    )


def spectral_by_modes(
    masked, legendre, quad_weights, spectral_filter, trig_parts, live_rows, disco_work, prep, raw
):
    both = ("lat", "lon")
    lon_total = lax.axis_size("lon")
    mode_share = legendre.shape[0] // lon_total
    row_count, lon_count, channels = masked.shape
    share = row_count // lon_total
    body = raw.reshape(lon_total, share * lon_count, channels)
    edges = jnp.concatenate([raw[:, 0], raw[:, lon_count - 1]], axis=0)
    edges = jnp.broadcast_to(edges[None], (lon_total, 2 * row_count, channels))
    received = lax.all_to_all(
        jnp.concatenate([body, edges], axis=1), "lon", split_axis=0, concat_axis=0, tiled=True
    )
    own_legendre = lax.dynamic_slice_in_dim(
        legendre, lax.axis_index("lon") * mode_share, mode_share, 0
    )
    legendre_parts = split_bf16(own_legendre)
    received, legendre_parts, prep = lax.optimization_barrier((received, legendre_parts, prep))
    portion = received[:, : share * lon_count].reshape(lon_total, share, lon_count, channels)
    portion = portion.transpose(1, 0, 2, 3).reshape(share, lon_total * lon_count, channels)
    portion_live = lax.axis_index("lon") * share + jnp.arange(share) < live_rows
    portion = jnp.where(portion_live[:, None, None], portion, jnp.zeros_like(portion))
    edge_block = received[:, share * lon_count :]
    lon_index = lax.axis_index("lon")
    left = lax.dynamic_index_in_dim(edge_block, (lon_index - 1) % lon_total, 0, keepdims=False)
    right = lax.dynamic_index_in_dim(edge_block, (lon_index + 1) % lon_total, 0, keepdims=False)
    own = jnp.concatenate([left[row_count:, None], masked, right[:row_count, None]], axis=1)
    disco_parts = []
    spectra = jnp.stack(
        [dot_split("rnc,nk->rkc", (portion,), parts).astype(jnp.bfloat16) for parts in trig_parts],
        axis=1,
    )
    spectra, own = lax.optimization_barrier((spectra, own))
    ext = pad_lon(lat_extend(own, live_rows), lon_count)
    ext_now = ext
    columns = lax.all_to_all(spectra, both, split_axis=2, concat_axis=0, tiled=True)
    disco_parts.append(disco_work(ext_now, 0, prep))
    columns, disco_parts[0] = lax.optimization_barrier((columns, disco_parts[0]))
    coefficients = dot_split("mls,spmc->lpmc", legendre_parts, (columns,))
    filtered = filter_modes(coefficients, spectral_filter)
    returned = dot_split("mls,lpmc->spmc", legendre_parts, split_bf16(filtered))
    returned = (returned * quad_weights[:, None, None, None]).astype(jnp.bfloat16)
    returned, ext_now = lax.optimization_barrier((returned, ext))
    portion = lax.all_to_all(returned, both, split_axis=0, concat_axis=2, tiled=True)
    disco_parts.append(disco_work(ext_now, 1, prep))
    portion, disco_parts = lax.optimization_barrier((portion, disco_parts))
    spectral_rows = None
    for p, parts in enumerate(trig_parts):
        term = dot_split("rkc,nk->rnc", (portion[:, p],), parts)
        spectral_rows = term if spectral_rows is None else spectral_rows + term
    spectral_rows = spectral_rows.astype(jnp.bfloat16)
    spectral_rows, ext_now = lax.optimization_barrier((spectral_rows, ext))
    spectral = lax.all_to_all(spectral_rows, "lon", split_axis=1, concat_axis=0, tiled=True)
    disco_parts.append(disco_work(ext_now, 2, prep))
    spectral, disco_parts = lax.optimization_barrier((spectral, disco_parts))
    return spectral, disco_parts


def on_device(
    grad_output, band_rows, legendre, quad_weights, spectral_filter, disco_kernel, disco_weight
):
    row_count, lon_count, channels = grad_output.shape
    band_index = lax.axis_index("lat")
    band_total = lax.axis_size("lat")
    lon_total = lax.axis_size("lon")
    point_count = lon_count * lon_total
    mode_count = legendre.shape[0] * band_total
    slot_ids = jnp.arange(row_count, dtype=jnp.int32)
    live_rows = band_rows[band_index]
    live_slot = slot_ids < live_rows
    masked = jnp.where(live_slot[:, None, None], grad_output, jnp.zeros_like(grad_output))
    trig_parts = make_trig(mode_count, point_count)
    src_rows, coef = disco_tables(band_rows, disco_kernel, band_index, band_total, row_count)
    weight_flat = disco_weight.reshape(channels, -1)
    pieces = min(3, row_count)

    def disco_work(ext_now, piece, prep):
        return disco_piece(prep[0], prep[1], ext_now, prep[2], piece, pieces, lon_count)

    by_modes = legendre.shape[0] % lon_total == 0 and row_count % lon_total == 0
    path = spectral_by_modes if by_modes else spectral_by_channels
    spectral, disco_parts = path(
        masked,
        legendre,
        quad_weights,
        spectral_filter,
        trig_parts,
        live_rows,
        disco_work,
        (src_rows, coef, weight_flat),
        grad_output,
    )
    disco_full = jnp.concatenate(disco_parts, axis=0)
    disco_term = disco_full[:, :lon_count, :]
    summed = masked.astype(jnp.float32) + disco_term + spectral.astype(jnp.float32)
    return jnp.where(live_slot[:, None, None], summed, 0.0).astype(jnp.bfloat16)


def solution(mesh):
    placed = (P("lat", "lon", None), P(), P("lat", None, None), P(), P(), P(), P())
    return jax.shard_map(
        on_device, mesh=mesh, in_specs=placed, out_specs=P("lat", "lon", None), check_vma=False
    )
```

```python
import functools

import ml_dtypes
import numpy as np
import jax
import jax.numpy as jnp
from jax import lax
from jax.experimental import pallas as pl
from jax.experimental.pallas import tpu as pltpu
from jax.sharding import PartitionSpec as P


def make_trig(mode_count, point_count):
    step = 16 if point_count % 16 == 0 else 1
    coarse = np.arange(point_count // step)[:, None] * step
    fine = np.arange(step)[:, None]
    wavenumber = np.arange(mode_count)[None, :]
    coarse_angle = (wavenumber * coarse % point_count) * (2.0 * np.pi / point_count)
    fine_angle = (wavenumber * fine % point_count) * (2.0 * np.pi / point_count)
    scale = point_count ** (-0.5)
    coarse_cos = jnp.asarray((np.cos(coarse_angle) * scale).astype(np.float32))[:, None, :]
    coarse_sin = jnp.asarray((np.sin(coarse_angle) * scale).astype(np.float32))[:, None, :]
    fine_cos = jnp.asarray(np.cos(fine_angle).astype(np.float32))[None, :, :]
    fine_sin = jnp.asarray(np.sin(fine_angle).astype(np.float32))[None, :, :]
    cosine = coarse_cos * fine_cos - coarse_sin * fine_sin
    minus_sine = -(coarse_sin * fine_cos + coarse_cos * fine_sin)
    return tuple(
        split_bf16(part.reshape(point_count, mode_count)) for part in (cosine, minus_sine)
    )


def split_bf16(values):
    rounded = lax.reduce_precision(values, exponent_bits=8, mantissa_bits=7)
    return rounded.astype(jnp.bfloat16), (values - rounded).astype(jnp.bfloat16)


def dot_split(spec, left_parts, right_parts):
    total = None
    for lp in left_parts:
        for rp in right_parts:
            if lp is not left_parts[0] and rp is not right_parts[0]:
                continue
            term = jnp.einsum(spec, lp, rp, preferred_element_type=jnp.float32)
            total = term if total is None else total + term
    return total


CHUNK = 64


def round_up(value, step):
    return -(-value // step) * step


def disco_body(first, last, src_ref, coef_ref, ext_ref, w_ref, out_ref, mix_ref):
    kinds = w_ref.shape[1] // w_ref.shape[0]
    channels = w_ref.shape[0]
    span = last - first + 2
    below = ext_ref.shape[0] - 1
    for r in range(span):
        mix_ref[r] = jnp.dot(ext_ref[first + r], w_ref[...], preferred_element_type=jnp.float32)
    mix_ref[span] = jnp.dot(ext_ref[below], w_ref[...], preferred_element_type=jnp.float32)

    def slot_step(s, carry):
        for c0 in range(0, out_ref.shape[1], CHUNK):
            acc = jnp.zeros((CHUNK, channels), jnp.float32)
            for a_i in range(3):
                source = src_ref[(first + s) * 3 + a_i]
                row = jnp.where(source == below, span, source - first)
                for b_i in range(3):
                    for k in range(kinds):
                        coef = coef_ref[(((first + s) * 3 + a_i) * 3 + b_i) * kinds + k]
                        acc = acc + coef * mix_ref[
                            row, pl.ds(c0 + 2 - b_i, CHUNK), pl.ds(k * channels, channels)
                        ]
            out_ref[s, pl.ds(c0, CHUNK), :] = acc
        return carry

    lax.fori_loop(0, last - first, slot_step, 0)


def disco_piece(src_rows, coef, ext, weight_flat, piece, pieces, lon_count):
    slot_total = ext.shape[0] - 2
    bounds = [i * slot_total // pieces for i in range(pieces + 1)]
    if pieces == 3 and slot_total >= 8:
        bounds = [0, slot_total // 8, slot_total // 2, slot_total]
    first, last = bounds[piece], bounds[piece + 1]
    lon_pad, channels = ext.shape[1:]
    out_rows = round_up(lon_count, CHUNK)
    smem = pltpu.MemorySpace.SMEM if hasattr(pltpu, "MemorySpace") else pltpu.SMEM
    return pl.pallas_call(
        functools.partial(disco_body, first, last),
        out_shape=jax.ShapeDtypeStruct((last - first, out_rows, channels), jnp.float32),
        in_specs=[
            pl.BlockSpec(memory_space=smem),
            pl.BlockSpec(memory_space=smem),
            pl.BlockSpec(memory_space=pltpu.VMEM),
            pl.BlockSpec(memory_space=pltpu.VMEM),
        ],
        out_specs=pl.BlockSpec(memory_space=pltpu.VMEM),
        scratch_shapes=[pltpu.VMEM((last - first + 3, lon_pad, weight_flat.shape[1]), jnp.float32)],
    )(src_rows, coef, ext, weight_flat)


def disco_tables(band_rows, disco_kernel, band_index, band_total, row_count):
    slot_ids = jnp.arange(row_count, dtype=jnp.int32)
    live_rows = band_rows[band_index]
    has_next = slot_ids + 1 < live_rows
    prev_band = jnp.maximum(band_index - 1, 0)
    next_band = jnp.minimum(band_index + 1, band_total - 1)
    base = band_index * row_count
    up_src = jnp.where(slot_ids == 0, 0, slot_ids)
    down_src = jnp.where(has_next, slot_ids + 2, row_count + 1)
    src = jnp.stack([up_src, slot_ids + 1, down_src], axis=1)
    up_row = jnp.where(
        slot_ids == 0, prev_band * row_count + band_rows[prev_band] - 1, base + slot_ids - 1
    )
    down_row = jnp.where(has_next, base + slot_ids + 1, next_band * row_count)
    kernel_row = jnp.stack([up_row, base + slot_ids, down_row], axis=1)
    kernel_row = jnp.clip(kernel_row, 0, disco_kernel.shape[0] - 1)
    up_ok = (slot_ids > 0) | (band_index > 0)
    down_ok = has_next | (band_index < band_total - 1)
    valid = jnp.stack([up_ok, jnp.ones_like(up_ok), down_ok], axis=1)
    gathered = disco_kernel[kernel_row]
    gathered = gathered.reshape(row_count, 3, 3, 3, disco_kernel.shape[2])
    coef = jnp.stack([gathered[:, 0, 2], gathered[:, 1, 1], gathered[:, 2, 0]], axis=1)
    coef = jnp.where(valid[:, :, None, None], coef, 0.0)
    return src.reshape(-1).astype(jnp.int32), coef.reshape(-1).astype(jnp.float32)


def lat_extend(block, live_rows):
    lat_total = lax.axis_size("lat")
    lat_up = [(i, (i + 1) % lat_total) for i in range(lat_total)]
    lat_down = [(j, i) for i, j in lat_up]
    last_row = lax.dynamic_slice_in_dim(block, live_rows - 1, 1, 0)
    from_above = lax.ppermute(last_row, "lat", lat_up)
    from_below = lax.ppermute(block[0:1], "lat", lat_down)
    return jnp.concatenate([from_above, block, from_below], axis=0)


def pad_lon(rows, lon_count):
    lon_pad = round_up(round_up(lon_count, CHUNK) + 2, 16)
    pad = jnp.zeros((rows.shape[0], lon_pad - rows.shape[1], rows.shape[2]), rows.dtype)
    return jnp.concatenate([rows, pad], axis=1)


def halo_extend(masked, live_rows):
    row_count, lon_count, channels = masked.shape
    lat_total = lax.axis_size("lat")
    lon_total = lax.axis_size("lon")
    lat_up = [(i, (i + 1) % lat_total) for i in range(lat_total)]
    lat_down = [(j, i) for i, j in lat_up]
    lon_up = [(i, (i + 1) % lon_total) for i in range(lon_total)]
    lon_down = [(j, i) for i, j in lon_up]
    last_row = lax.dynamic_slice_in_dim(masked, live_rows - 1, 1, 0)
    from_above = lax.ppermute(last_row, "lat", lat_up)
    from_below = lax.ppermute(masked[0:1], "lat", lat_down)
    rows = jnp.concatenate([from_above, masked, from_below], axis=0)
    from_left = lax.ppermute(rows[:, lon_count - 1 : lon_count], "lon", lon_up)
    from_right = lax.ppermute(rows[:, 0:1], "lon", lon_down)
    lon_pad = round_up(round_up(lon_count, CHUNK) + 2, 16)
    pad = jnp.zeros((row_count + 2, lon_pad - lon_count - 2, channels), masked.dtype)
    return jnp.concatenate([from_left, rows, from_right, pad], axis=1)


def spectral_by_channels(
    masked, legendre, quad_weights, spectral_filter, trig_parts, live_rows, disco_work, prep, raw
):
    ext = halo_extend(masked, live_rows)
    channels = masked.shape[2]
    lon_index = lax.axis_index("lon")
    chan_share = channels // lax.axis_size("lon")
    disco_parts = []
    portion = lax.all_to_all(masked, "lon", split_axis=2, concat_axis=1, tiled=True)
    spectra = jnp.stack(
        [dot_split("rnc,nk->rkc", (portion,), parts).astype(jnp.bfloat16) for parts in trig_parts],
        axis=1,
    )
    spectra, ext_now = lax.optimization_barrier((spectra, ext))
    columns = lax.all_to_all(spectra, "lat", split_axis=2, concat_axis=0, tiled=True)
    disco_parts.append(disco_work(ext_now, 0, prep))
    columns, disco_parts[0] = lax.optimization_barrier((columns, disco_parts[0]))
    legendre_parts = split_bf16(legendre)
    coefficients = dot_split("mls,spmc->lpmc", legendre_parts, (columns,))
    filter_slice = lax.dynamic_slice_in_dim(spectral_filter, lon_index * chan_share, chan_share, 2)
    filter_real = filter_slice[0][:, None, :]
    filter_imag = filter_slice[1][:, None, :]
    real_part = coefficients[:, 0]
    imag_part = coefficients[:, 1]
    filtered = jnp.stack(
        [
            filter_real * real_part + filter_imag * imag_part,
            filter_real * imag_part - filter_imag * real_part,
        ],
        axis=1,
    )
    returned = dot_split("mls,lpmc->spmc", legendre_parts, split_bf16(filtered))
    returned = (returned * quad_weights[:, None, None, None]).astype(jnp.bfloat16)
    returned, ext_now = lax.optimization_barrier((returned, ext))
    portion = lax.all_to_all(returned, "lat", split_axis=0, concat_axis=2, tiled=True)
    disco_parts.append(disco_work(ext_now, 1, prep))
    portion, disco_parts = lax.optimization_barrier((portion, disco_parts))
    spectral_rows = None
    for p, parts in enumerate(trig_parts):
        term = dot_split("rkc,nk->rnc", (portion[:, p],), parts)
        spectral_rows = term if spectral_rows is None else spectral_rows + term
    spectral_rows = spectral_rows.astype(jnp.bfloat16)
    spectral_rows, ext_now = lax.optimization_barrier((spectral_rows, ext))
    spectral = lax.all_to_all(spectral_rows, "lon", split_axis=1, concat_axis=2, tiled=True)
    disco_parts.append(disco_work(ext_now, 2, prep))
    spectral, disco_parts = lax.optimization_barrier((spectral, disco_parts))
    return spectral, disco_parts, masked


def filter_modes(coefficients, spectral_filter):
    filter_real = spectral_filter[0][:, None, :]
    filter_imag = spectral_filter[1][:, None, :]
    real_part = coefficients[:, 0]
    imag_part = coefficients[:, 1]
    return jnp.stack(
        [
            filter_real * real_part + filter_imag * imag_part,
            filter_real * imag_part - filter_imag * real_part,
        ],
        axis=1,
    )


def spectral_by_modes(
    masked, legendre, quad_weights, spectral_filter, trig_parts, live_rows, disco_work, prep, raw
):
    both = ("lat", "lon")
    lon_total = lax.axis_size("lon")
    mode_share = legendre.shape[0] // lon_total
    row_count, lon_count, channels = masked.shape
    share = row_count // lon_total
    body = raw.reshape(lon_total, share * lon_count, channels)
    edges = jnp.concatenate([raw[:, 0], raw[:, lon_count - 1]], axis=0)
    edges = jnp.broadcast_to(edges[None], (lon_total, 2 * row_count, channels))
    send, raw = lax.optimization_barrier((jnp.concatenate([body, edges], axis=1), raw))
    received = lax.all_to_all(send, "lon", split_axis=0, concat_axis=0, tiled=True)
    slot_live = jnp.arange(row_count) < live_rows
    masked = jnp.where(slot_live[:, None, None], raw, jnp.zeros_like(raw))
    own_legendre = lax.dynamic_slice_in_dim(
        legendre, lax.axis_index("lon") * mode_share, mode_share, 0
    )
    legendre_parts = split_bf16(own_legendre)
    received, legendre_parts, prep = lax.optimization_barrier((received, legendre_parts, prep))
    portion = received[:, : share * lon_count].reshape(lon_total, share, lon_count, channels)
    portion = portion.transpose(1, 0, 2, 3).reshape(share, lon_total * lon_count, channels)
    portion_live = lax.axis_index("lon") * share + jnp.arange(share) < live_rows
    portion = jnp.where(portion_live[:, None, None], portion, jnp.zeros_like(portion))
    edge_block = received[:, share * lon_count :]
    lon_index = lax.axis_index("lon")
    left = lax.dynamic_index_in_dim(edge_block, (lon_index - 1) % lon_total, 0, keepdims=False)
    right = lax.dynamic_index_in_dim(edge_block, (lon_index + 1) % lon_total, 0, keepdims=False)
    own = jnp.concatenate([left[row_count:, None], masked, right[:row_count, None]], axis=1)
    disco_parts = []
    spectra = jnp.stack(
        [dot_split("rnc,nk->rkc", (portion,), parts).astype(jnp.bfloat16) for parts in trig_parts],
        axis=1,
    )
    spectra, own = lax.optimization_barrier((spectra, own))
    ext = pad_lon(lat_extend(own, live_rows), lon_count)
    ext_now = ext
    columns = lax.all_to_all(spectra, both, split_axis=2, concat_axis=0, tiled=True)
    disco_parts.append(disco_work(ext_now, 0, prep))
    columns, disco_parts[0] = lax.optimization_barrier((columns, disco_parts[0]))
    coefficients = dot_split("mls,spmc->lpmc", legendre_parts, (columns,))
    filtered = filter_modes(coefficients, spectral_filter)
    returned = dot_split("mls,lpmc->spmc", legendre_parts, split_bf16(filtered))
    returned = (returned * quad_weights[:, None, None, None]).astype(jnp.bfloat16)
    returned, ext_now = lax.optimization_barrier((returned, ext))
    portion = lax.all_to_all(returned, both, split_axis=0, concat_axis=2, tiled=True)
    disco_parts.append(disco_work(ext_now, 1, prep))
    portion, disco_parts = lax.optimization_barrier((portion, disco_parts))
    spectral_rows = None
    for p, parts in enumerate(trig_parts):
        term = dot_split("rkc,nk->rnc", (portion[:, p],), parts)
        spectral_rows = term if spectral_rows is None else spectral_rows + term
    spectral_rows = spectral_rows.astype(jnp.bfloat16)
    spectral_rows, ext_now = lax.optimization_barrier((spectral_rows, ext))
    spectral = lax.all_to_all(spectral_rows, "lon", split_axis=1, concat_axis=0, tiled=True)
    disco_parts.append(disco_work(ext_now, 2, prep))
    spectral, disco_parts = lax.optimization_barrier((spectral, disco_parts))
    return spectral, disco_parts, masked


def on_device(
    grad_output, band_rows, legendre, quad_weights, spectral_filter, disco_kernel, disco_weight
):
    row_count, lon_count, channels = grad_output.shape
    band_index = lax.axis_index("lat")
    band_total = lax.axis_size("lat")
    lon_total = lax.axis_size("lon")
    point_count = lon_count * lon_total
    mode_count = legendre.shape[0] * band_total
    slot_ids = jnp.arange(row_count, dtype=jnp.int32)
    live_rows = band_rows[band_index]
    live_slot = slot_ids < live_rows
    masked = jnp.where(live_slot[:, None, None], grad_output, jnp.zeros_like(grad_output))
    trig_parts = make_trig(mode_count, point_count)
    src_rows, coef = disco_tables(band_rows, disco_kernel, band_index, band_total, row_count)
    weight_flat = disco_weight.reshape(channels, -1)
    pieces = min(3, row_count)

    def disco_work(ext_now, piece, prep):
        return disco_piece(prep[0], prep[1], ext_now, prep[2], piece, pieces, lon_count)

    by_modes = legendre.shape[0] % lon_total == 0 and row_count % lon_total == 0
    path = spectral_by_modes if by_modes else spectral_by_channels
    spectral, disco_parts, masked = path(
        masked,
        legendre,
        quad_weights,
        spectral_filter,
        trig_parts,
        live_rows,
        disco_work,
        (src_rows, coef, weight_flat),
        grad_output,
    )
    disco_full = jnp.concatenate(disco_parts, axis=0)
    disco_term = disco_full[:, :lon_count, :]
    summed = masked.astype(jnp.float32) + disco_term + spectral.astype(jnp.float32)
    return jnp.where(live_slot[:, None, None], summed, 0.0).astype(jnp.bfloat16)


def solution(mesh):
    placed = (P("lat", "lon", None), P(), P("lat", None, None), P(), P(), P(), P())
    return jax.shard_map(
        on_device, mesh=mesh, in_specs=placed, out_specs=P("lat", "lon", None), check_vma=False
    )
```

```python
import functools

import ml_dtypes
import numpy as np
import jax
import jax.numpy as jnp
from jax import lax
from jax.experimental import pallas as pl
from jax.experimental.pallas import tpu as pltpu
from jax.sharding import PartitionSpec as P


def make_trig(mode_count, point_count):
    step = 16 if point_count % 16 == 0 else 1
    coarse = np.arange(point_count // step)[:, None] * step
    fine = np.arange(step)[:, None]
    wavenumber = np.arange(mode_count)[None, :]
    coarse_angle = (wavenumber * coarse % point_count) * (2.0 * np.pi / point_count)
    fine_angle = (wavenumber * fine % point_count) * (2.0 * np.pi / point_count)
    scale = point_count ** (-0.5)
    coarse_cos = jnp.asarray((np.cos(coarse_angle) * scale).astype(np.float32))[:, None, :]
    coarse_sin = jnp.asarray((np.sin(coarse_angle) * scale).astype(np.float32))[:, None, :]
    fine_cos = jnp.asarray(np.cos(fine_angle).astype(np.float32))[None, :, :]
    fine_sin = jnp.asarray(np.sin(fine_angle).astype(np.float32))[None, :, :]
    cosine = coarse_cos * fine_cos - coarse_sin * fine_sin
    minus_sine = -(coarse_sin * fine_cos + coarse_cos * fine_sin)
    return tuple(
        split_bf16(part.reshape(point_count, mode_count)) for part in (cosine, minus_sine)
    )


def split_bf16(values):
    rounded = lax.reduce_precision(values, exponent_bits=8, mantissa_bits=7)
    return rounded.astype(jnp.bfloat16), (values - rounded).astype(jnp.bfloat16)


def dot_split(spec, left_parts, right_parts):
    total = None
    for lp in left_parts:
        for rp in right_parts:
            if lp is not left_parts[0] and rp is not right_parts[0]:
                continue
            term = jnp.einsum(spec, lp, rp, preferred_element_type=jnp.float32)
            total = term if total is None else total + term
    return total


CHUNK = 64


def round_up(value, step):
    return -(-value // step) * step


def disco_body(first, last, src_ref, coef_ref, ext_ref, w_ref, out_ref, mix_ref):
    kinds = w_ref.shape[1] // w_ref.shape[0]
    channels = w_ref.shape[0]
    span = last - first + 2
    below = ext_ref.shape[0] - 1
    for r in range(span):
        mix_ref[r] = jnp.dot(ext_ref[first + r], w_ref[...], preferred_element_type=jnp.float32)
    mix_ref[span] = jnp.dot(ext_ref[below], w_ref[...], preferred_element_type=jnp.float32)

    def slot_step(s, carry):
        for c0 in range(0, out_ref.shape[1], CHUNK):
            acc = jnp.zeros((CHUNK, channels), jnp.float32)
            for a_i in range(3):
                source = src_ref[(first + s) * 3 + a_i]
                row = jnp.where(source == below, span, source - first)
                for b_i in range(3):
                    for k in range(kinds):
                        coef = coef_ref[(((first + s) * 3 + a_i) * 3 + b_i) * kinds + k]
                        acc = acc + coef * mix_ref[
                            row, pl.ds(c0 + 2 - b_i, CHUNK), pl.ds(k * channels, channels)
                        ]
            out_ref[s, pl.ds(c0, CHUNK), :] = acc
        return carry

    lax.fori_loop(0, last - first, slot_step, 0)


def disco_piece(src_rows, coef, ext, weight_flat, piece, pieces, lon_count):
    slot_total = ext.shape[0] - 2
    bounds = [i * slot_total // pieces for i in range(pieces + 1)]
    if pieces == 3 and slot_total >= 8:
        bounds = [0, slot_total // 8, slot_total // 2, slot_total]
    first, last = bounds[piece], bounds[piece + 1]
    lon_pad, channels = ext.shape[1:]
    out_rows = round_up(lon_count, CHUNK)
    smem = pltpu.MemorySpace.SMEM if hasattr(pltpu, "MemorySpace") else pltpu.SMEM
    return pl.pallas_call(
        functools.partial(disco_body, first, last),
        out_shape=jax.ShapeDtypeStruct((last - first, out_rows, channels), jnp.float32),
        in_specs=[
            pl.BlockSpec(memory_space=smem),
            pl.BlockSpec(memory_space=smem),
            pl.BlockSpec(memory_space=pltpu.VMEM),
            pl.BlockSpec(memory_space=pltpu.VMEM),
        ],
        out_specs=pl.BlockSpec(memory_space=pltpu.VMEM),
        scratch_shapes=[pltpu.VMEM((last - first + 3, lon_pad, weight_flat.shape[1]), jnp.float32)],
    )(src_rows, coef, ext, weight_flat)


def disco_tables(band_rows, disco_kernel, band_index, band_total, row_count):
    slot_ids = jnp.arange(row_count, dtype=jnp.int32)
    live_rows = band_rows[band_index]
    has_next = slot_ids + 1 < live_rows
    prev_band = jnp.maximum(band_index - 1, 0)
    next_band = jnp.minimum(band_index + 1, band_total - 1)
    base = band_index * row_count
    up_src = jnp.where(slot_ids == 0, 0, slot_ids)
    down_src = jnp.where(has_next, slot_ids + 2, row_count + 1)
    src = jnp.stack([up_src, slot_ids + 1, down_src], axis=1)
    up_row = jnp.where(
        slot_ids == 0, prev_band * row_count + band_rows[prev_band] - 1, base + slot_ids - 1
    )
    down_row = jnp.where(has_next, base + slot_ids + 1, next_band * row_count)
    kernel_row = jnp.stack([up_row, base + slot_ids, down_row], axis=1)
    kernel_row = jnp.clip(kernel_row, 0, disco_kernel.shape[0] - 1)
    up_ok = (slot_ids > 0) | (band_index > 0)
    down_ok = has_next | (band_index < band_total - 1)
    valid = jnp.stack([up_ok, jnp.ones_like(up_ok), down_ok], axis=1)
    gathered = disco_kernel[kernel_row]
    gathered = gathered.reshape(row_count, 3, 3, 3, disco_kernel.shape[2])
    coef = jnp.stack([gathered[:, 0, 2], gathered[:, 1, 1], gathered[:, 2, 0]], axis=1)
    coef = jnp.where(valid[:, :, None, None], coef, 0.0)
    return src.reshape(-1).astype(jnp.int32), coef.reshape(-1).astype(jnp.float32)


def lat_extend(block, live_rows):
    lat_total = lax.axis_size("lat")
    lat_up = [(i, (i + 1) % lat_total) for i in range(lat_total)]
    lat_down = [(j, i) for i, j in lat_up]
    last_row = lax.dynamic_slice_in_dim(block, live_rows - 1, 1, 0)
    from_above = lax.ppermute(last_row, "lat", lat_up)
    from_below = lax.ppermute(block[0:1], "lat", lat_down)
    return jnp.concatenate([from_above, block, from_below], axis=0)


def pad_lon(rows, lon_count):
    lon_pad = round_up(round_up(lon_count, CHUNK) + 2, 16)
    pad = jnp.zeros((rows.shape[0], lon_pad - rows.shape[1], rows.shape[2]), rows.dtype)
    return jnp.concatenate([rows, pad], axis=1)


def halo_extend(masked, live_rows):
    row_count, lon_count, channels = masked.shape
    lat_total = lax.axis_size("lat")
    lon_total = lax.axis_size("lon")
    lat_up = [(i, (i + 1) % lat_total) for i in range(lat_total)]
    lat_down = [(j, i) for i, j in lat_up]
    lon_up = [(i, (i + 1) % lon_total) for i in range(lon_total)]
    lon_down = [(j, i) for i, j in lon_up]
    last_row = lax.dynamic_slice_in_dim(masked, live_rows - 1, 1, 0)
    from_above = lax.ppermute(last_row, "lat", lat_up)
    from_below = lax.ppermute(masked[0:1], "lat", lat_down)
    rows = jnp.concatenate([from_above, masked, from_below], axis=0)
    from_left = lax.ppermute(rows[:, lon_count - 1 : lon_count], "lon", lon_up)
    from_right = lax.ppermute(rows[:, 0:1], "lon", lon_down)
    lon_pad = round_up(round_up(lon_count, CHUNK) + 2, 16)
    pad = jnp.zeros((row_count + 2, lon_pad - lon_count - 2, channels), masked.dtype)
    return jnp.concatenate([from_left, rows, from_right, pad], axis=1)


def spectral_by_channels(
    masked, legendre, quad_weights, spectral_filter, trig_parts, live_rows, disco_work, prep, raw
):
    ext = halo_extend(masked, live_rows)
    channels = masked.shape[2]
    lon_index = lax.axis_index("lon")
    chan_share = channels // lax.axis_size("lon")
    disco_parts = []
    portion = lax.all_to_all(masked, "lon", split_axis=2, concat_axis=1, tiled=True)
    spectra = jnp.stack(
        [dot_split("rnc,nk->rkc", (portion,), parts).astype(jnp.bfloat16) for parts in trig_parts],
        axis=1,
    )
    spectra, ext_now = lax.optimization_barrier((spectra, ext))
    columns = lax.all_to_all(spectra, "lat", split_axis=2, concat_axis=0, tiled=True)
    disco_parts.append(disco_work(ext_now, 0, prep))
    columns, disco_parts[0] = lax.optimization_barrier((columns, disco_parts[0]))
    legendre_parts = split_bf16(legendre)
    coefficients = dot_split("mls,spmc->lpmc", legendre_parts, (columns,))
    filter_slice = lax.dynamic_slice_in_dim(spectral_filter, lon_index * chan_share, chan_share, 2)
    filter_real = filter_slice[0][:, None, :]
    filter_imag = filter_slice[1][:, None, :]
    real_part = coefficients[:, 0]
    imag_part = coefficients[:, 1]
    filtered = jnp.stack(
        [
            filter_real * real_part + filter_imag * imag_part,
            filter_real * imag_part - filter_imag * real_part,
        ],
        axis=1,
    )
    returned = dot_split("mls,lpmc->spmc", legendre_parts, split_bf16(filtered))
    returned = (returned * quad_weights[:, None, None, None]).astype(jnp.bfloat16)
    returned, ext_now = lax.optimization_barrier((returned, ext))
    portion = lax.all_to_all(returned, "lat", split_axis=0, concat_axis=2, tiled=True)
    disco_parts.append(disco_work(ext_now, 1, prep))
    portion, disco_parts = lax.optimization_barrier((portion, disco_parts))
    spectral_rows = None
    for p, parts in enumerate(trig_parts):
        term = dot_split("rkc,nk->rnc", (portion[:, p],), parts)
        spectral_rows = term if spectral_rows is None else spectral_rows + term
    spectral_rows = spectral_rows.astype(jnp.bfloat16)
    spectral_rows, ext_now = lax.optimization_barrier((spectral_rows, ext))
    spectral = lax.all_to_all(spectral_rows, "lon", split_axis=1, concat_axis=2, tiled=True)
    disco_parts.append(disco_work(ext_now, 2, prep))
    spectral, disco_parts = lax.optimization_barrier((spectral, disco_parts))
    return spectral, disco_parts


def filter_modes(coefficients, spectral_filter):
    filter_real = spectral_filter[0][:, None, :]
    filter_imag = spectral_filter[1][:, None, :]
    real_part = coefficients[:, 0]
    imag_part = coefficients[:, 1]
    return jnp.stack(
        [
            filter_real * real_part + filter_imag * imag_part,
            filter_real * imag_part - filter_imag * real_part,
        ],
        axis=1,
    )


def spectral_by_modes(
    masked, legendre, quad_weights, spectral_filter, trig_parts, live_rows, disco_work, prep, raw
):
    both = ("lat", "lon")
    lon_total = lax.axis_size("lon")
    mode_share = legendre.shape[0] // lon_total
    row_count, lon_count, channels = masked.shape
    share = row_count // lon_total
    body = raw.reshape(lon_total, share * lon_count, channels)
    edges = jnp.concatenate([raw[:, 0], raw[:, lon_count - 1]], axis=0)
    edges = jnp.broadcast_to(edges[None], (lon_total, 2 * row_count, channels))
    received = lax.all_to_all(
        jnp.concatenate([body, edges], axis=1), "lon", split_axis=0, concat_axis=0, tiled=True
    )
    own_legendre = lax.dynamic_slice_in_dim(
        legendre, lax.axis_index("lon") * mode_share, mode_share, 0
    )
    legendre_parts = split_bf16(own_legendre)
    received, legendre_parts, prep = lax.optimization_barrier((received, legendre_parts, prep))
    portion = received[:, : share * lon_count].reshape(lon_total, share, lon_count, channels)
    portion = portion.transpose(1, 0, 2, 3).reshape(share, lon_total * lon_count, channels)
    portion_live = lax.axis_index("lon") * share + jnp.arange(share) < live_rows
    portion = jnp.where(portion_live[:, None, None], portion, jnp.zeros_like(portion))
    edge_block = received[:, share * lon_count :]
    lon_index = lax.axis_index("lon")
    left = lax.dynamic_index_in_dim(edge_block, (lon_index - 1) % lon_total, 0, keepdims=False)
    right = lax.dynamic_index_in_dim(edge_block, (lon_index + 1) % lon_total, 0, keepdims=False)
    own = jnp.concatenate([left[row_count:, None], masked, right[:row_count, None]], axis=1)
    disco_parts = []
    spectra = jnp.stack(
        [dot_split("rnc,nk->rkc", (portion,), parts).astype(jnp.bfloat16) for parts in trig_parts],
        axis=1,
    )
    spectra, own = lax.optimization_barrier((spectra, own))
    ext = pad_lon(lat_extend(own, live_rows), lon_count)
    ext_now = ext
    columns = lax.all_to_all(spectra, both, split_axis=2, concat_axis=0, tiled=True)
    coefficients = dot_split("mls,spmc->lpmc", legendre_parts, (columns,))
    filtered = filter_modes(coefficients, spectral_filter)
    returned = dot_split("mls,lpmc->spmc", legendre_parts, split_bf16(filtered))
    returned = (returned * quad_weights[:, None, None, None]).astype(jnp.bfloat16)
    returned, ext_now = lax.optimization_barrier((returned, ext))
    portion = lax.all_to_all(returned, both, split_axis=0, concat_axis=2, tiled=True)
    disco_parts.append(disco_work(ext_now, 0, prep))
    portion, disco_parts = lax.optimization_barrier((portion, disco_parts))
    spectral_rows = None
    for p, parts in enumerate(trig_parts):
        term = dot_split("rkc,nk->rnc", (portion[:, p],), parts)
        spectral_rows = term if spectral_rows is None else spectral_rows + term
    spectral_rows = spectral_rows.astype(jnp.bfloat16)
    spectral_rows, ext_now = lax.optimization_barrier((spectral_rows, ext))
    spectral = lax.all_to_all(spectral_rows, "lon", split_axis=1, concat_axis=0, tiled=True)
    disco_parts.append(disco_work(ext_now, 1, prep))
    spectral, disco_parts = lax.optimization_barrier((spectral, disco_parts))
    return spectral, disco_parts


def on_device(
    grad_output, band_rows, legendre, quad_weights, spectral_filter, disco_kernel, disco_weight
):
    row_count, lon_count, channels = grad_output.shape
    band_index = lax.axis_index("lat")
    band_total = lax.axis_size("lat")
    lon_total = lax.axis_size("lon")
    point_count = lon_count * lon_total
    mode_count = legendre.shape[0] * band_total
    slot_ids = jnp.arange(row_count, dtype=jnp.int32)
    live_rows = band_rows[band_index]
    live_slot = slot_ids < live_rows
    masked = jnp.where(live_slot[:, None, None], grad_output, jnp.zeros_like(grad_output))
    trig_parts = make_trig(mode_count, point_count)
    src_rows, coef = disco_tables(band_rows, disco_kernel, band_index, band_total, row_count)
    weight_flat = disco_weight.reshape(channels, -1)
    by_modes = legendre.shape[0] % lon_total == 0 and row_count % lon_total == 0
    pieces = min(2 if by_modes else 3, row_count)

    def disco_work(ext_now, piece, prep):
        return disco_piece(prep[0], prep[1], ext_now, prep[2], piece, pieces, lon_count)

    path = spectral_by_modes if by_modes else spectral_by_channels
    spectral, disco_parts = path(
        masked,
        legendre,
        quad_weights,
        spectral_filter,
        trig_parts,
        live_rows,
        disco_work,
        (src_rows, coef, weight_flat),
        grad_output,
    )
    disco_full = jnp.concatenate(disco_parts, axis=0)
    disco_term = disco_full[:, :lon_count, :]
    summed = masked.astype(jnp.float32) + disco_term + spectral.astype(jnp.float32)
    return jnp.where(live_slot[:, None, None], summed, 0.0).astype(jnp.bfloat16)


def solution(mesh):
    placed = (P("lat", "lon", None), P(), P("lat", None, None), P(), P(), P(), P())
    return jax.shard_map(
        on_device, mesh=mesh, in_specs=placed, out_specs=P("lat", "lon", None), check_vma=False
    )
```

```python
import functools

import ml_dtypes
import numpy as np
import jax
import jax.numpy as jnp
from jax import lax
from jax.experimental import pallas as pl
from jax.experimental.pallas import tpu as pltpu
from jax.sharding import PartitionSpec as P


def make_trig(mode_count, point_count):
    step = 16 if point_count % 16 == 0 else 1
    coarse = np.arange(point_count // step)[:, None] * step
    fine = np.arange(step)[:, None]
    wavenumber = np.arange(mode_count)[None, :]
    coarse_angle = (wavenumber * coarse % point_count) * (2.0 * np.pi / point_count)
    fine_angle = (wavenumber * fine % point_count) * (2.0 * np.pi / point_count)
    scale = point_count ** (-0.5)
    coarse_cos = jnp.asarray((np.cos(coarse_angle) * scale).astype(np.float32))[:, None, :]
    coarse_sin = jnp.asarray((np.sin(coarse_angle) * scale).astype(np.float32))[:, None, :]
    fine_cos = jnp.asarray(np.cos(fine_angle).astype(np.float32))[None, :, :]
    fine_sin = jnp.asarray(np.sin(fine_angle).astype(np.float32))[None, :, :]
    cosine = coarse_cos * fine_cos - coarse_sin * fine_sin
    minus_sine = -(coarse_sin * fine_cos + coarse_cos * fine_sin)
    return tuple(
        split_bf16(part.reshape(point_count, mode_count)) for part in (cosine, minus_sine)
    )


def split_bf16(values):
    rounded = lax.reduce_precision(values, exponent_bits=8, mantissa_bits=7)
    return rounded.astype(jnp.bfloat16), (values - rounded).astype(jnp.bfloat16)


def dot_split(spec, left_parts, right_parts):
    total = None
    for lp in left_parts:
        for rp in right_parts:
            if lp is not left_parts[0] and rp is not right_parts[0]:
                continue
            term = jnp.einsum(spec, lp, rp, preferred_element_type=jnp.float32)
            total = term if total is None else total + term
    return total


CHUNK = 64


def round_up(value, step):
    return -(-value // step) * step


def disco_body(first, last, src_ref, coef_ref, ext_ref, w_ref, out_ref, mix_ref):
    kinds = w_ref.shape[1] // w_ref.shape[0]
    channels = w_ref.shape[0]
    span = last - first + 2
    below = ext_ref.shape[0] - 1
    for r in range(span):
        mix_ref[r] = jnp.dot(ext_ref[first + r], w_ref[...], preferred_element_type=jnp.float32)
    mix_ref[span] = jnp.dot(ext_ref[below], w_ref[...], preferred_element_type=jnp.float32)

    def slot_step(s, carry):
        for c0 in range(0, out_ref.shape[1], CHUNK):
            acc = jnp.zeros((CHUNK, channels), jnp.float32)
            for a_i in range(3):
                source = src_ref[(first + s) * 3 + a_i]
                row = jnp.where(source == below, span, source - first)
                for b_i in range(3):
                    for k in range(kinds):
                        coef = coef_ref[(((first + s) * 3 + a_i) * 3 + b_i) * kinds + k]
                        acc = acc + coef * mix_ref[
                            row, pl.ds(c0 + 2 - b_i, CHUNK), pl.ds(k * channels, channels)
                        ]
            out_ref[s, pl.ds(c0, CHUNK), :] = acc
        return carry

    lax.fori_loop(0, last - first, slot_step, 0)


def disco_piece(src_rows, coef, ext, weight_flat, piece, pieces, lon_count):
    slot_total = ext.shape[0] - 2
    bounds = [i * slot_total // pieces for i in range(pieces + 1)]
    if pieces == 3 and slot_total >= 8:
        bounds = [0, slot_total // 8, slot_total // 2, slot_total]
    first, last = bounds[piece], bounds[piece + 1]
    lon_pad, channels = ext.shape[1:]
    out_rows = round_up(lon_count, CHUNK)
    smem = pltpu.MemorySpace.SMEM if hasattr(pltpu, "MemorySpace") else pltpu.SMEM
    return pl.pallas_call(
        functools.partial(disco_body, first, last),
        out_shape=jax.ShapeDtypeStruct((last - first, out_rows, channels), jnp.float32),
        in_specs=[
            pl.BlockSpec(memory_space=smem),
            pl.BlockSpec(memory_space=smem),
            pl.BlockSpec(memory_space=pltpu.VMEM),
            pl.BlockSpec(memory_space=pltpu.VMEM),
        ],
        out_specs=pl.BlockSpec(memory_space=pltpu.VMEM),
        scratch_shapes=[pltpu.VMEM((last - first + 3, lon_pad, weight_flat.shape[1]), jnp.float32)],
    )(src_rows, coef, ext, weight_flat)


def disco_tables(band_rows, disco_kernel, band_index, band_total, row_count):
    slot_ids = jnp.arange(row_count, dtype=jnp.int32)
    live_rows = band_rows[band_index]
    has_next = slot_ids + 1 < live_rows
    prev_band = jnp.maximum(band_index - 1, 0)
    next_band = jnp.minimum(band_index + 1, band_total - 1)
    base = band_index * row_count
    up_src = jnp.where(slot_ids == 0, 0, slot_ids)
    down_src = jnp.where(has_next, slot_ids + 2, row_count + 1)
    src = jnp.stack([up_src, slot_ids + 1, down_src], axis=1)
    up_row = jnp.where(
        slot_ids == 0, prev_band * row_count + band_rows[prev_band] - 1, base + slot_ids - 1
    )
    down_row = jnp.where(has_next, base + slot_ids + 1, next_band * row_count)
    kernel_row = jnp.stack([up_row, base + slot_ids, down_row], axis=1)
    kernel_row = jnp.clip(kernel_row, 0, disco_kernel.shape[0] - 1)
    up_ok = (slot_ids > 0) | (band_index > 0)
    down_ok = has_next | (band_index < band_total - 1)
    valid = jnp.stack([up_ok, jnp.ones_like(up_ok), down_ok], axis=1)
    gathered = disco_kernel[kernel_row]
    gathered = gathered.reshape(row_count, 3, 3, 3, disco_kernel.shape[2])
    coef = jnp.stack([gathered[:, 0, 2], gathered[:, 1, 1], gathered[:, 2, 0]], axis=1)
    coef = jnp.where(valid[:, :, None, None], coef, 0.0)
    return src.reshape(-1).astype(jnp.int32), coef.reshape(-1).astype(jnp.float32)


def lat_extend(block, live_rows):
    lat_total = lax.axis_size("lat")
    lat_up = [(i, (i + 1) % lat_total) for i in range(lat_total)]
    lat_down = [(j, i) for i, j in lat_up]
    last_row = lax.dynamic_slice_in_dim(block, live_rows - 1, 1, 0)
    from_above = lax.ppermute(last_row, "lat", lat_up)
    from_below = lax.ppermute(block[0:1], "lat", lat_down)
    return jnp.concatenate([from_above, block, from_below], axis=0)


def pad_lon(rows, lon_count):
    lon_pad = round_up(round_up(lon_count, CHUNK) + 2, 16)
    pad = jnp.zeros((rows.shape[0], lon_pad - rows.shape[1], rows.shape[2]), rows.dtype)
    return jnp.concatenate([rows, pad], axis=1)


def halo_extend(masked, live_rows):
    row_count, lon_count, channels = masked.shape
    lat_total = lax.axis_size("lat")
    lon_total = lax.axis_size("lon")
    lat_up = [(i, (i + 1) % lat_total) for i in range(lat_total)]
    lat_down = [(j, i) for i, j in lat_up]
    lon_up = [(i, (i + 1) % lon_total) for i in range(lon_total)]
    lon_down = [(j, i) for i, j in lon_up]
    last_row = lax.dynamic_slice_in_dim(masked, live_rows - 1, 1, 0)
    from_above = lax.ppermute(last_row, "lat", lat_up)
    from_below = lax.ppermute(masked[0:1], "lat", lat_down)
    rows = jnp.concatenate([from_above, masked, from_below], axis=0)
    from_left = lax.ppermute(rows[:, lon_count - 1 : lon_count], "lon", lon_up)
    from_right = lax.ppermute(rows[:, 0:1], "lon", lon_down)
    lon_pad = round_up(round_up(lon_count, CHUNK) + 2, 16)
    pad = jnp.zeros((row_count + 2, lon_pad - lon_count - 2, channels), masked.dtype)
    return jnp.concatenate([from_left, rows, from_right, pad], axis=1)


def spectral_by_channels(
    masked, legendre, quad_weights, spectral_filter, trig_parts, live_rows, disco_work, prep, raw
):
    ext = halo_extend(masked, live_rows)
    channels = masked.shape[2]
    lon_index = lax.axis_index("lon")
    chan_share = channels // lax.axis_size("lon")
    disco_parts = []
    portion = lax.all_to_all(masked, "lon", split_axis=2, concat_axis=1, tiled=True)
    spectra = jnp.stack(
        [dot_split("rnc,nk->rkc", (portion,), parts).astype(jnp.bfloat16) for parts in trig_parts],
        axis=1,
    )
    spectra, ext_now = lax.optimization_barrier((spectra, ext))
    columns = lax.all_to_all(spectra, "lat", split_axis=2, concat_axis=0, tiled=True)
    disco_parts.append(disco_work(ext_now, 0, prep))
    columns, disco_parts[0] = lax.optimization_barrier((columns, disco_parts[0]))
    legendre_parts = split_bf16(legendre)
    coefficients = dot_split("mls,spmc->lpmc", legendre_parts, (columns,))
    filter_slice = lax.dynamic_slice_in_dim(spectral_filter, lon_index * chan_share, chan_share, 2)
    filter_real = filter_slice[0][:, None, :]
    filter_imag = filter_slice[1][:, None, :]
    real_part = coefficients[:, 0]
    imag_part = coefficients[:, 1]
    filtered = jnp.stack(
        [
            filter_real * real_part + filter_imag * imag_part,
            filter_real * imag_part - filter_imag * real_part,
        ],
        axis=1,
    )
    returned = dot_split("mls,lpmc->spmc", legendre_parts, split_bf16(filtered))
    returned = (returned * quad_weights[:, None, None, None]).astype(jnp.bfloat16)
    returned, ext_now = lax.optimization_barrier((returned, ext))
    portion = lax.all_to_all(returned, "lat", split_axis=0, concat_axis=2, tiled=True)
    disco_parts.append(disco_work(ext_now, 1, prep))
    portion, disco_parts = lax.optimization_barrier((portion, disco_parts))
    spectral_rows = None
    for p, parts in enumerate(trig_parts):
        term = dot_split("rkc,nk->rnc", (portion[:, p],), parts)
        spectral_rows = term if spectral_rows is None else spectral_rows + term
    spectral_rows = spectral_rows.astype(jnp.bfloat16)
    spectral_rows, ext_now = lax.optimization_barrier((spectral_rows, ext))
    spectral = lax.all_to_all(spectral_rows, "lon", split_axis=1, concat_axis=2, tiled=True)
    disco_parts.append(disco_work(ext_now, 2, prep))
    spectral, disco_parts = lax.optimization_barrier((spectral, disco_parts))
    return spectral, disco_parts, masked


def filter_modes(coefficients, spectral_filter):
    filter_real = spectral_filter[0][:, None, :]
    filter_imag = spectral_filter[1][:, None, :]
    real_part = coefficients[:, 0]
    imag_part = coefficients[:, 1]
    return jnp.stack(
        [
            filter_real * real_part + filter_imag * imag_part,
            filter_real * imag_part - filter_imag * real_part,
        ],
        axis=1,
    )


def spectral_by_modes(
    masked, legendre, quad_weights, spectral_filter, trig_parts, live_rows, disco_work, prep, raw
):
    both = ("lat", "lon")
    lon_total = lax.axis_size("lon")
    mode_share = legendre.shape[0] // lon_total
    row_count, lon_count, channels = masked.shape
    share = row_count // lon_total
    body = raw.reshape(lon_total, share * lon_count, channels)
    edges = jnp.concatenate([raw[:, 0], raw[:, lon_count - 1]], axis=0)
    edges = jnp.broadcast_to(edges[None], (lon_total, 2 * row_count, channels))
    send, raw = lax.optimization_barrier((jnp.concatenate([body, edges], axis=1), raw))
    received = lax.all_to_all(send, "lon", split_axis=0, concat_axis=0, tiled=True)
    slot_live = jnp.arange(row_count) < live_rows
    masked = jnp.where(slot_live[:, None, None], raw, jnp.zeros_like(raw))
    own_legendre = lax.dynamic_slice_in_dim(
        legendre, lax.axis_index("lon") * mode_share, mode_share, 0
    )
    legendre_parts = split_bf16(own_legendre)
    received, legendre_parts, prep = lax.optimization_barrier((received, legendre_parts, prep))
    portion = received[:, : share * lon_count].reshape(lon_total, share, lon_count, channels)
    portion = portion.transpose(1, 0, 2, 3).reshape(share, lon_total * lon_count, channels)
    portion_live = lax.axis_index("lon") * share + jnp.arange(share) < live_rows
    portion = jnp.where(portion_live[:, None, None], portion, jnp.zeros_like(portion))
    edge_block = received[:, share * lon_count :]
    lon_index = lax.axis_index("lon")
    left = lax.dynamic_index_in_dim(edge_block, (lon_index - 1) % lon_total, 0, keepdims=False)
    right = lax.dynamic_index_in_dim(edge_block, (lon_index + 1) % lon_total, 0, keepdims=False)
    own = jnp.concatenate([left[row_count:, None], masked, right[:row_count, None]], axis=1)
    disco_parts = []
    spectra = jnp.stack(
        [dot_split("rnc,nk->rkc", (portion,), parts).astype(jnp.bfloat16) for parts in trig_parts],
        axis=1,
    )
    spectra, own = lax.optimization_barrier((spectra, own))
    ext = pad_lon(lat_extend(own, live_rows), lon_count)
    ext_now = ext
    columns = lax.all_to_all(spectra, both, split_axis=2, concat_axis=0, tiled=True)
    coefficients = dot_split("mls,spmc->lpmc", legendre_parts, (columns,))
    filtered = filter_modes(coefficients, spectral_filter)
    returned = dot_split("mls,lpmc->spmc", legendre_parts, split_bf16(filtered))
    returned = (returned * quad_weights[:, None, None, None]).astype(jnp.bfloat16)
    returned, ext_now = lax.optimization_barrier((returned, ext))
    portion = lax.all_to_all(returned, both, split_axis=0, concat_axis=2, tiled=True)
    disco_parts.append(disco_work(ext_now, 0, prep))
    portion, disco_parts = lax.optimization_barrier((portion, disco_parts))
    spectral_rows = None
    for p, parts in enumerate(trig_parts):
        term = dot_split("rkc,nk->rnc", (portion[:, p],), parts)
        spectral_rows = term if spectral_rows is None else spectral_rows + term
    spectral_rows = spectral_rows.astype(jnp.bfloat16)
    spectral_rows, ext_now = lax.optimization_barrier((spectral_rows, ext))
    spectral = lax.all_to_all(spectral_rows, "lon", split_axis=1, concat_axis=0, tiled=True)
    disco_parts.append(disco_work(ext_now, 1, prep))
    spectral, disco_parts = lax.optimization_barrier((spectral, disco_parts))
    return spectral, disco_parts, masked


def on_device(
    grad_output, band_rows, legendre, quad_weights, spectral_filter, disco_kernel, disco_weight
):
    row_count, lon_count, channels = grad_output.shape
    band_index = lax.axis_index("lat")
    band_total = lax.axis_size("lat")
    lon_total = lax.axis_size("lon")
    point_count = lon_count * lon_total
    mode_count = legendre.shape[0] * band_total
    slot_ids = jnp.arange(row_count, dtype=jnp.int32)
    live_rows = band_rows[band_index]
    live_slot = slot_ids < live_rows
    masked = jnp.where(live_slot[:, None, None], grad_output, jnp.zeros_like(grad_output))
    trig_parts = make_trig(mode_count, point_count)
    src_rows, coef = disco_tables(band_rows, disco_kernel, band_index, band_total, row_count)
    weight_flat = disco_weight.reshape(channels, -1)
    by_modes = legendre.shape[0] % lon_total == 0 and row_count % lon_total == 0
    pieces = min(2 if by_modes else 3, row_count)

    def disco_work(ext_now, piece, prep):
        return disco_piece(prep[0], prep[1], ext_now, prep[2], piece, pieces, lon_count)

    path = spectral_by_modes if by_modes else spectral_by_channels
    spectral, disco_parts, masked = path(
        masked,
        legendre,
        quad_weights,
        spectral_filter,
        trig_parts,
        live_rows,
        disco_work,
        (src_rows, coef, weight_flat),
        grad_output,
    )
    disco_full = jnp.concatenate(disco_parts, axis=0)
    disco_term = disco_full[:, :lon_count, :]
    summed = masked.astype(jnp.float32) + disco_term + spectral.astype(jnp.float32)
    return jnp.where(live_slot[:, None, None], summed, 0.0).astype(jnp.bfloat16)


def solution(mesh):
    placed = (P("lat", "lon", None), P(), P("lat", None, None), P(), P(), P(), P())
    return jax.shard_map(
        on_device, mesh=mesh, in_specs=placed, out_specs=P("lat", "lon", None), check_vma=False
    )
```

```python
import functools

import ml_dtypes
import numpy as np
import jax
import jax.numpy as jnp
from jax import lax
from jax.experimental import pallas as pl
from jax.experimental.pallas import tpu as pltpu
from jax.sharding import PartitionSpec as P


def make_trig(mode_count, point_count):
    step = 16 if point_count % 16 == 0 else 1
    coarse = np.arange(point_count // step)[:, None] * step
    fine = np.arange(step)[:, None]
    wavenumber = np.arange(mode_count)[None, :]
    coarse_angle = (wavenumber * coarse % point_count) * (2.0 * np.pi / point_count)
    fine_angle = (wavenumber * fine % point_count) * (2.0 * np.pi / point_count)
    scale = point_count ** (-0.5)
    coarse_cos = jnp.asarray((np.cos(coarse_angle) * scale).astype(np.float32))[:, None, :]
    coarse_sin = jnp.asarray((np.sin(coarse_angle) * scale).astype(np.float32))[:, None, :]
    fine_cos = jnp.asarray(np.cos(fine_angle).astype(np.float32))[None, :, :]
    fine_sin = jnp.asarray(np.sin(fine_angle).astype(np.float32))[None, :, :]
    cosine = coarse_cos * fine_cos - coarse_sin * fine_sin
    minus_sine = -(coarse_sin * fine_cos + coarse_cos * fine_sin)
    return tuple(
        split_bf16(part.reshape(point_count, mode_count)) for part in (cosine, minus_sine)
    )


def split_bf16(values):
    rounded = lax.reduce_precision(values, exponent_bits=8, mantissa_bits=7)
    return rounded.astype(jnp.bfloat16), (values - rounded).astype(jnp.bfloat16)


def dot_split(spec, left_parts, right_parts):
    total = None
    for lp in left_parts:
        for rp in right_parts:
            if lp is not left_parts[0] and rp is not right_parts[0]:
                continue
            term = jnp.einsum(spec, lp, rp, preferred_element_type=jnp.float32)
            total = term if total is None else total + term
    return total


CHUNK = 64


def round_up(value, step):
    return -(-value // step) * step


def disco_body(first, last, src_ref, coef_ref, ext_ref, w_ref, out_ref, mix_ref):
    kinds = w_ref.shape[1] // w_ref.shape[0]
    channels = w_ref.shape[0]
    span = last - first + 2
    below = ext_ref.shape[0] - 1
    for r in range(span):
        mix_ref[r] = jnp.dot(ext_ref[first + r], w_ref[...], preferred_element_type=jnp.float32)
    mix_ref[span] = jnp.dot(ext_ref[below], w_ref[...], preferred_element_type=jnp.float32)

    def slot_step(s, carry):
        for c0 in range(0, out_ref.shape[1], CHUNK):
            acc = jnp.zeros((CHUNK, channels), jnp.float32)
            for a_i in range(3):
                source = src_ref[(first + s) * 3 + a_i]
                row = jnp.where(source == below, span, source - first)
                for b_i in range(3):
                    for k in range(kinds):
                        coef = coef_ref[(((first + s) * 3 + a_i) * 3 + b_i) * kinds + k]
                        acc = acc + coef * mix_ref[
                            row, pl.ds(c0 + 2 - b_i, CHUNK), pl.ds(k * channels, channels)
                        ]
            out_ref[s, pl.ds(c0, CHUNK), :] = acc
        return carry

    lax.fori_loop(0, last - first, slot_step, 0)


def disco_piece(src_rows, coef, ext, weight_flat, piece, pieces, lon_count):
    slot_total = ext.shape[0] - 2
    bounds = [i * slot_total // pieces for i in range(pieces + 1)]
    if pieces == 3 and slot_total >= 8:
        bounds = [0, slot_total // 8, slot_total // 2, slot_total]
    if pieces == 2 and slot_total >= 8:
        bounds = [0, 3 * slot_total // 8, slot_total]
    first, last = bounds[piece], bounds[piece + 1]
    lon_pad, channels = ext.shape[1:]
    out_rows = round_up(lon_count, CHUNK)
    smem = pltpu.MemorySpace.SMEM if hasattr(pltpu, "MemorySpace") else pltpu.SMEM
    return pl.pallas_call(
        functools.partial(disco_body, first, last),
        out_shape=jax.ShapeDtypeStruct((last - first, out_rows, channels), jnp.float32),
        in_specs=[
            pl.BlockSpec(memory_space=smem),
            pl.BlockSpec(memory_space=smem),
            pl.BlockSpec(memory_space=pltpu.VMEM),
            pl.BlockSpec(memory_space=pltpu.VMEM),
        ],
        out_specs=pl.BlockSpec(memory_space=pltpu.VMEM),
        scratch_shapes=[pltpu.VMEM((last - first + 3, lon_pad, weight_flat.shape[1]), jnp.float32)],
    )(src_rows, coef, ext, weight_flat)


def disco_tables(band_rows, disco_kernel, band_index, band_total, row_count):
    slot_ids = jnp.arange(row_count, dtype=jnp.int32)
    live_rows = band_rows[band_index]
    has_next = slot_ids + 1 < live_rows
    prev_band = jnp.maximum(band_index - 1, 0)
    next_band = jnp.minimum(band_index + 1, band_total - 1)
    base = band_index * row_count
    up_src = jnp.where(slot_ids == 0, 0, slot_ids)
    down_src = jnp.where(has_next, slot_ids + 2, row_count + 1)
    src = jnp.stack([up_src, slot_ids + 1, down_src], axis=1)
    up_row = jnp.where(
        slot_ids == 0, prev_band * row_count + band_rows[prev_band] - 1, base + slot_ids - 1
    )
    down_row = jnp.where(has_next, base + slot_ids + 1, next_band * row_count)
    kernel_row = jnp.stack([up_row, base + slot_ids, down_row], axis=1)
    kernel_row = jnp.clip(kernel_row, 0, disco_kernel.shape[0] - 1)
    up_ok = (slot_ids > 0) | (band_index > 0)
    down_ok = has_next | (band_index < band_total - 1)
    valid = jnp.stack([up_ok, jnp.ones_like(up_ok), down_ok], axis=1)
    gathered = disco_kernel[kernel_row]
    gathered = gathered.reshape(row_count, 3, 3, 3, disco_kernel.shape[2])
    coef = jnp.stack([gathered[:, 0, 2], gathered[:, 1, 1], gathered[:, 2, 0]], axis=1)
    coef = jnp.where(valid[:, :, None, None], coef, 0.0)
    return src.reshape(-1).astype(jnp.int32), coef.reshape(-1).astype(jnp.float32)


def lat_extend(block, live_rows):
    lat_total = lax.axis_size("lat")
    lat_up = [(i, (i + 1) % lat_total) for i in range(lat_total)]
    lat_down = [(j, i) for i, j in lat_up]
    last_row = lax.dynamic_slice_in_dim(block, live_rows - 1, 1, 0)
    from_above = lax.ppermute(last_row, "lat", lat_up)
    from_below = lax.ppermute(block[0:1], "lat", lat_down)
    return jnp.concatenate([from_above, block, from_below], axis=0)


def pad_lon(rows, lon_count):
    lon_pad = round_up(round_up(lon_count, CHUNK) + 2, 16)
    pad = jnp.zeros((rows.shape[0], lon_pad - rows.shape[1], rows.shape[2]), rows.dtype)
    return jnp.concatenate([rows, pad], axis=1)


def halo_extend(masked, live_rows):
    row_count, lon_count, channels = masked.shape
    lat_total = lax.axis_size("lat")
    lon_total = lax.axis_size("lon")
    lat_up = [(i, (i + 1) % lat_total) for i in range(lat_total)]
    lat_down = [(j, i) for i, j in lat_up]
    lon_up = [(i, (i + 1) % lon_total) for i in range(lon_total)]
    lon_down = [(j, i) for i, j in lon_up]
    last_row = lax.dynamic_slice_in_dim(masked, live_rows - 1, 1, 0)
    from_above = lax.ppermute(last_row, "lat", lat_up)
    from_below = lax.ppermute(masked[0:1], "lat", lat_down)
    rows = jnp.concatenate([from_above, masked, from_below], axis=0)
    from_left = lax.ppermute(rows[:, lon_count - 1 : lon_count], "lon", lon_up)
    from_right = lax.ppermute(rows[:, 0:1], "lon", lon_down)
    lon_pad = round_up(round_up(lon_count, CHUNK) + 2, 16)
    pad = jnp.zeros((row_count + 2, lon_pad - lon_count - 2, channels), masked.dtype)
    return jnp.concatenate([from_left, rows, from_right, pad], axis=1)


def spectral_by_channels(
    masked, legendre, quad_weights, spectral_filter, trig_parts, live_rows, disco_work, prep, raw
):
    ext = halo_extend(masked, live_rows)
    channels = masked.shape[2]
    lon_index = lax.axis_index("lon")
    chan_share = channels // lax.axis_size("lon")
    disco_parts = []
    portion = lax.all_to_all(masked, "lon", split_axis=2, concat_axis=1, tiled=True)
    spectra = jnp.stack(
        [dot_split("rnc,nk->rkc", (portion,), parts).astype(jnp.bfloat16) for parts in trig_parts],
        axis=1,
    )
    spectra, ext_now = lax.optimization_barrier((spectra, ext))
    columns = lax.all_to_all(spectra, "lat", split_axis=2, concat_axis=0, tiled=True)
    disco_parts.append(disco_work(ext_now, 0, prep))
    columns, disco_parts[0] = lax.optimization_barrier((columns, disco_parts[0]))
    legendre_parts = split_bf16(legendre)
    coefficients = dot_split("mls,spmc->lpmc", legendre_parts, (columns,))
    filter_slice = lax.dynamic_slice_in_dim(spectral_filter, lon_index * chan_share, chan_share, 2)
    filter_real = filter_slice[0][:, None, :]
    filter_imag = filter_slice[1][:, None, :]
    real_part = coefficients[:, 0]
    imag_part = coefficients[:, 1]
    filtered = jnp.stack(
        [
            filter_real * real_part + filter_imag * imag_part,
            filter_real * imag_part - filter_imag * real_part,
        ],
        axis=1,
    )
    returned = dot_split("mls,lpmc->spmc", legendre_parts, split_bf16(filtered))
    returned = (returned * quad_weights[:, None, None, None]).astype(jnp.bfloat16)
    returned, ext_now = lax.optimization_barrier((returned, ext))
    portion = lax.all_to_all(returned, "lat", split_axis=0, concat_axis=2, tiled=True)
    disco_parts.append(disco_work(ext_now, 1, prep))
    portion, disco_parts = lax.optimization_barrier((portion, disco_parts))
    spectral_rows = None
    for p, parts in enumerate(trig_parts):
        term = dot_split("rkc,nk->rnc", (portion[:, p],), parts)
        spectral_rows = term if spectral_rows is None else spectral_rows + term
    spectral_rows = spectral_rows.astype(jnp.bfloat16)
    spectral_rows, ext_now = lax.optimization_barrier((spectral_rows, ext))
    spectral = lax.all_to_all(spectral_rows, "lon", split_axis=1, concat_axis=2, tiled=True)
    disco_parts.append(disco_work(ext_now, 2, prep))
    spectral, disco_parts = lax.optimization_barrier((spectral, disco_parts))
    return spectral, disco_parts


def filter_modes(coefficients, spectral_filter):
    filter_real = spectral_filter[0][:, None, :]
    filter_imag = spectral_filter[1][:, None, :]
    real_part = coefficients[:, 0]
    imag_part = coefficients[:, 1]
    return jnp.stack(
        [
            filter_real * real_part + filter_imag * imag_part,
            filter_real * imag_part - filter_imag * real_part,
        ],
        axis=1,
    )


def spectral_by_modes(
    masked, legendre, quad_weights, spectral_filter, trig_parts, live_rows, disco_work, prep, raw
):
    both = ("lat", "lon")
    lon_total = lax.axis_size("lon")
    mode_share = legendre.shape[0] // lon_total
    row_count, lon_count, channels = masked.shape
    share = row_count // lon_total
    body = raw.reshape(lon_total, share * lon_count, channels)
    edges = jnp.concatenate([raw[:, 0], raw[:, lon_count - 1]], axis=0)
    edges = jnp.broadcast_to(edges[None], (lon_total, 2 * row_count, channels))
    received = lax.all_to_all(
        jnp.concatenate([body, edges], axis=1), "lon", split_axis=0, concat_axis=0, tiled=True
    )
    own_legendre = lax.dynamic_slice_in_dim(
        legendre, lax.axis_index("lon") * mode_share, mode_share, 0
    )
    legendre_parts = split_bf16(own_legendre)
    received, legendre_parts, prep = lax.optimization_barrier((received, legendre_parts, prep))
    portion = received[:, : share * lon_count].reshape(lon_total, share, lon_count, channels)
    portion = portion.transpose(1, 0, 2, 3).reshape(share, lon_total * lon_count, channels)
    portion_live = lax.axis_index("lon") * share + jnp.arange(share) < live_rows
    portion = jnp.where(portion_live[:, None, None], portion, jnp.zeros_like(portion))
    edge_block = received[:, share * lon_count :]
    lon_index = lax.axis_index("lon")
    left = lax.dynamic_index_in_dim(edge_block, (lon_index - 1) % lon_total, 0, keepdims=False)
    right = lax.dynamic_index_in_dim(edge_block, (lon_index + 1) % lon_total, 0, keepdims=False)
    own = jnp.concatenate([left[row_count:, None], masked, right[:row_count, None]], axis=1)
    disco_parts = []
    spectra = jnp.stack(
        [dot_split("rnc,nk->rkc", (portion,), parts).astype(jnp.bfloat16) for parts in trig_parts],
        axis=1,
    )
    spectra, own = lax.optimization_barrier((spectra, own))
    ext = pad_lon(lat_extend(own, live_rows), lon_count)
    ext_now = ext
    columns = lax.all_to_all(spectra, both, split_axis=2, concat_axis=0, tiled=True)
    coefficients = dot_split("mls,spmc->lpmc", legendre_parts, (columns,))
    filtered = filter_modes(coefficients, spectral_filter)
    returned = dot_split("mls,lpmc->spmc", legendre_parts, split_bf16(filtered))
    returned = (returned * quad_weights[:, None, None, None]).astype(jnp.bfloat16)
    returned, ext_now = lax.optimization_barrier((returned, ext))
    portion = lax.all_to_all(returned, both, split_axis=0, concat_axis=2, tiled=True)
    disco_parts.append(disco_work(ext_now, 0, prep))
    portion, disco_parts = lax.optimization_barrier((portion, disco_parts))
    spectral_rows = None
    for p, parts in enumerate(trig_parts):
        term = dot_split("rkc,nk->rnc", (portion[:, p],), parts)
        spectral_rows = term if spectral_rows is None else spectral_rows + term
    spectral_rows = spectral_rows.astype(jnp.bfloat16)
    spectral_rows, ext_now = lax.optimization_barrier((spectral_rows, ext))
    spectral = lax.all_to_all(spectral_rows, "lon", split_axis=1, concat_axis=0, tiled=True)
    disco_parts.append(disco_work(ext_now, 1, prep))
    spectral, disco_parts = lax.optimization_barrier((spectral, disco_parts))
    return spectral, disco_parts


def on_device(
    grad_output, band_rows, legendre, quad_weights, spectral_filter, disco_kernel, disco_weight
):
    row_count, lon_count, channels = grad_output.shape
    band_index = lax.axis_index("lat")
    band_total = lax.axis_size("lat")
    lon_total = lax.axis_size("lon")
    point_count = lon_count * lon_total
    mode_count = legendre.shape[0] * band_total
    slot_ids = jnp.arange(row_count, dtype=jnp.int32)
    live_rows = band_rows[band_index]
    live_slot = slot_ids < live_rows
    masked = jnp.where(live_slot[:, None, None], grad_output, jnp.zeros_like(grad_output))
    trig_parts = make_trig(mode_count, point_count)
    src_rows, coef = disco_tables(band_rows, disco_kernel, band_index, band_total, row_count)
    weight_flat = disco_weight.reshape(channels, -1)
    by_modes = legendre.shape[0] % lon_total == 0 and row_count % lon_total == 0
    pieces = min(2 if by_modes else 3, row_count)

    def disco_work(ext_now, piece, prep):
        return disco_piece(prep[0], prep[1], ext_now, prep[2], piece, pieces, lon_count)

    path = spectral_by_modes if by_modes else spectral_by_channels
    spectral, disco_parts = path(
        masked,
        legendre,
        quad_weights,
        spectral_filter,
        trig_parts,
        live_rows,
        disco_work,
        (src_rows, coef, weight_flat),
        grad_output,
    )
    disco_full = jnp.concatenate(disco_parts, axis=0)
    disco_term = disco_full[:, :lon_count, :]
    summed = masked.astype(jnp.float32) + disco_term + spectral.astype(jnp.float32)
    return jnp.where(live_slot[:, None, None], summed, 0.0).astype(jnp.bfloat16)


def solution(mesh):
    placed = (P("lat", "lon", None), P(), P("lat", None, None), P(), P(), P(), P())
    return jax.shard_map(
        on_device, mesh=mesh, in_specs=placed, out_specs=P("lat", "lon", None), check_vma=False
    )
```
